32 devices in a mesh: img: 8 (over z, y), sub: 4 (over x, core).
Axes of the slice: x: 2, y: 2, z: 4, core: 2. Of those that a mesh axis runs over, the one named last changes fastest.
Arguments:
- embeddings: bfloat16 [4096, 768], P('img'), may hold values from -60 to 60
- labels: bfloat16 [4096, 256], P('img', 'sub'), may hold values from -6 to 6
- image_lists: int32 [4096, 2], P('img'), may hold values from 0 to 7, all different within a row; in each aligned block of 512 rows (0 to 511, 512 to 1023, ...) at most 256 rows name the same one
- rank_keys: int32 [4096, 2], P('img'), may hold values from 0 to 255
Outputs:
- propagated: bfloat16 [4096, 256], P('img', 'sub')
The draws below stay inside these ranges and needn't reach their ends.
Inputs may be any that keep to these rules, and one draw needn't show every extreme that they name: `image_lists`: the two lists of an image differ. On the rows of one index of img no list is named more than 256 times, a bound that some block reaches.
All inputs are finite; a program needn't handle non-finite values.
Results may differ from the reference program's by a relative error of at most 0.0034.
Values may be sent and summed in bfloat16 or wider, within the bound.
No kernel may reach another device: no remote copies, remote signals or barrier semaphores. Data moves between devices by JAX's collectives and lax.ppermute only.
A program may use at most 64 MiB of HBM per device.

```python
import math
import jax
import jax.numpy as jnp
import numpy as np
from jax import lax

E = 768
C = 256
SLOTS = 2048
KEYS = 256
BAND = 64
IMG_DEV = 512
LISTS = 8
IMAGES = 4096
MOST = 256
N_IMG = 8


def draw_embeddings(key, part):
    key_common = jax.random.fold_in(key, 11)
    key_noise = jax.random.fold_in(key, 12)
    common = jax.random.normal(key_common, (1, E), jnp.float32)
    noise = jax.random.normal(key_noise, (IMAGES, E), jnp.float32)
    return (0.65 * common + noise).astype(jnp.bfloat16)


def plant(entries, key, low, largest):
    longest = entries.shape.index(max(entries.shape))
    spots = []
    for shift in (0, 1):
        where = [jax.random.randint(jax.random.fold_in(key, axis), (), 0, length) for axis, length in enumerate(entries.shape)]
        where[longest] = (where[longest] + shift) % entries.shape[longest]
        spots.append(tuple(where))
    return entries.at[spots[0]].set(low).at[spots[1]].set(largest)


def block_scale(own_key, extent, cuts, least, top_value):
    gain, own = 1.0, jax.random.fold_in(own_key, 6)
    for position, shards_of in cuts:
        steps = jnp.exp(jax.random.uniform(jax.random.fold_in(own, position), (shards_of,), jnp.float32, least / len(cuts), top_value / len(cuts)))
        gain = gain * jnp.repeat(steps, extent[position] // shards_of).reshape([-1 if axis == position else 1 for axis in range(len(extent))])
    return gain


def deal_out(stream_key, own, number, rows, number_of, top, reach, slope):
    ranking = jax.random.permutation(stream_key, number_of)
    heavy_load, ordinary = shares(number_of, rows * top, reach, slope, True), shares(number_of, rows * top, reach, slope, False)
    places = jnp.arange(number_of)

    def named(tallies, rotation):
        used = int((tallies > 0).sum())
        fixed = max(1, used // 4)
        passed = fixed + (places - fixed + rotation * (used - fixed)) % max(1, number_of - fixed)
        return jnp.zeros((number_of,), jnp.int32).at[ranking[jnp.where(places < fixed, places, passed)]].set(jnp.asarray(tallies, jnp.int32))

    tallies = jnp.where(number % 4 == 0, named(heavy_load, number // 4), named(ordinary, number - number // 4 - 1))
    mixed = jax.random.permutation(jax.random.fold_in(own, 3), number_of)
    donor, taker = mixed[0:number_of // 2 * 2:2], mixed[1:number_of // 2 * 2:2]
    margin = jnp.minimum(tallies[donor] - 1, reach - tallies[taker]) // 2
    margin = jnp.where((donor == ranking[0]) | (taker == ranking[0]) | (tallies[taker] == 0), 0, jnp.maximum(margin, 0))
    passed = jax.random.randint(jax.random.fold_in(own, 4), (number_of // 2,), 0, 1 << 20) % (margin + 1)
    tallies = tallies.at[donor].add(-passed).at[taker].add(passed)
    items = jnp.searchsorted(jnp.cumsum(tallies), jnp.arange(rows * top), side="right").astype(jnp.int32)
    grid = items.reshape(top, rows).T
    grid = grid[jax.random.permutation(jax.random.fold_in(own, 1), rows)]
    rotation = jax.random.randint(jax.random.fold_in(own, 2), (rows, 1), 0, top)
    return jnp.take_along_axis(grid, (jnp.arange(top)[None, :] + rotation) % top, axis=1)


def shares(amount, total, reach, slope, full):
    weights = [(1 << 20) // math.isqrt(standing ** slope) + 1 for standing in range(1, amount + 1)]
    largest = reach if full else min(reach, max(-(-total // amount), total * weights[0] // sum(weights)))
    least = 1 if total - largest >= amount - 1 else 0
    counts, spare = [largest] + [least] * (amount - 1), total - largest - least * (amount - 1)
    while spare > 0:
        free = [i for i in range(1, amount) if counts[i] < largest] or [i for i in range(1, amount) if counts[i] < reach]
        mass, budget = sum([weights[i] for i in free]), spare
        for i in free:
            addition = min(reach - counts[i], max(1, budget * weights[i] // mass), spare)
            counts[i] = counts[i] + addition
            spare = spare - addition
    return np.array(counts)


def normal_values(stream_key, extent, deviation, bound, shards=(), held_as=jnp.bfloat16):
    result = jax.random.normal(stream_key, extent, jnp.float32) * deviation
    if len(shards) > 0:
        result = block_scale(stream_key, extent, shards, -0.22, 0.18) * result
    return jnp.clip(result, min=-bound, max=bound).astype(held_as)


def setup_inputs(seed: int = 0) -> dict:
    seeds = jax.random.split(jax.random.key(seed), 5)
    embeddings = draw_embeddings(jax.random.fold_in(seeds[4], 71), 0)
    labels = normal_values(seeds[1], (IMAGES, C), 1.0, 6.0, ((0, 8), (1, 4)))
    image_lists_keys = jax.random.split(jax.random.fold_in(seeds[2], 1), IMAGES // IMG_DEV)
    image_lists_turns = jax.random.permutation(jax.random.fold_in(seeds[2], 3), IMAGES // IMG_DEV)
    image_lists = jax.vmap(lambda own, number: deal_out(jax.random.fold_in(seeds[2], 2), own, number, IMG_DEV, LISTS, 2, MOST, 1))(image_lists_keys, image_lists_turns).reshape((IMAGES, 2))
    rank_keys = plant(jax.random.randint(seeds[3], (IMAGES, 2), 0, KEYS), jax.random.fold_in(seeds[3], 1), 0, KEYS - 1).astype(jnp.int32)
    return dict(embeddings=embeddings, labels=labels, image_lists=image_lists, rank_keys=rank_keys)


def member_table(image_lists):
    per_list = SLOTS // N_IMG
    pair_count = IMG_DEV * 2
    blocks = image_lists.reshape(N_IMG, pair_count).astype(jnp.int32)
    order = jnp.arange(pair_count, dtype=jnp.int32)

    def ranks(block_lists):
        same = (block_lists[:, None] == block_lists[None, :]) & (order[None, :] < order[:, None])
        return lax.optimization_barrier(jnp.sum(same.astype(jnp.int32), axis=1)).astype(jnp.int32)
    within = lax.map(ranks, blocks)
    source = jnp.arange(N_IMG, dtype=jnp.int32)[:, None]
    flat_slot = (blocks * SLOTS + source * per_list + within).reshape(-1).astype(jnp.int32)
    pair_ids = jnp.arange(IMAGES * 2, dtype=jnp.int32)
    members = jnp.full((LISTS * SLOTS,), IMAGES * 2, jnp.int32).at[flat_slot].set(pair_ids)
    return members.reshape(LISTS, SLOTS)

def reference(embeddings, labels, image_lists, rank_keys):
    values = embeddings.astype(jnp.float32)
    unit = (values * lax.rsqrt(lax.optimization_barrier(jnp.sum(values * values, axis=1, keepdims=True)) + 1e-06)).astype(jnp.bfloat16)
    unit_pad = jnp.concatenate([unit, jnp.zeros((1, E), jnp.bfloat16)], axis=0)
    key_pad = jnp.concatenate([rank_keys.reshape(-1).astype(jnp.float32), jnp.full((1,), -4096.0, jnp.float32)])
    members = member_table(image_lists)
    member_img = (members // 2).astype(jnp.int32)

    def one_list(slot_pairs):
        rows = unit_pad[slot_pairs // 2]
        slot_keys = key_pad[slot_pairs]
        gram = jnp.dot(rows, rows.T, preferred_element_type=jnp.float32)
        keep = jnp.abs(slot_keys[:, None] - slot_keys[None, :]) <= BAND
        positive = jnp.maximum(gram, 0.0)
        return jnp.where(keep, positive * positive * positive, 0.0).astype(jnp.bfloat16)
    weights = lax.map(one_list, members)
    row_sums = lax.optimization_barrier(jnp.sum(weights, axis=2, dtype=jnp.float32))
    degree = jnp.zeros((IMAGES + 1,), jnp.float32).at[member_img.reshape(-1)].add(row_sums.reshape(-1))[:IMAGES]
    inv = lax.rsqrt(degree)
    starting = labels.astype(jnp.float32)
    current = starting
    for step in range(2):
        scaled = (inv[:, None] * current).astype(jnp.bfloat16)
        scaled_pad = jnp.concatenate([scaled, jnp.zeros((1, C), jnp.bfloat16)], axis=0)

        def list_product(packed):
            block_weights, slot_imgs = packed
            return jnp.dot(block_weights, scaled_pad[slot_imgs], preferred_element_type=jnp.float32)
        product = lax.map(list_product, (weights, member_img))
        spread = jnp.zeros((IMAGES + 1, C), jnp.float32).at[member_img.reshape(-1)].add(product.reshape(-1, C))[:IMAGES]
        current = 0.8 * inv[:, None] * spread + 0.2 * starting
    return current.astype(jnp.bfloat16)
```

```python
import jax
import jax.numpy as jnp
from jax import lax
from jax.sharding import PartitionSpec as P

SLOTS = 2048
BAND = 64
LIST_DEV = 1


def affinity(gram, row_keys, col_keys):
    keep = jnp.abs(row_keys[:, :, None] - col_keys[:, None, :]) <= BAND
    positive = jnp.maximum(gram, 0.0)
    return jnp.where(keep, positive * positive * positive, 0.0).astype(jnp.bfloat16)


def list_major(bucket):
    moved = jnp.moveaxis(bucket, 1, 0)
    return moved.reshape((moved.shape[0], moved.shape[1] * moved.shape[2]) + moved.shape[3:])


def blocked_affinity(rows, key_rows):
    lists_here = rows.shape[0]
    slot_count = rows.shape[1]
    block_rows = min(512, slot_count)
    block_count = slot_count // block_rows
    row_blocks = jnp.moveaxis(
        rows.reshape(lists_here, block_count, block_rows, rows.shape[2]), 1, 0
    )
    key_blocks = jnp.moveaxis(key_rows.reshape(lists_here, block_count, block_rows), 1, 0)

    def one_block(packed):
        picked, picked_keys = packed
        gram = jnp.einsum("ajf,akf->ajk", picked, rows, preferred_element_type=jnp.float32)
        return affinity(gram, picked_keys, key_rows)

    blocks = lax.map(one_block, (row_blocks, key_blocks))
    return jnp.moveaxis(blocks, 0, 1).reshape(lists_here, slot_count, slot_count)


def on_device(embeddings, labels, image_lists, rank_keys):
    img_count = lax.axis_size("img")
    per_list = SLOTS // img_count
    rows_here = image_lists.shape[0]
    pair_count = rows_here * 2
    lists_flat = image_lists.reshape(-1)
    order = jnp.arange(pair_count, dtype=jnp.int32)
    same = (lists_flat[:, None] == lists_flat[None, :]) & (order[None, :] < order[:, None])
    within = jnp.sum(same.astype(jnp.int32), axis=1)
    slot_of_pair = lists_flat * per_list + within
    slot_total = LIST_DEV * img_count * per_list
    filler = jnp.full((slot_total,), pair_count, jnp.int32).at[slot_of_pair].set(order)
    image_of_slot = filler // 2

    def to_bucket(rows):
        padded = jnp.concatenate([rows, jnp.zeros((1, rows.shape[1]), rows.dtype)], axis=0)
        return padded[image_of_slot].reshape(img_count, LIST_DEV, per_list, rows.shape[1])

    def bucket_major(listed):
        shaped = listed.reshape((listed.shape[0], img_count, per_list) + listed.shape[2:])
        return jnp.moveaxis(shaped, 0, 1)

    def from_bucket(returned):
        flat = returned.reshape(slot_total, -1)
        return jnp.sum(flat[slot_of_pair].reshape(rows_here, 2, -1), axis=1)

    values = embeddings.astype(jnp.float32)
    unit = (values * lax.rsqrt(jnp.sum(values * values, axis=1, keepdims=True) + 1e-06)).astype(
        jnp.bfloat16
    )
    key_pad = jnp.concatenate(
        [rank_keys.reshape(-1).astype(jnp.float32), jnp.full((1,), -4096.0, jnp.float32)]
    )
    slot_keys = key_pad[filler].astype(jnp.bfloat16).reshape(img_count, LIST_DEV, per_list)
    sub_count = lax.axis_size("sub")
    part = per_list // sub_count
    mine = lax.dynamic_index_in_dim(
        image_of_slot.reshape(img_count, sub_count, part), lax.axis_index("sub"), axis=1,
        keepdims=False,
    )
    unit_pad = jnp.concatenate([unit, jnp.zeros((1, unit.shape[1]), unit.dtype)], axis=0)
    sent = lax.all_to_all(unit_pad[mine], "img", split_axis=0, concat_axis=0, tiled=True)
    feats = lax.all_gather(sent, "sub", axis=1, tiled=False).reshape(
        img_count, LIST_DEV, per_list, unit.shape[1]
    )
    got_keys = lax.all_to_all(slot_keys, "img", split_axis=0, concat_axis=0, tiled=True)
    rows = list_major(feats)
    key_rows = list_major(got_keys).astype(jnp.float32)
    weights = blocked_affinity(rows, key_rows)
    row_sums = jnp.sum(weights, axis=2, dtype=jnp.float32)
    degree_slots = lax.all_to_all(
        bucket_major(row_sums), "img", split_axis=0, concat_axis=0, tiled=True
    )
    degree = from_bucket(degree_slots)[:, 0]
    inv = lax.rsqrt(degree)
    starting = labels.astype(jnp.float32)
    current = starting
    for step in range(2):
        scaled = (inv[:, None] * current).astype(jnp.bfloat16)
        arrived = lax.all_to_all(to_bucket(scaled), "img", split_axis=0, concat_axis=0, tiled=True)
        product = jnp.einsum(
            "ajk,akc->ajc", weights, list_major(arrived), preferred_element_type=jnp.float32
        )
        returned = lax.all_to_all(
            bucket_major(product), "img", split_axis=0, concat_axis=0, tiled=True
        )
        spread = from_bucket(returned)
        current = 0.8 * inv[:, None] * spread + 0.2 * starting
    return current.astype(jnp.bfloat16)


def solution(mesh):
    return jax.shard_map(
        on_device,
        mesh=mesh,
        in_specs=(P("img", None), P("img", "sub"), P("img", None), P("img", None)),
        out_specs=P("img", "sub"),
        check_vma=False,
    )
```

```python
import jax
import jax.numpy as jnp
from jax import lax
from jax.sharding import PartitionSpec as P

SLOTS = 2048
BAND = 64
LIST_DEV = 1


def affinity(gram, row_keys, col_keys):
    keep = jnp.abs(row_keys[:, :, None] - col_keys[:, None, :]) <= BAND
    positive = jnp.maximum(gram, 0.0)
    return jnp.where(keep, positive * positive * positive, 0.0).astype(jnp.bfloat16)


def list_major(bucket):
    moved = jnp.moveaxis(bucket, 1, 0)
    return moved.reshape((moved.shape[0], moved.shape[1] * moved.shape[2]) + moved.shape[3:])


def blocked_affinity(rows, key_rows):
    lists_here = rows.shape[0]
    slot_count = rows.shape[1]
    block_rows = min(512, slot_count)
    block_count = slot_count // block_rows
    row_blocks = jnp.moveaxis(
        rows.reshape(lists_here, block_count, block_rows, rows.shape[2]), 1, 0
    )
    key_blocks = jnp.moveaxis(key_rows.reshape(lists_here, block_count, block_rows), 1, 0)

    def one_block(packed):
        picked, picked_keys = packed
        gram = jnp.einsum("ajf,akf->ajk", picked, rows, preferred_element_type=jnp.float32)
        return affinity(gram, picked_keys, key_rows)

    blocks = lax.map(one_block, (row_blocks, key_blocks))
    return jnp.moveaxis(blocks, 0, 1).reshape(lists_here, slot_count, slot_count)


def on_device(embeddings, labels, image_lists, rank_keys):
    img_count = lax.axis_size("img")
    sub_count = lax.axis_size("sub")
    per_list = SLOTS // img_count
    part = per_list // sub_count
    rows_here = image_lists.shape[0]
    pair_count = rows_here * 2
    lists_flat = image_lists.reshape(-1)
    order = jnp.arange(pair_count, dtype=jnp.int32)
    same = (lists_flat[:, None] == lists_flat[None, :]) & (order[None, :] < order[:, None])
    within = jnp.sum(same.astype(jnp.int32), axis=1)
    slot_of_pair = (lists_flat * per_list + within).reshape(rows_here, 2)
    slot_total = LIST_DEV * img_count * per_list

    slot_ids = jnp.arange(slot_total, dtype=jnp.int32)[:, None]
    hit_a = slot_of_pair[None, :, 0] == slot_ids
    hit_b = slot_of_pair[None, :, 1] == slot_ids
    hit = hit_a | hit_b
    pick = hit.astype(jnp.bfloat16)

    def to_bucket(rows):
        picked = jnp.dot(pick, rows, preferred_element_type=jnp.float32).astype(rows.dtype)
        return picked.reshape(img_count, LIST_DEV, per_list, rows.shape[1])

    def bucket_major(listed):
        shaped = listed.reshape((listed.shape[0], img_count, per_list) + listed.shape[2:])
        return jnp.moveaxis(shaped, 0, 1)

    def from_bucket(returned):
        flat = returned.reshape(slot_total, -1)
        return jnp.einsum(
            "kg,kc->gc", pick.astype(jnp.float32), flat,
            precision=lax.Precision.HIGHEST, preferred_element_type=jnp.float32,
        )

    values = embeddings.astype(jnp.float32)
    unit = (values * lax.rsqrt(jnp.sum(values * values, axis=1, keepdims=True) + 1e-06)).astype(
        jnp.bfloat16
    )
    keys_f = rank_keys.astype(jnp.float32)
    key_sum = jnp.sum(
        jnp.where(hit_a, keys_f[None, :, 0], 0.0) + jnp.where(hit_b, keys_f[None, :, 1], 0.0),
        axis=1,
    )
    key_of_slot = jnp.where(jnp.any(hit, axis=1), key_sum, -4096.0)
    slot_keys = key_of_slot.astype(jnp.bfloat16).reshape(img_count, LIST_DEV, per_list)

    me_sub = lax.axis_index("sub")
    mine = (
        jnp.arange(img_count, dtype=jnp.int32)[:, None] * per_list
        + me_sub * part
        + jnp.arange(part, dtype=jnp.int32)[None, :]
    ).reshape(-1, 1)
    pick_mine = (
        (slot_of_pair[None, :, 0] == mine) | (slot_of_pair[None, :, 1] == mine)
    ).astype(jnp.bfloat16)
    quarter = jnp.dot(pick_mine, unit, preferred_element_type=jnp.float32).astype(jnp.bfloat16)
    sent = lax.all_to_all(
        quarter.reshape(img_count, part, unit.shape[1]), "img", split_axis=0, concat_axis=0,
        tiled=True,
    )
    feats = lax.all_gather(sent, "sub", axis=1, tiled=False).reshape(
        img_count, LIST_DEV, per_list, unit.shape[1]
    )
    got_keys = lax.all_to_all(slot_keys, "img", split_axis=0, concat_axis=0, tiled=True)
    rows = list_major(feats)
    key_rows = list_major(got_keys).astype(jnp.float32)
    weights = blocked_affinity(rows, key_rows)
    row_sums = jnp.sum(weights, axis=2, dtype=jnp.float32)
    degree_slots = lax.all_to_all(
        bucket_major(row_sums), "img", split_axis=0, concat_axis=0, tiled=True
    )
    degree = jnp.sum(jnp.where(hit, degree_slots.reshape(slot_total, 1), 0.0), axis=0)
    inv = lax.rsqrt(degree)
    starting = labels.astype(jnp.float32)
    current = starting
    for step in range(2):
        scaled = (inv[:, None] * current).astype(jnp.bfloat16)
        arrived = lax.all_to_all(to_bucket(scaled), "img", split_axis=0, concat_axis=0, tiled=True)
        product = jnp.einsum(
            "ajk,akc->ajc", weights, list_major(arrived), preferred_element_type=jnp.float32
        )
        returned = lax.all_to_all(
            bucket_major(product), "img", split_axis=0, concat_axis=0, tiled=True
        )
        spread = from_bucket(returned)
        current = 0.8 * inv[:, None] * spread + 0.2 * starting
    return current.astype(jnp.bfloat16)


def solution(mesh):
    return jax.shard_map(
        on_device,
        mesh=mesh,
        in_specs=(P("img", None), P("img", "sub"), P("img", None), P("img", None)),
        out_specs=P("img", "sub"),
        check_vma=False,
    )
```

```python
import jax
import jax.numpy as jnp
from jax import lax
from jax.sharding import PartitionSpec as P

SLOTS = 2048
BAND = 64
RING_MOST = 16


def affinity(gram, row_keys, col_keys):
    keep = jnp.abs(row_keys[:, :, None] - col_keys[:, None, :]) <= BAND
    positive = jnp.maximum(gram, 0.0)
    return jnp.where(keep, positive * positive * positive, 0.0).astype(jnp.bfloat16)


def blocked_affinity(rows, key_rows):
    lists_here = rows.shape[0]
    slot_count = rows.shape[1]
    block_rows = min(512, slot_count)
    block_count = slot_count // block_rows
    row_blocks = jnp.moveaxis(
        rows.reshape(lists_here, block_count, block_rows, rows.shape[2]), 1, 0
    )
    key_blocks = jnp.moveaxis(key_rows.reshape(lists_here, block_count, block_rows), 1, 0)

    def one_block(packed):
        picked, picked_keys = packed
        gram = jnp.einsum("ajf,akf->ajk", picked, rows, preferred_element_type=jnp.float32)
        return affinity(gram, picked_keys, key_rows)

    blocks = lax.map(one_block, (row_blocks, key_blocks))
    return jnp.moveaxis(blocks, 0, 1).reshape(lists_here, slot_count, slot_count)


def on_device(embeddings, labels, image_lists, rank_keys):
    img_count = lax.axis_size("img")
    sub_count = lax.axis_size("sub")
    per_list = SLOTS // img_count
    part = per_list // sub_count
    width = embeddings.shape[1]
    rows_here = image_lists.shape[0]
    pair_count = rows_here * 2
    me_img = lax.axis_index("img")
    me_sub = lax.axis_index("sub")
    lists_flat = image_lists.reshape(-1)
    order = jnp.arange(pair_count, dtype=jnp.int32)
    same = (lists_flat[:, None] == lists_flat[None, :]) & (order[None, :] < order[:, None])
    within = jnp.sum(same.astype(jnp.int32), axis=1)
    slot_of_pair = (lists_flat * per_list + within).reshape(rows_here, 2)

    def picker(ids):
        ids = ids.reshape(-1, 1)
        return slot_of_pair[None, :, 0] == ids, slot_of_pair[None, :, 1] == ids

    shifts = jnp.arange(img_count, dtype=jnp.int32)
    ring = img_count <= RING_MOST
    dest = (me_img + shifts) % img_count if ring else shifts
    quarters = (me_sub - jnp.arange(sub_count, dtype=jnp.int32)) % sub_count
    within_part = jnp.arange(part, dtype=jnp.int32)
    bucket_ids = (
        dest[:, None, None] * per_list + quarters[None, :, None] * part + within_part[None, None, :]
    )
    hit_a, hit_b = picker(bucket_ids)
    hit = hit_a | hit_b
    pick = hit.astype(jnp.bfloat16)
    pick_f32 = hit.astype(jnp.float32)

    def over_img(blocks, back=False):
        if not ring:
            return lax.all_to_all(blocks, "img", split_axis=0, concat_axis=0, tiled=True)
        out = [blocks[0]]
        for k in range(1, img_count):
            shift = img_count - k if back else k
            pairs = [(i, (i + shift) % img_count) for i in range(img_count)]
            out.append(lax.ppermute(blocks[k], "img", pairs))
        return jnp.stack(out)

    values = embeddings.astype(jnp.float32)
    unit = (values * lax.rsqrt(jnp.sum(values * values, axis=1, keepdims=True) + 1e-06)).astype(
        jnp.bfloat16
    )
    quarter_ids = dest[:, None] * per_list + me_sub * part + within_part[None, :]
    q_a, q_b = picker(quarter_ids)
    q_hit = q_a | q_b
    keys_f = rank_keys.astype(jnp.float32)
    key_sum = jnp.sum(
        jnp.where(q_a, keys_f[None, :, 0], 0.0) + jnp.where(q_b, keys_f[None, :, 1], 0.0), axis=1
    )
    q_keys = jnp.where(jnp.any(q_hit, axis=1), key_sum, -4096.0).astype(jnp.bfloat16)
    quarter = jnp.dot(q_hit.astype(jnp.bfloat16), unit, preferred_element_type=jnp.float32)
    payload = jnp.concatenate(
        [
            quarter.astype(jnp.bfloat16).reshape(img_count, part, width),
            jnp.pad(q_keys.reshape(img_count, 1, part), ((0, 0), (0, 0), (0, width - part))),
        ],
        axis=1,
    )
    got = over_img(payload)
    gathered = [got]
    for m in range(1, sub_count):
        pairs = [(t, (t + m) % sub_count) for t in range(sub_count)]
        gathered.append(lax.ppermute(got, "sub", pairs))
    every = jnp.stack(gathered, axis=1)
    slot_count = img_count * per_list
    rows = every[:, :, :part, :].reshape(1, slot_count, width)
    key_rows = every[:, :, part, :part].reshape(1, slot_count).astype(jnp.float32)
    weights = blocked_affinity(rows, key_rows)
    row_sums = jnp.sum(weights, axis=2, dtype=jnp.float32)
    degree_slots = over_img(row_sums.reshape(img_count, per_list), back=True)
    degree = jnp.sum(jnp.where(hit, degree_slots.reshape(slot_count, 1), 0.0), axis=0)
    inv = lax.rsqrt(degree)
    starting = labels.astype(jnp.float32)
    current = starting
    channels = labels.shape[1]
    for step in range(2):
        scaled = (inv[:, None] * current).astype(jnp.bfloat16)
        bucket = jnp.dot(pick, scaled, preferred_element_type=jnp.float32).astype(jnp.bfloat16)
        arrived = over_img(bucket.reshape(img_count, per_list, channels))
        product = jnp.dot(
            weights[0], arrived.reshape(slot_count, channels), preferred_element_type=jnp.float32
        )
        returned = over_img(product.reshape(img_count, per_list, channels), back=True)
        spread = jnp.einsum(
            "kg,kc->gc", pick_f32, returned.reshape(slot_count, channels),
            precision=lax.Precision.HIGHEST, preferred_element_type=jnp.float32,
        )
        current = 0.8 * inv[:, None] * spread + 0.2 * starting
    return current.astype(jnp.bfloat16)


def solution(mesh):
    return jax.shard_map(
        on_device,
        mesh=mesh,
        in_specs=(P("img", None), P("img", "sub"), P("img", None), P("img", None)),
        out_specs=P("img", "sub"),
        check_vma=False,
    )
```

```python
import jax
import jax.numpy as jnp
from jax import lax
from jax.experimental import pallas as pl
from jax.experimental.pallas import tpu as pltpu
from jax.sharding import PartitionSpec as P

SLOTS = 2048
BAND = 64
LIST_DEV = 1


def list_major(bucket):
    moved = jnp.moveaxis(bucket, 1, 0)
    return moved.reshape((moved.shape[0], moved.shape[1] * moved.shape[2]) + moved.shape[3:])


def affinity_kernel(row_keys, col_keys, picked, rows, weights, row_sums):
    gram = lax.dot_general(
        picked[...], rows[...], (((1,), (1,)), ((), ())), preferred_element_type=jnp.float32
    )
    keep = jnp.abs(row_keys[...] - col_keys[...]) <= BAND
    positive = jnp.maximum(gram, 0.0)
    cubed = jnp.where(keep, positive * positive * positive, 0.0).astype(jnp.bfloat16)
    weights[...] = cubed
    row_sums[...] = jnp.sum(cubed.astype(jnp.float32), axis=1, keepdims=True)


def fused_affinity(rows, keys):
    slot_count, width = rows.shape
    block_rows = min(256, slot_count)
    return pl.pallas_call(
        affinity_kernel,
        grid=(slot_count // block_rows,),
        in_specs=[
            pl.BlockSpec((block_rows, 1), lambda i: (i, 0)),
            pl.BlockSpec((1, slot_count), lambda i: (0, 0)),
            pl.BlockSpec((block_rows, width), lambda i: (i, 0)),
            pl.BlockSpec((slot_count, width), lambda i: (0, 0)),
        ],
        out_specs=[
            pl.BlockSpec((block_rows, slot_count), lambda i: (i, 0)),
            pl.BlockSpec((block_rows, 1), lambda i: (i, 0)),
        ],
        out_shape=[
            jax.ShapeDtypeStruct((slot_count, slot_count), jnp.bfloat16),
            jax.ShapeDtypeStruct((slot_count, 1), jnp.float32),
        ],
        compiler_params=pltpu.CompilerParams(dimension_semantics=("arbitrary",)),
        cost_estimate=pl.CostEstimate(
            flops=2 * slot_count * slot_count * width + 6 * slot_count * slot_count,
            transcendentals=0,
            bytes_accessed=2 * slot_count * width * 2 + 2 * slot_count * slot_count,
        ),
    )(keys.reshape(slot_count, 1), keys.reshape(1, slot_count), rows, rows)


def on_device(embeddings, labels, image_lists, rank_keys):
    img_count = lax.axis_size("img")
    sub_count = lax.axis_size("sub")
    per_list = SLOTS // img_count
    part = per_list // sub_count
    rows_here = image_lists.shape[0]
    pair_count = rows_here * 2
    lists_flat = image_lists.reshape(-1)
    order = jnp.arange(pair_count, dtype=jnp.int32)
    same = (lists_flat[:, None] == lists_flat[None, :]) & (order[None, :] < order[:, None])
    within = jnp.sum(same.astype(jnp.int32), axis=1)
    slot_of_pair = (lists_flat * per_list + within).reshape(rows_here, 2)
    slot_total = LIST_DEV * img_count * per_list

    slot_ids = jnp.arange(slot_total, dtype=jnp.int32)[:, None]
    hit_a = slot_of_pair[None, :, 0] == slot_ids
    hit_b = slot_of_pair[None, :, 1] == slot_ids
    hit = hit_a | hit_b
    pick = hit.astype(jnp.bfloat16)

    def to_bucket(rows):
        picked = jnp.dot(pick, rows, preferred_element_type=jnp.float32).astype(rows.dtype)
        return picked.reshape(img_count, LIST_DEV, per_list, rows.shape[1])

    def bucket_major(listed):
        shaped = listed.reshape((listed.shape[0], img_count, per_list) + listed.shape[2:])
        return jnp.moveaxis(shaped, 0, 1)

    def from_bucket(returned):
        flat = returned.reshape(slot_total, -1)
        return jnp.einsum(
            "kg,kc->gc", pick.astype(jnp.float32), flat,
            precision=lax.Precision.HIGHEST, preferred_element_type=jnp.float32,
        )

    values = embeddings.astype(jnp.float32)
    unit = (values * lax.rsqrt(jnp.sum(values * values, axis=1, keepdims=True) + 1e-06)).astype(
        jnp.bfloat16
    )
    keys_f = rank_keys.astype(jnp.float32)
    key_sum = jnp.sum(
        jnp.where(hit_a, keys_f[None, :, 0], 0.0) + jnp.where(hit_b, keys_f[None, :, 1], 0.0),
        axis=1,
    )
    key_of_slot = jnp.where(jnp.any(hit, axis=1), key_sum, -4096.0)
    slot_keys = key_of_slot.astype(jnp.bfloat16).reshape(img_count, LIST_DEV, per_list)

    me_sub = lax.axis_index("sub")
    mine = (
        jnp.arange(img_count, dtype=jnp.int32)[:, None] * per_list
        + me_sub * part
        + jnp.arange(part, dtype=jnp.int32)[None, :]
    ).reshape(-1, 1)
    pick_mine = (
        (slot_of_pair[None, :, 0] == mine) | (slot_of_pair[None, :, 1] == mine)
    ).astype(jnp.bfloat16)
    quarter = jnp.dot(pick_mine, unit, preferred_element_type=jnp.float32).astype(jnp.bfloat16)
    sent = lax.all_to_all(
        quarter.reshape(img_count, part, unit.shape[1]), "img", split_axis=0, concat_axis=0,
        tiled=True,
    )
    feats = lax.all_gather(sent, "sub", axis=1, tiled=False).reshape(
        img_count, LIST_DEV, per_list, unit.shape[1]
    )
    got_keys = lax.all_to_all(slot_keys, "img", split_axis=0, concat_axis=0, tiled=True)
    rows = list_major(feats)
    key_rows = list_major(got_keys).astype(jnp.float32)
    lists_here, slot_count = key_rows.shape
    weight_mat, row_sum_col = fused_affinity(rows.reshape(slot_count, -1), key_rows.reshape(-1))
    weights = weight_mat.reshape(lists_here, slot_count, slot_count)
    row_sums = row_sum_col.reshape(lists_here, slot_count)
    degree_slots = lax.all_to_all(
        bucket_major(row_sums), "img", split_axis=0, concat_axis=0, tiled=True
    )
    degree = jnp.sum(jnp.where(hit, degree_slots.reshape(slot_total, 1), 0.0), axis=0)
    inv = lax.rsqrt(degree)
    starting = labels.astype(jnp.float32)
    current = starting
    for step in range(2):
        scaled = (inv[:, None] * current).astype(jnp.bfloat16)
        arrived = lax.all_to_all(to_bucket(scaled), "img", split_axis=0, concat_axis=0, tiled=True)
        product = jnp.einsum(
            "ajk,akc->ajc", weights, list_major(arrived), preferred_element_type=jnp.float32
        )
        returned = lax.all_to_all(
            bucket_major(product), "img", split_axis=0, concat_axis=0, tiled=True
        )
        spread = from_bucket(returned)
        current = 0.8 * inv[:, None] * spread + 0.2 * starting
    return current.astype(jnp.bfloat16)


def solution(mesh):
    return jax.shard_map(
        on_device,
        mesh=mesh,
        in_specs=(P("img", None), P("img", "sub"), P("img", None), P("img", None)),
        out_specs=P("img", "sub"),
        check_vma=False,
    )
```

```python
import jax
import jax.numpy as jnp
from jax import lax
from jax.experimental import pallas as pl
from jax.experimental.pallas import tpu as pltpu
from jax.sharding import PartitionSpec as P

SLOTS = 2048
BAND = 64
LIST_DEV = 1


def list_major(bucket):
    moved = jnp.moveaxis(bucket, 1, 0)
    return moved.reshape((moved.shape[0], moved.shape[1] * moved.shape[2]) + moved.shape[3:])


def affinity_kernel(row_keys, col_keys, picked, rows, weights, row_sums):
    gram = lax.dot_general(
        picked[...], rows[...], (((1,), (1,)), ((), ())), preferred_element_type=jnp.float32
    )
    keep = jnp.abs(row_keys[...] - col_keys[...]) <= BAND
    positive = jnp.maximum(gram, 0.0)
    cubed = jnp.where(keep, positive * positive * positive, 0.0).astype(jnp.bfloat16)
    weights[...] = cubed
    row_sums[...] = jnp.sum(cubed.astype(jnp.float32), axis=1, keepdims=True)


def fused_affinity(rows, keys):
    slot_count, width = rows.shape
    block_rows = min(256, slot_count)
    return pl.pallas_call(
        affinity_kernel,
        grid=(slot_count // block_rows,),
        in_specs=[
            pl.BlockSpec((block_rows, 1), lambda i: (i, 0)),
            pl.BlockSpec((1, slot_count), lambda i: (0, 0)),
            pl.BlockSpec((block_rows, width), lambda i: (i, 0)),
            pl.BlockSpec((slot_count, width), lambda i: (0, 0)),
        ],
        out_specs=[
            pl.BlockSpec((block_rows, slot_count), lambda i: (i, 0)),
            pl.BlockSpec((block_rows, 1), lambda i: (i, 0)),
        ],
        out_shape=[
            jax.ShapeDtypeStruct((slot_count, slot_count), jnp.bfloat16),
            jax.ShapeDtypeStruct((slot_count, 1), jnp.float32),
        ],
        compiler_params=pltpu.CompilerParams(dimension_semantics=("arbitrary",)),
        cost_estimate=pl.CostEstimate(
            flops=2 * slot_count * slot_count * width + 6 * slot_count * slot_count,
            transcendentals=0,
            bytes_accessed=2 * slot_count * width * 2 + 2 * slot_count * slot_count,
        ),
    )(keys.reshape(slot_count, 1), keys.reshape(1, slot_count), rows, rows)


def on_device(embeddings, labels, image_lists, rank_keys):
    img_count = lax.axis_size("img")
    sub_count = lax.axis_size("sub")
    per_list = SLOTS // img_count
    part = per_list // sub_count
    rows_here = image_lists.shape[0]
    pair_count = rows_here * 2
    lists_flat = image_lists.reshape(-1)
    order = jnp.arange(pair_count, dtype=jnp.int32)
    same = (lists_flat[:, None] == lists_flat[None, :]) & (order[None, :] < order[:, None])
    within = jnp.sum(same.astype(jnp.int32), axis=1)
    slot_of_pair = (lists_flat * per_list + within).reshape(rows_here, 2)
    slot_total = LIST_DEV * img_count * per_list

    me_sub = lax.axis_index("sub")
    quarters = (me_sub - jnp.arange(sub_count, dtype=jnp.int32)) % sub_count
    slot_ids = (
        jnp.arange(img_count, dtype=jnp.int32)[:, None, None] * per_list
        + quarters[None, :, None] * part
        + jnp.arange(part, dtype=jnp.int32)[None, None, :]
    ).reshape(-1, 1)
    hit_a = slot_of_pair[None, :, 0] == slot_ids
    hit_b = slot_of_pair[None, :, 1] == slot_ids
    hit = hit_a | hit_b
    pick = hit.astype(jnp.bfloat16)

    def to_bucket(rows):
        picked = jnp.dot(pick, rows, preferred_element_type=jnp.float32).astype(rows.dtype)
        return picked.reshape(img_count, LIST_DEV, per_list, rows.shape[1])

    def bucket_major(listed):
        shaped = listed.reshape((listed.shape[0], img_count, per_list) + listed.shape[2:])
        return jnp.moveaxis(shaped, 0, 1)

    def from_bucket(returned):
        flat = returned.reshape(slot_total, -1)
        return jnp.einsum(
            "kg,kc->gc", pick.astype(jnp.float32), flat,
            precision=lax.Precision.HIGHEST, preferred_element_type=jnp.float32,
        )

    values = embeddings.astype(jnp.float32)
    unit = (values * lax.rsqrt(jnp.sum(values * values, axis=1, keepdims=True) + 1e-06)).astype(
        jnp.bfloat16
    )
    mine = (
        jnp.arange(img_count, dtype=jnp.int32)[:, None] * per_list
        + me_sub * part
        + jnp.arange(part, dtype=jnp.int32)[None, :]
    ).reshape(-1, 1)
    mine_a = slot_of_pair[None, :, 0] == mine
    mine_b = slot_of_pair[None, :, 1] == mine
    mine_hit = mine_a | mine_b
    keys_f = rank_keys.astype(jnp.float32)
    key_sum = jnp.sum(
        jnp.where(mine_a, keys_f[None, :, 0], 0.0) + jnp.where(mine_b, keys_f[None, :, 1], 0.0),
        axis=1,
    )
    mine_keys = jnp.where(jnp.any(mine_hit, axis=1), key_sum, -4096.0).astype(jnp.bfloat16)
    width = unit.shape[1]
    quarter = jnp.dot(mine_hit.astype(jnp.bfloat16), unit, preferred_element_type=jnp.float32)
    payload = jnp.concatenate(
        [
            quarter.astype(jnp.bfloat16).reshape(img_count, part, width),
            jnp.pad(mine_keys.reshape(img_count, 1, part), ((0, 0), (0, 0), (0, width - part))),
        ],
        axis=1,
    )
    got = lax.all_to_all(payload, "img", split_axis=0, concat_axis=0, tiled=True)
    gathered = [got]
    for m in range(1, sub_count):
        pairs = [(t, (t + m) % sub_count) for t in range(sub_count)]
        gathered.append(lax.ppermute(got, "sub", pairs))
    every = jnp.stack(gathered, axis=1)
    rows = every[:, :, :part, :].reshape(1, slot_total, width)
    key_rows = every[:, :, part, :part].reshape(1, slot_total).astype(jnp.float32)
    lists_here, slot_count = key_rows.shape
    weight_mat, row_sum_col = fused_affinity(rows.reshape(slot_count, -1), key_rows.reshape(-1))
    weights = weight_mat.reshape(lists_here, slot_count, slot_count)
    row_sums = row_sum_col.reshape(lists_here, slot_count)
    degree_slots = lax.all_to_all(
        bucket_major(row_sums), "img", split_axis=0, concat_axis=0, tiled=True
    )
    degree = jnp.sum(jnp.where(hit, degree_slots.reshape(slot_total, 1), 0.0), axis=0)
    inv = lax.rsqrt(degree)
    starting = labels.astype(jnp.float32)
    current = starting
    for step in range(2):
        scaled = (inv[:, None] * current).astype(jnp.bfloat16)
        arrived = lax.all_to_all(to_bucket(scaled), "img", split_axis=0, concat_axis=0, tiled=True)
        product = jnp.einsum(
            "ajk,akc->ajc", weights, list_major(arrived), preferred_element_type=jnp.float32
        )
        returned = lax.all_to_all(
            bucket_major(product), "img", split_axis=0, concat_axis=0, tiled=True
        )
        spread = from_bucket(returned)
        current = 0.8 * inv[:, None] * spread + 0.2 * starting
    return current.astype(jnp.bfloat16)


def solution(mesh):
    return jax.shard_map(
        on_device,
        mesh=mesh,
        in_specs=(P("img", None), P("img", "sub"), P("img", None), P("img", None)),
        out_specs=P("img", "sub"),
        check_vma=False,
    )
```

```python
import jax
import jax.numpy as jnp
from jax import lax
from jax.experimental import pallas as pl
from jax.experimental.pallas import tpu as pltpu
from jax.sharding import PartitionSpec as P

SLOTS = 2048
BAND = 64
LIST_DEV = 1


def list_major(bucket):
    moved = jnp.moveaxis(bucket, 1, 0)
    return moved.reshape((moved.shape[0], moved.shape[1] * moved.shape[2]) + moved.shape[3:])


def affinity_kernel(row_keys, col_keys, picked, rows, weights, row_sums):
    gram = lax.dot_general(
        picked[...], rows[...], (((1,), (1,)), ((), ())), preferred_element_type=jnp.float32
    )
    keep = jnp.abs(row_keys[...] - col_keys[...]) <= BAND
    positive = jnp.maximum(gram, 0.0)
    cubed = jnp.where(keep, positive * positive * positive, 0.0).astype(jnp.bfloat16)
    weights[...] = cubed
    row_sums[...] = jnp.sum(cubed.astype(jnp.float32), axis=1, keepdims=True)


def fused_affinity(rows, keys):
    slot_count, width = rows.shape
    block_rows = min(256, slot_count)
    return pl.pallas_call(
        affinity_kernel,
        grid=(slot_count // block_rows,),
        in_specs=[
            pl.BlockSpec((block_rows, 1), lambda i: (i, 0)),
            pl.BlockSpec((1, slot_count), lambda i: (0, 0)),
            pl.BlockSpec((block_rows, width), lambda i: (i, 0)),
            pl.BlockSpec((slot_count, width), lambda i: (0, 0)),
        ],
        out_specs=[
            pl.BlockSpec((block_rows, slot_count), lambda i: (i, 0)),
            pl.BlockSpec((block_rows, 1), lambda i: (i, 0)),
        ],
        out_shape=[
            jax.ShapeDtypeStruct((slot_count, slot_count), jnp.bfloat16),
            jax.ShapeDtypeStruct((slot_count, 1), jnp.float32),
        ],
        compiler_params=pltpu.CompilerParams(dimension_semantics=("arbitrary",)),
        cost_estimate=pl.CostEstimate(
            flops=2 * slot_count * slot_count * width + 6 * slot_count * slot_count,
            transcendentals=0,
            bytes_accessed=2 * slot_count * width * 2 + 2 * slot_count * slot_count,
        ),
    )(keys.reshape(slot_count, 1), keys.reshape(1, slot_count), rows, rows)


def on_device(embeddings, labels, image_lists, rank_keys):
    img_count = lax.axis_size("img")
    sub_count = lax.axis_size("sub")
    per_list = SLOTS // img_count
    part = per_list // sub_count
    rows_here = image_lists.shape[0]
    pair_count = rows_here * 2
    lists_flat = image_lists.reshape(-1)
    order = jnp.arange(pair_count, dtype=jnp.int32)
    same = (lists_flat[:, None] == lists_flat[None, :]) & (order[None, :] < order[:, None])
    within = jnp.sum(same.astype(jnp.int32), axis=1)
    slot_of_pair = (lists_flat * per_list + within).reshape(rows_here, 2)
    slot_total = LIST_DEV * img_count * per_list

    arrival = [0]
    bit = sub_count // 2
    while bit >= 1:
        arrival = arrival + [d ^ bit for d in arrival]
        bit //= 2
    me_sub = lax.axis_index("sub")
    quarters = jnp.bitwise_xor(me_sub, jnp.array(arrival, dtype=jnp.int32))
    slot_ids = (
        jnp.arange(img_count, dtype=jnp.int32)[:, None, None] * per_list
        + quarters[None, :, None] * part
        + jnp.arange(part, dtype=jnp.int32)[None, None, :]
    ).reshape(-1, 1)
    hit_a = slot_of_pair[None, :, 0] == slot_ids
    hit_b = slot_of_pair[None, :, 1] == slot_ids
    hit = hit_a | hit_b
    pick = hit.astype(jnp.bfloat16)

    def to_bucket(rows):
        picked = jnp.dot(pick, rows, preferred_element_type=jnp.float32).astype(rows.dtype)
        return picked.reshape(img_count, LIST_DEV, per_list, rows.shape[1])

    def bucket_major(listed):
        shaped = listed.reshape((listed.shape[0], img_count, per_list) + listed.shape[2:])
        return jnp.moveaxis(shaped, 0, 1)

    def from_bucket(returned):
        flat = returned.reshape(slot_total, -1)
        return jnp.einsum(
            "kg,kc->gc", pick.astype(jnp.float32), flat,
            precision=lax.Precision.HIGHEST, preferred_element_type=jnp.float32,
        )

    values = embeddings.astype(jnp.float32)
    unit = (values * lax.rsqrt(jnp.sum(values * values, axis=1, keepdims=True) + 1e-06)).astype(
        jnp.bfloat16
    )
    mine = (
        jnp.arange(img_count, dtype=jnp.int32)[:, None] * per_list
        + me_sub * part
        + jnp.arange(part, dtype=jnp.int32)[None, :]
    ).reshape(-1, 1)
    mine_a = slot_of_pair[None, :, 0] == mine
    mine_b = slot_of_pair[None, :, 1] == mine
    mine_hit = mine_a | mine_b
    keys_f = rank_keys.astype(jnp.float32)
    key_sum = jnp.sum(
        jnp.where(mine_a, keys_f[None, :, 0], 0.0) + jnp.where(mine_b, keys_f[None, :, 1], 0.0),
        axis=1,
    )
    mine_keys = jnp.where(jnp.any(mine_hit, axis=1), key_sum, -4096.0).astype(jnp.bfloat16)
    width = unit.shape[1]
    quarter = jnp.dot(mine_hit.astype(jnp.bfloat16), unit, preferred_element_type=jnp.float32)
    payload = jnp.concatenate(
        [
            quarter.astype(jnp.bfloat16).reshape(img_count, part, width),
            jnp.pad(mine_keys.reshape(img_count, 1, part), ((0, 0), (0, 0), (0, width - part))),
        ],
        axis=1,
    )
    got = lax.all_to_all(payload, "img", split_axis=0, concat_axis=0, tiled=True)[:, None]
    bit = sub_count // 2
    while bit >= 1:
        pairs = [(t, t ^ bit) for t in range(sub_count)]
        got = jnp.concatenate([got, lax.ppermute(got, "sub", pairs)], axis=1)
        bit //= 2
    rows = got[:, :, :part, :].reshape(1, slot_total, width)
    key_rows = got[:, :, part, :part].reshape(1, slot_total).astype(jnp.float32)
    lists_here, slot_count = key_rows.shape
    weight_mat, row_sum_col = fused_affinity(rows.reshape(slot_count, -1), key_rows.reshape(-1))
    weights = weight_mat.reshape(lists_here, slot_count, slot_count)
    row_sums = row_sum_col.reshape(lists_here, slot_count)
    degree_slots = lax.all_to_all(
        bucket_major(row_sums), "img", split_axis=0, concat_axis=0, tiled=True
    )
    degree = jnp.sum(jnp.where(hit, degree_slots.reshape(slot_total, 1), 0.0), axis=0)
    inv = lax.rsqrt(degree)
    starting = labels.astype(jnp.float32)
    current = starting
    for step in range(2):
        scaled = (inv[:, None] * current).astype(jnp.bfloat16)
        arrived = lax.all_to_all(to_bucket(scaled), "img", split_axis=0, concat_axis=0, tiled=True)
        product = jnp.einsum(
            "ajk,akc->ajc", weights, list_major(arrived), preferred_element_type=jnp.float32
        )
        returned = lax.all_to_all(
            bucket_major(product), "img", split_axis=0, concat_axis=0, tiled=True
        )
        spread = from_bucket(returned)
        current = 0.8 * inv[:, None] * spread + 0.2 * starting
    return current.astype(jnp.bfloat16)


def solution(mesh):
    return jax.shard_map(
        on_device,
        mesh=mesh,
        in_specs=(P("img", None), P("img", "sub"), P("img", None), P("img", None)),
        out_specs=P("img", "sub"),
        check_vma=False,
    )
```

```python
import jax
import jax.numpy as jnp
from jax import lax
from jax.experimental import pallas as pl
from jax.experimental.pallas import tpu as pltpu
from jax.sharding import PartitionSpec as P

SLOTS = 2048
BAND = 64
LIST_DEV = 1


def list_major(bucket):
    moved = jnp.moveaxis(bucket, 1, 0)
    return moved.reshape((moved.shape[0], moved.shape[1] * moved.shape[2]) + moved.shape[3:])


def affinity_kernel(row_keys, col_keys, low_picked, high_picked, low_rows, high_rows, weights, row_sums):
    contract = (((1,), (1,)), ((), ()))
    gram = lax.dot_general(
        low_picked[...], low_rows[...], contract, preferred_element_type=jnp.float32
    ) + lax.dot_general(high_picked[...], high_rows[...], contract, preferred_element_type=jnp.float32)
    keep = jnp.abs(row_keys[...] - col_keys[...]) <= BAND
    positive = jnp.maximum(gram, 0.0)
    cubed = jnp.where(keep, positive * positive * positive, 0.0).astype(jnp.bfloat16)
    weights[...] = cubed
    ones = jnp.ones((8, cubed.shape[1]), jnp.bfloat16)
    summed = lax.dot_general(ones, cubed, contract, preferred_element_type=jnp.float32)
    row_sums[...] = summed[0:1, :]


def fused_affinity(low, high, keys):
    slot_count = low.shape[0]
    block_rows = min(256, slot_count)
    width = low.shape[1] + high.shape[1]
    return pl.pallas_call(
        affinity_kernel,
        grid=(slot_count // block_rows,),
        in_specs=[
            pl.BlockSpec((block_rows, 1), lambda i: (i, 0)),
            pl.BlockSpec((1, slot_count), lambda i: (0, 0)),
            pl.BlockSpec((block_rows, low.shape[1]), lambda i: (i, 0)),
            pl.BlockSpec((block_rows, high.shape[1]), lambda i: (i, 0)),
            pl.BlockSpec((slot_count, low.shape[1]), lambda i: (0, 0)),
            pl.BlockSpec((slot_count, high.shape[1]), lambda i: (0, 0)),
        ],
        out_specs=[
            pl.BlockSpec((block_rows, slot_count), lambda i: (i, 0)),
            pl.BlockSpec((1, block_rows), lambda i: (0, i)),
        ],
        out_shape=[
            jax.ShapeDtypeStruct((slot_count, slot_count), jnp.bfloat16),
            jax.ShapeDtypeStruct((1, slot_count), jnp.float32),
        ],
        compiler_params=pltpu.CompilerParams(dimension_semantics=("arbitrary",)),
        cost_estimate=pl.CostEstimate(
            flops=2 * slot_count * slot_count * width + 22 * slot_count * slot_count,
            transcendentals=0,
            bytes_accessed=2 * slot_count * width * 2 + 2 * slot_count * slot_count,
        ),
    )(keys.reshape(slot_count, 1), keys.reshape(1, slot_count), low, high, low, high)


def on_device(embeddings, labels, image_lists, rank_keys):
    img_count = lax.axis_size("img")
    sub_count = lax.axis_size("sub")
    per_list = SLOTS // img_count
    part = per_list // sub_count
    rows_here = image_lists.shape[0]
    pair_count = rows_here * 2
    lists_flat = image_lists.reshape(-1)
    order = jnp.arange(pair_count, dtype=jnp.int32)
    same = (lists_flat[:, None] == lists_flat[None, :]) & (order[None, :] < order[:, None])
    within = jnp.sum(same.astype(jnp.int32), axis=1)
    slot_of_pair = (lists_flat * per_list + within).reshape(rows_here, 2)
    slot_total = LIST_DEV * img_count * per_list

    arrival = [0]
    bit = sub_count // 2
    while bit >= 1:
        arrival = arrival + [d ^ bit for d in arrival]
        bit //= 2
    me_sub = lax.axis_index("sub")
    quarters = jnp.bitwise_xor(me_sub, jnp.array(arrival, dtype=jnp.int32))
    slot_ids = (
        jnp.arange(img_count, dtype=jnp.int32)[:, None, None] * per_list
        + quarters[None, :, None] * part
        + jnp.arange(part, dtype=jnp.int32)[None, None, :]
    ).reshape(-1, 1)
    hit_a = slot_of_pair[None, :, 0] == slot_ids
    hit_b = slot_of_pair[None, :, 1] == slot_ids
    hit = hit_a | hit_b
    pick = hit.astype(jnp.bfloat16)

    def to_bucket(rows):
        picked = jnp.dot(pick, rows, preferred_element_type=jnp.float32).astype(rows.dtype)
        return picked.reshape(img_count, LIST_DEV, per_list, rows.shape[1])

    def bucket_major(listed):
        shaped = listed.reshape((listed.shape[0], img_count, per_list) + listed.shape[2:])
        return jnp.moveaxis(shaped, 0, 1)

    def from_bucket(returned):
        flat = returned.reshape(slot_total, -1)
        return jnp.einsum(
            "kg,kc->gc", pick.astype(jnp.float32), flat,
            precision=lax.Precision.HIGHEST, preferred_element_type=jnp.float32,
        )

    values = embeddings.astype(jnp.float32)
    unit = (values * lax.rsqrt(jnp.sum(values * values, axis=1, keepdims=True) + 1e-06)).astype(
        jnp.bfloat16
    )
    mine = (
        jnp.arange(img_count, dtype=jnp.int32)[:, None] * per_list
        + me_sub * part
        + jnp.arange(part, dtype=jnp.int32)[None, :]
    ).reshape(-1, 1)
    mine_a = slot_of_pair[None, :, 0] == mine
    mine_b = slot_of_pair[None, :, 1] == mine
    mine_hit = mine_a | mine_b
    keys_f = rank_keys.astype(jnp.float32)
    key_sum = jnp.sum(
        jnp.where(mine_a, keys_f[None, :, 0], 0.0) + jnp.where(mine_b, keys_f[None, :, 1], 0.0),
        axis=1,
    )
    mine_keys = jnp.where(jnp.any(mine_hit, axis=1), key_sum, -4096.0).astype(jnp.bfloat16)
    width = unit.shape[1]
    quarter = jnp.dot(mine_hit.astype(jnp.bfloat16), unit, preferred_element_type=jnp.float32)
    half = width // 2
    quarter = quarter.astype(jnp.bfloat16).reshape(img_count, part, width)
    low_payload = jnp.concatenate(
        [
            quarter[:, :, :half],
            jnp.pad(mine_keys.reshape(img_count, 1, part), ((0, 0), (0, 0), (0, half - part))),
        ],
        axis=1,
    )
    high_payload = quarter[:, :, half:]

    def exchange_stage(got, bit):
        pairs = [(t, t ^ bit) for t in range(sub_count)]
        return jnp.concatenate([got, lax.ppermute(got, "sub", pairs)], axis=1)

    low_got = lax.all_to_all(low_payload, "img", split_axis=0, concat_axis=0, tiled=True)[:, None]
    high_got = lax.all_to_all(high_payload, "img", split_axis=0, concat_axis=0, tiled=True)[:, None]
    bit = sub_count // 2
    while bit >= 1:
        low_got = exchange_stage(low_got, bit)
        high_got = exchange_stage(high_got, bit)
        bit //= 2
    slot_count = slot_total
    low_rows = low_got[:, :, :part, :].reshape(slot_count, half)
    high_rows = high_got.reshape(slot_count, width - half)
    key_rows = low_got[:, :, part, :part].reshape(slot_count).astype(jnp.float32)
    weight_mat, row_sums = fused_affinity(low_rows, high_rows, key_rows)
    weights = weight_mat.reshape(1, slot_count, slot_count)
    degree_slots = lax.all_to_all(
        bucket_major(row_sums), "img", split_axis=0, concat_axis=0, tiled=True
    )
    degree = jnp.sum(jnp.where(hit, degree_slots.reshape(slot_total, 1), 0.0), axis=0)
    inv = lax.rsqrt(degree)
    starting = labels.astype(jnp.float32)
    current = starting
    for step in range(2):
        scaled = (inv[:, None] * current).astype(jnp.bfloat16)
        arrived = lax.all_to_all(to_bucket(scaled), "img", split_axis=0, concat_axis=0, tiled=True)
        product = jnp.einsum(
            "ajk,akc->ajc", weights, list_major(arrived), preferred_element_type=jnp.float32
        )
        returned = lax.all_to_all(
            bucket_major(product), "img", split_axis=0, concat_axis=0, tiled=True
        )
        spread = from_bucket(returned)
        current = 0.8 * inv[:, None] * spread + 0.2 * starting
    return current.astype(jnp.bfloat16)


def solution(mesh):
    return jax.shard_map(
        on_device,
        mesh=mesh,
        in_specs=(P("img", None), P("img", "sub"), P("img", None), P("img", None)),
        out_specs=P("img", "sub"),
        check_vma=False,
    )
```

```python
import jax
import jax.numpy as jnp
from jax import lax
from jax.experimental import pallas as pl
from jax.experimental.pallas import tpu as pltpu
from jax.sharding import PartitionSpec as P

SLOTS = 2048
BAND = 64
LIST_DEV = 1


def list_major(bucket):
    moved = jnp.moveaxis(bucket, 1, 0)
    return moved.reshape((moved.shape[0], moved.shape[1] * moved.shape[2]) + moved.shape[3:])


def affinity_kernel(row_keys, col_keys, picked, rows, weights, row_sums):
    contract = (((1,), (1,)), ((), ()))
    gram = lax.dot_general(picked[...], rows[...], contract, preferred_element_type=jnp.float32)
    keep = jnp.abs(row_keys[...] - col_keys[...]) <= BAND
    positive = jnp.maximum(gram, 0.0)
    cubed = jnp.where(keep, positive * positive * positive, 0.0).astype(jnp.bfloat16)
    weights[...] = cubed
    ones = jnp.ones((8, cubed.shape[1]), jnp.bfloat16)
    summed = lax.dot_general(ones, cubed, contract, preferred_element_type=jnp.float32)
    row_sums[...] = summed[0:1, :]


def fused_affinity(rows, keys):
    slot_count, width = rows.shape
    block_rows = min(256, slot_count)
    return pl.pallas_call(
        affinity_kernel,
        grid=(slot_count // block_rows,),
        in_specs=[
            pl.BlockSpec((block_rows, 1), lambda i: (i, 0)),
            pl.BlockSpec((1, slot_count), lambda i: (0, 0)),
            pl.BlockSpec((block_rows, width), lambda i: (i, 0)),
            pl.BlockSpec((slot_count, width), lambda i: (0, 0)),
        ],
        out_specs=[
            pl.BlockSpec((block_rows, slot_count), lambda i: (i, 0)),
            pl.BlockSpec((1, block_rows), lambda i: (0, i)),
        ],
        out_shape=[
            jax.ShapeDtypeStruct((slot_count, slot_count), jnp.bfloat16),
            jax.ShapeDtypeStruct((1, slot_count), jnp.float32),
        ],
        compiler_params=pltpu.CompilerParams(dimension_semantics=("arbitrary",)),
        cost_estimate=pl.CostEstimate(
            flops=2 * slot_count * slot_count * width + 22 * slot_count * slot_count,
            transcendentals=0,
            bytes_accessed=2 * slot_count * width * 2 + 2 * slot_count * slot_count,
        ),
    )(keys.reshape(slot_count, 1), keys.reshape(1, slot_count), rows, rows)


def on_device(embeddings, labels, image_lists, rank_keys):
    img_count = lax.axis_size("img")
    sub_count = lax.axis_size("sub")
    per_list = SLOTS // img_count
    part = per_list // sub_count
    rows_here = image_lists.shape[0]
    pair_count = rows_here * 2
    lists_flat = image_lists.reshape(-1)
    order = jnp.arange(pair_count, dtype=jnp.int32)
    same = (lists_flat[:, None] == lists_flat[None, :]) & (order[None, :] < order[:, None])
    within = jnp.sum(same.astype(jnp.int32), axis=1)
    slot_of_pair = (lists_flat * per_list + within).reshape(rows_here, 2)
    slot_total = LIST_DEV * img_count * per_list

    arrival = [0]
    bit = sub_count // 2
    while bit >= 1:
        arrival = arrival + [d ^ bit for d in arrival]
        bit //= 2
    me_sub = lax.axis_index("sub")
    quarters = jnp.bitwise_xor(me_sub, jnp.array(arrival, dtype=jnp.int32))
    slot_ids = (
        jnp.arange(img_count, dtype=jnp.int32)[:, None, None] * per_list
        + quarters[None, :, None] * part
        + jnp.arange(part, dtype=jnp.int32)[None, None, :]
    ).reshape(-1, 1)
    hit_a = slot_of_pair[None, :, 0] == slot_ids
    hit_b = slot_of_pair[None, :, 1] == slot_ids
    hit = hit_a | hit_b
    pick = hit.astype(jnp.bfloat16)

    def to_bucket(rows):
        picked = jnp.dot(pick, rows, preferred_element_type=jnp.float32).astype(rows.dtype)
        return picked.reshape(img_count, LIST_DEV, per_list, rows.shape[1])

    def bucket_major(listed):
        shaped = listed.reshape((listed.shape[0], img_count, per_list) + listed.shape[2:])
        return jnp.moveaxis(shaped, 0, 1)

    def from_bucket(returned):
        flat = returned.reshape(slot_total, -1)
        return jnp.einsum(
            "kg,kc->gc", pick.astype(jnp.float32), flat,
            precision=lax.Precision.HIGHEST, preferred_element_type=jnp.float32,
        )

    values = embeddings.astype(jnp.float32)
    unit = (values * lax.rsqrt(jnp.sum(values * values, axis=1, keepdims=True) + 1e-06)).astype(
        jnp.bfloat16
    )
    mine = (
        jnp.arange(img_count, dtype=jnp.int32)[:, None] * per_list
        + me_sub * part
        + jnp.arange(part, dtype=jnp.int32)[None, :]
    ).reshape(-1, 1)
    mine_a = slot_of_pair[None, :, 0] == mine
    mine_b = slot_of_pair[None, :, 1] == mine
    mine_hit = mine_a | mine_b
    keys_f = rank_keys.astype(jnp.float32)
    key_sum = jnp.sum(
        jnp.where(mine_a, keys_f[None, :, 0], 0.0) + jnp.where(mine_b, keys_f[None, :, 1], 0.0),
        axis=1,
    )
    mine_keys = jnp.where(jnp.any(mine_hit, axis=1), key_sum, -4096.0).astype(jnp.bfloat16)
    width = unit.shape[1]
    quarter = jnp.dot(mine_hit.astype(jnp.bfloat16), unit, preferred_element_type=jnp.float32)
    half = width // 2
    quarter = quarter.astype(jnp.bfloat16).reshape(img_count, part, width)
    low_payload = jnp.concatenate(
        [
            quarter[:, :, :half],
            jnp.pad(mine_keys.reshape(img_count, 1, part), ((0, 0), (0, 0), (0, half - part))),
        ],
        axis=1,
    )
    high_payload = quarter[:, :, half:]

    def exchange_stage(got, bit):
        pairs = [(t, t ^ bit) for t in range(sub_count)]
        return jnp.concatenate([got, lax.ppermute(got, "sub", pairs)], axis=1)

    low_got = lax.all_to_all(low_payload, "img", split_axis=0, concat_axis=0, tiled=True)[:, None]
    high_got = lax.all_to_all(high_payload, "img", split_axis=0, concat_axis=0, tiled=True)[:, None]
    bit = sub_count // 2
    while bit >= 1:
        low_got = exchange_stage(low_got, bit)
        high_got = exchange_stage(high_got, bit)
        bit //= 2
    slot_count = slot_total
    rows = jnp.concatenate(
        [low_got[:, :, :part, :], high_got], axis=3
    ).reshape(slot_count, width)
    key_rows = low_got[:, :, part, :part].reshape(slot_count).astype(jnp.float32)
    weight_mat, row_sums = fused_affinity(rows, key_rows)
    weights = weight_mat.reshape(1, slot_count, slot_count)
    degree_slots = lax.all_to_all(
        bucket_major(row_sums), "img", split_axis=0, concat_axis=0, tiled=True
    )
    degree = jnp.sum(jnp.where(hit, degree_slots.reshape(slot_total, 1), 0.0), axis=0)
    inv = lax.rsqrt(degree)
    starting = labels.astype(jnp.float32)
    current = starting
    for step in range(2):
        scaled = (inv[:, None] * current).astype(jnp.bfloat16)
        arrived = lax.all_to_all(to_bucket(scaled), "img", split_axis=0, concat_axis=0, tiled=True)
        product = jnp.einsum(
            "ajk,akc->ajc", weights, list_major(arrived), preferred_element_type=jnp.float32
        )
        returned = lax.all_to_all(
            bucket_major(product), "img", split_axis=0, concat_axis=0, tiled=True
        )
        spread = from_bucket(returned)
        current = 0.8 * inv[:, None] * spread + 0.2 * starting
    return current.astype(jnp.bfloat16)


def solution(mesh):
    return jax.shard_map(
        on_device,
        mesh=mesh,
        in_specs=(P("img", None), P("img", "sub"), P("img", None), P("img", None)),
        out_specs=P("img", "sub"),
        check_vma=False,
    )
```

```python
import jax
import jax.numpy as jnp
from jax import lax
from jax.experimental import pallas as pl
from jax.experimental.pallas import tpu as pltpu
from jax.sharding import PartitionSpec as P

SLOTS = 2048
BAND = 64
LIST_DEV = 1


def list_major(bucket):
    moved = jnp.moveaxis(bucket, 1, 0)
    return moved.reshape((moved.shape[0], moved.shape[1] * moved.shape[2]) + moved.shape[3:])


def affinity_kernel(row_keys, col_keys, picked, rows, weights, row_sums):
    contract = (((1,), (1,)), ((), ()))
    gram = lax.dot_general(picked[...], rows[...], contract, preferred_element_type=jnp.float32)
    keep = jnp.abs(row_keys[...] - col_keys[...]) <= BAND
    positive = jnp.maximum(gram, 0.0)
    cubed = jnp.where(keep, positive * positive * positive, 0.0).astype(jnp.bfloat16)
    weights[...] = cubed
    ones = jnp.ones((8, cubed.shape[1]), jnp.bfloat16)
    summed = lax.dot_general(ones, cubed, contract, preferred_element_type=jnp.float32)
    row_sums[...] = summed[0:1, :]


def fused_affinity(rows, keys):
    slot_count, width = rows.shape
    block_rows = min(512, slot_count)
    return pl.pallas_call(
        affinity_kernel,
        grid=(slot_count // block_rows,),
        in_specs=[
            pl.BlockSpec((block_rows, 1), lambda i: (i, 0)),
            pl.BlockSpec((1, slot_count), lambda i: (0, 0)),
            pl.BlockSpec((block_rows, width), lambda i: (i, 0)),
            pl.BlockSpec((slot_count, width), lambda i: (0, 0)),
        ],
        out_specs=[
            pl.BlockSpec((block_rows, slot_count), lambda i: (i, 0)),
            pl.BlockSpec((1, block_rows), lambda i: (0, i)),
        ],
        out_shape=[
            jax.ShapeDtypeStruct((slot_count, slot_count), jnp.bfloat16),
            jax.ShapeDtypeStruct((1, slot_count), jnp.float32),
        ],
        compiler_params=pltpu.CompilerParams(dimension_semantics=("arbitrary",)),
        cost_estimate=pl.CostEstimate(
            flops=2 * slot_count * slot_count * width + 22 * slot_count * slot_count,
            transcendentals=0,
            bytes_accessed=2 * slot_count * width * 2 + 2 * slot_count * slot_count,
        ),
    )(keys.reshape(slot_count, 1), keys.reshape(1, slot_count), rows, rows)


def product_kernel(weights, scaled_rows, product):
    product[...] = jnp.dot(weights[...], scaled_rows[...], preferred_element_type=jnp.float32)


def weighted_sum(weights, scaled_rows):
    slot_count, channels = scaled_rows.shape
    block_rows = min(512, slot_count)
    return pl.pallas_call(
        product_kernel,
        grid=(slot_count // block_rows,),
        in_specs=[
            pl.BlockSpec((block_rows, slot_count), lambda i: (i, 0)),
            pl.BlockSpec((slot_count, channels), lambda i: (0, 0)),
        ],
        out_specs=pl.BlockSpec((block_rows, channels), lambda i: (i, 0)),
        out_shape=jax.ShapeDtypeStruct((slot_count, channels), jnp.float32),
        compiler_params=pltpu.CompilerParams(dimension_semantics=("arbitrary",)),
        cost_estimate=pl.CostEstimate(
            flops=2 * slot_count * slot_count * channels,
            transcendentals=0,
            bytes_accessed=2 * slot_count * slot_count + 6 * slot_count * channels,
        ),
    )(weights, scaled_rows)


def on_device(embeddings, labels, image_lists, rank_keys):
    img_count = lax.axis_size("img")
    sub_count = lax.axis_size("sub")
    per_list = SLOTS // img_count
    part = per_list // sub_count
    rows_here = image_lists.shape[0]
    pair_count = rows_here * 2
    lists_flat = image_lists.reshape(-1)
    order = jnp.arange(pair_count, dtype=jnp.int32)
    same = (lists_flat[:, None] == lists_flat[None, :]) & (order[None, :] < order[:, None])
    within = jnp.sum(same.astype(jnp.int32), axis=1)
    slot_of_pair = (lists_flat * per_list + within).reshape(rows_here, 2)
    slot_total = LIST_DEV * img_count * per_list

    arrival = [0]
    bit = sub_count // 2
    while bit >= 1:
        arrival = arrival + [d ^ bit for d in arrival]
        bit //= 2
    me_sub = lax.axis_index("sub")
    quarters = jnp.bitwise_xor(me_sub, jnp.array(arrival, dtype=jnp.int32))
    slot_ids = (
        jnp.arange(img_count, dtype=jnp.int32)[:, None, None] * per_list
        + quarters[None, :, None] * part
        + jnp.arange(part, dtype=jnp.int32)[None, None, :]
    ).reshape(-1, 1)
    hit_a = slot_of_pair[None, :, 0] == slot_ids
    hit_b = slot_of_pair[None, :, 1] == slot_ids
    hit = hit_a | hit_b
    pick = hit.astype(jnp.bfloat16)

    def to_bucket(rows):
        picked = jnp.dot(pick, rows, preferred_element_type=jnp.float32).astype(rows.dtype)
        return picked.reshape(img_count, LIST_DEV, per_list, rows.shape[1])

    def bucket_major(listed):
        shaped = listed.reshape((listed.shape[0], img_count, per_list) + listed.shape[2:])
        return jnp.moveaxis(shaped, 0, 1)

    def from_bucket(returned):
        flat = returned.reshape(slot_total, -1)
        return jnp.einsum(
            "kg,kc->gc", pick.astype(jnp.float32), flat,
            precision=lax.Precision.HIGHEST, preferred_element_type=jnp.float32,
        )

    values = embeddings.astype(jnp.float32)
    unit = (values * lax.rsqrt(jnp.sum(values * values, axis=1, keepdims=True) + 1e-06)).astype(
        jnp.bfloat16
    )
    mine = (
        jnp.arange(img_count, dtype=jnp.int32)[:, None] * per_list
        + me_sub * part
        + jnp.arange(part, dtype=jnp.int32)[None, :]
    ).reshape(-1, 1)
    mine_a = slot_of_pair[None, :, 0] == mine
    mine_b = slot_of_pair[None, :, 1] == mine
    mine_hit = mine_a | mine_b
    keys_f = rank_keys.astype(jnp.float32)
    key_sum = jnp.sum(
        jnp.where(mine_a, keys_f[None, :, 0], 0.0) + jnp.where(mine_b, keys_f[None, :, 1], 0.0),
        axis=1,
    )
    mine_keys = jnp.where(jnp.any(mine_hit, axis=1), key_sum, -4096.0).astype(jnp.bfloat16)
    width = unit.shape[1]
    quarter = jnp.dot(mine_hit.astype(jnp.bfloat16), unit, preferred_element_type=jnp.float32)
    half = width // 2
    quarter = quarter.astype(jnp.bfloat16).reshape(img_count, part, width)
    low_payload = jnp.concatenate(
        [
            quarter[:, :, :half],
            jnp.pad(mine_keys.reshape(img_count, 1, part), ((0, 0), (0, 0), (0, half - part))),
        ],
        axis=1,
    )
    high_payload = quarter[:, :, half:]

    def exchange_stage(got, bit):
        pairs = [(t, t ^ bit) for t in range(sub_count)]
        return jnp.concatenate([got, lax.ppermute(got, "sub", pairs)], axis=1)

    low_got = lax.all_to_all(low_payload, "img", split_axis=0, concat_axis=0, tiled=True)[:, None]
    high_got = lax.all_to_all(high_payload, "img", split_axis=0, concat_axis=0, tiled=True)[:, None]
    bit = sub_count // 2
    while bit >= 1:
        low_got = exchange_stage(low_got, bit)
        high_got = exchange_stage(high_got, bit)
        bit //= 2
    slot_count = slot_total
    rows = jnp.concatenate(
        [low_got[:, :, :part, :], high_got], axis=3
    ).reshape(slot_count, width)
    key_rows = low_got[:, :, part, :part].reshape(slot_count).astype(jnp.float32)
    weight_mat, row_sums = fused_affinity(rows, key_rows)
    degree_slots = lax.all_to_all(
        bucket_major(row_sums), "img", split_axis=0, concat_axis=0, tiled=True
    )
    degree = jnp.sum(jnp.where(hit, degree_slots.reshape(slot_total, 1), 0.0), axis=0)
    inv = lax.rsqrt(degree)
    starting = labels.astype(jnp.float32)
    current = starting
    for step in range(2):
        scaled = (inv[:, None] * current).astype(jnp.bfloat16)
        arrived = lax.all_to_all(to_bucket(scaled), "img", split_axis=0, concat_axis=0, tiled=True)
        product = weighted_sum(weight_mat, list_major(arrived)[0])[None]
        returned = lax.all_to_all(
            bucket_major(product), "img", split_axis=0, concat_axis=0, tiled=True
        )
        spread = from_bucket(returned)
        current = 0.8 * inv[:, None] * spread + 0.2 * starting
    return current.astype(jnp.bfloat16)


def solution(mesh):
    return jax.shard_map(
        on_device,
        mesh=mesh,
        in_specs=(P("img", None), P("img", "sub"), P("img", None), P("img", None)),
        out_specs=P("img", "sub"),
        check_vma=False,
    )
```

```python
import jax
import jax.numpy as jnp
from jax import lax
from jax.experimental import pallas as pl
from jax.experimental.pallas import tpu as pltpu
from jax.sharding import PartitionSpec as P

SLOTS = 2048
BAND = 64
LIST_DEV = 1


def list_major(bucket):
    moved = jnp.moveaxis(bucket, 1, 0)
    return moved.reshape((moved.shape[0], moved.shape[1] * moved.shape[2]) + moved.shape[3:])


def affinity_kernel(row_keys, col_keys, picked, rows, weights, row_sums):
    contract = (((1,), (1,)), ((), ()))
    gram = lax.dot_general(picked[...], rows[...], contract, preferred_element_type=jnp.float32)
    keep = jnp.abs(row_keys[...] - col_keys[...]) <= BAND
    positive = jnp.maximum(gram, 0.0)
    cubed = jnp.where(keep, positive * positive * positive, 0.0).astype(jnp.bfloat16)
    weights[...] = cubed
    ones = jnp.ones((8, cubed.shape[1]), jnp.bfloat16)
    summed = lax.dot_general(ones, cubed, contract, preferred_element_type=jnp.float32)
    row_sums[...] = summed[0:1, :]


def fused_affinity(rows, keys):
    slot_count, width = rows.shape
    block_rows = min(512, slot_count)
    return pl.pallas_call(
        affinity_kernel,
        grid=(slot_count // block_rows,),
        in_specs=[
            pl.BlockSpec((block_rows, 1), lambda i: (i, 0)),
            pl.BlockSpec((1, slot_count), lambda i: (0, 0)),
            pl.BlockSpec((block_rows, width), lambda i: (i, 0)),
            pl.BlockSpec((slot_count, width), lambda i: (0, 0)),
        ],
        out_specs=[
            pl.BlockSpec((block_rows, slot_count), lambda i: (i, 0)),
            pl.BlockSpec((1, block_rows), lambda i: (0, i)),
        ],
        out_shape=[
            jax.ShapeDtypeStruct((slot_count, slot_count), jnp.bfloat16),
            jax.ShapeDtypeStruct((1, slot_count), jnp.float32),
        ],
        compiler_params=pltpu.CompilerParams(dimension_semantics=("arbitrary",)),
        cost_estimate=pl.CostEstimate(
            flops=2 * slot_count * slot_count * width + 22 * slot_count * slot_count,
            transcendentals=0,
            bytes_accessed=2 * slot_count * width * 2 + 2 * slot_count * slot_count,
        ),
    )(keys.reshape(slot_count, 1), keys.reshape(1, slot_count), rows, rows)


def on_device(embeddings, labels, image_lists, rank_keys):
    img_count = lax.axis_size("img")
    sub_count = lax.axis_size("sub")
    per_list = SLOTS // img_count
    part = per_list // sub_count
    rows_here = image_lists.shape[0]
    pair_count = rows_here * 2
    lists_flat = image_lists.reshape(-1)
    order = jnp.arange(pair_count, dtype=jnp.int32)
    same = (lists_flat[:, None] == lists_flat[None, :]) & (order[None, :] < order[:, None])
    within = jnp.sum(same.astype(jnp.int32), axis=1)
    slot_of_pair = (lists_flat * per_list + within).reshape(rows_here, 2)
    slot_total = LIST_DEV * img_count * per_list

    arrival = [0]
    bit = sub_count // 2
    while bit >= 1:
        arrival = arrival + [d ^ bit for d in arrival]
        bit //= 2
    me_sub = lax.axis_index("sub")
    quarters = jnp.bitwise_xor(me_sub, jnp.array(arrival, dtype=jnp.int32))
    slot_ids = (
        jnp.arange(img_count, dtype=jnp.int32)[:, None, None] * per_list
        + quarters[None, :, None] * part
        + jnp.arange(part, dtype=jnp.int32)[None, None, :]
    ).reshape(-1, 1)
    hit_a = slot_of_pair[None, :, 0] == slot_ids
    hit_b = slot_of_pair[None, :, 1] == slot_ids
    hit = hit_a | hit_b
    pick = hit.astype(jnp.bfloat16)

    def to_bucket(rows):
        picked = jnp.dot(pick, rows, preferred_element_type=jnp.float32).astype(rows.dtype)
        return picked.reshape(img_count, LIST_DEV, per_list, rows.shape[1])

    def bucket_major(listed):
        shaped = listed.reshape((listed.shape[0], img_count, per_list) + listed.shape[2:])
        return jnp.moveaxis(shaped, 0, 1)

    def from_bucket(returned):
        flat = returned.reshape(slot_total, -1)
        top = flat.astype(jnp.bfloat16)
        rest = flat - top.astype(jnp.float32)
        middle = rest.astype(jnp.bfloat16)
        bottom = (rest - middle.astype(jnp.float32)).astype(jnp.bfloat16)

        def select(piece):
            return jnp.einsum("kg,kc->gc", pick, piece, preferred_element_type=jnp.float32)

        return select(top) + select(middle) + select(bottom)

    values = embeddings.astype(jnp.float32)
    unit = (values * lax.rsqrt(jnp.sum(values * values, axis=1, keepdims=True) + 1e-06)).astype(
        jnp.bfloat16
    )
    mine = (
        jnp.arange(img_count, dtype=jnp.int32)[:, None] * per_list
        + me_sub * part
        + jnp.arange(part, dtype=jnp.int32)[None, :]
    ).reshape(-1, 1)
    mine_a = slot_of_pair[None, :, 0] == mine
    mine_b = slot_of_pair[None, :, 1] == mine
    mine_hit = mine_a | mine_b
    keys_f = rank_keys.astype(jnp.float32)
    key_sum = jnp.sum(
        jnp.where(mine_a, keys_f[None, :, 0], 0.0) + jnp.where(mine_b, keys_f[None, :, 1], 0.0),
        axis=1,
    )
    mine_keys = jnp.where(jnp.any(mine_hit, axis=1), key_sum, -4096.0).astype(jnp.bfloat16)
    width = unit.shape[1]
    quarter = jnp.dot(mine_hit.astype(jnp.bfloat16), unit, preferred_element_type=jnp.float32)
    half = width // 2
    quarter = quarter.astype(jnp.bfloat16).reshape(img_count, part, width)
    low_payload = jnp.concatenate(
        [
            quarter[:, :, :half],
            jnp.pad(mine_keys.reshape(img_count, 1, part), ((0, 0), (0, 0), (0, half - part))),
        ],
        axis=1,
    )
    high_payload = quarter[:, :, half:]

    def exchange_stage(got, bit):
        pairs = [(t, t ^ bit) for t in range(sub_count)]
        return jnp.concatenate([got, lax.ppermute(got, "sub", pairs)], axis=1)

    low_got = lax.all_to_all(low_payload, "img", split_axis=0, concat_axis=0, tiled=True)[:, None]
    high_got = lax.all_to_all(high_payload, "img", split_axis=0, concat_axis=0, tiled=True)[:, None]
    bit = sub_count // 2
    while bit >= 1:
        low_got = exchange_stage(low_got, bit)
        high_got = exchange_stage(high_got, bit)
        bit //= 2
    slot_count = slot_total
    rows = jnp.concatenate(
        [low_got[:, :, :part, :], high_got], axis=3
    ).reshape(slot_count, width)
    key_rows = low_got[:, :, part, :part].reshape(slot_count).astype(jnp.float32)
    weight_mat, row_sums = fused_affinity(rows, key_rows)
    weights = weight_mat.reshape(1, slot_count, slot_count)
    degree_slots = lax.all_to_all(
        bucket_major(row_sums), "img", split_axis=0, concat_axis=0, tiled=True
    )
    degree = jnp.sum(jnp.where(hit, degree_slots.reshape(slot_total, 1), 0.0), axis=0)
    inv = lax.rsqrt(degree)
    starting = labels.astype(jnp.float32)
    current = starting
    for step in range(2):
        scaled = (inv[:, None] * current).astype(jnp.bfloat16)
        arrived = lax.all_to_all(to_bucket(scaled), "img", split_axis=0, concat_axis=0, tiled=True)
        product = jnp.einsum(
            "ajk,akc->ajc", weights, list_major(arrived), preferred_element_type=jnp.float32
        )
        returned = lax.all_to_all(
            bucket_major(product), "img", split_axis=0, concat_axis=0, tiled=True
        )
        spread = from_bucket(returned)
        current = 0.8 * inv[:, None] * spread + 0.2 * starting
    return current.astype(jnp.bfloat16)


def solution(mesh):
    return jax.shard_map(
        on_device,
        mesh=mesh,
        in_specs=(P("img", None), P("img", "sub"), P("img", None), P("img", None)),
        out_specs=P("img", "sub"),
        check_vma=False,
    )
```

```python
import jax
import jax.numpy as jnp
from jax import lax
from jax.experimental import pallas as pl
from jax.experimental.pallas import tpu as pltpu
from jax.sharding import PartitionSpec as P

SLOTS = 2048
BAND = 64
LIST_DEV = 1


def list_major(bucket):
    moved = jnp.moveaxis(bucket, 1, 0)
    return moved.reshape((moved.shape[0], moved.shape[1] * moved.shape[2]) + moved.shape[3:])


def affinity_kernel(col_keys, low_picked, high_picked, low_rows, high_rows, weights, row_sums):
    block_rows = weights.shape[0]
    slot_count = weights.shape[1]

    def flat(ref):
        value = ref[...]
        return value.reshape(-1, value.shape[-1])

    contract = (((1,), (1,)), ((), ()))
    gram = lax.dot_general(
        flat(low_picked), flat(low_rows), contract, preferred_element_type=jnp.float32
    ) + lax.dot_general(
        flat(high_picked), flat(high_rows), contract, preferred_element_type=jnp.float32
    )
    start = pl.multiple_of(pl.program_id(0) * block_rows, block_rows)
    own_keys = col_keys[:, pl.ds(start, block_rows)]
    diagonal = (
        lax.broadcasted_iota(jnp.int32, (block_rows, block_rows), 0)
        == lax.broadcasted_iota(jnp.int32, (block_rows, block_rows), 1)
    )
    row_keys = jnp.sum(jnp.where(diagonal, own_keys, 0.0), axis=1, keepdims=True)
    keep = jnp.abs(row_keys - col_keys[...]) <= BAND
    positive = jnp.maximum(gram, 0.0)
    cubed = jnp.where(keep, positive * positive * positive, 0.0).astype(jnp.bfloat16)
    weights[...] = cubed
    ones = jnp.ones((8, slot_count), jnp.bfloat16)
    summed = lax.dot_general(ones, cubed, contract, preferred_element_type=jnp.float32)
    row_sums[...] = summed[0:1, :]


def fused_affinity(low, high, keys, part):
    sources, quarters = high.shape[0], high.shape[1]
    slot_count = sources * quarters * part
    block_rows = quarters * part
    aligned = part % 16 == 0 and block_rows % 128 == 0
    if aligned:
        def spec(array, count):
            shape = (count, quarters, part, array.shape[3])
            return pl.BlockSpec(shape, (lambda i: (i, 0, 0, 0)) if count == 1 else (lambda i: (0, 0, 0, 0)))
        operands = (low, high, low, high)
        in_specs = [spec(low, 1), spec(high, 1), spec(low, sources), spec(high, sources)]
    else:
        low = low[:, :, :part, :].reshape(slot_count, -1)
        high = high.reshape(slot_count, -1)
        block_rows = min(256, slot_count)
        operands = (low, high, low, high)
        in_specs = [
            pl.BlockSpec((block_rows, low.shape[1]), lambda i: (i, 0)),
            pl.BlockSpec((block_rows, high.shape[1]), lambda i: (i, 0)),
            pl.BlockSpec((slot_count, low.shape[1]), lambda i: (0, 0)),
            pl.BlockSpec((slot_count, high.shape[1]), lambda i: (0, 0)),
        ]
    width = low.shape[-1] + high.shape[-1]
    return pl.pallas_call(
        affinity_kernel,
        grid=(slot_count // block_rows,),
        in_specs=[pl.BlockSpec((1, slot_count), lambda i: (0, 0))] + in_specs,
        out_specs=[
            pl.BlockSpec((block_rows, slot_count), lambda i: (i, 0)),
            pl.BlockSpec((1, block_rows), lambda i: (0, i)),
        ],
        out_shape=[
            jax.ShapeDtypeStruct((slot_count, slot_count), jnp.bfloat16),
            jax.ShapeDtypeStruct((1, slot_count), jnp.float32),
        ],
        compiler_params=pltpu.CompilerParams(dimension_semantics=("arbitrary",)),
        cost_estimate=pl.CostEstimate(
            flops=2 * slot_count * slot_count * width + 22 * slot_count * slot_count,
            transcendentals=0,
            bytes_accessed=2 * slot_count * width * 2 + 2 * slot_count * slot_count,
        ),
    )(keys.reshape(1, slot_count), *operands)


def on_device(embeddings, labels, image_lists, rank_keys):
    img_count = lax.axis_size("img")
    sub_count = lax.axis_size("sub")
    per_list = SLOTS // img_count
    part = per_list // sub_count
    rows_here = image_lists.shape[0]
    pair_count = rows_here * 2
    lists_flat = image_lists.reshape(-1)
    order = jnp.arange(pair_count, dtype=jnp.int32)
    same = (lists_flat[:, None] == lists_flat[None, :]) & (order[None, :] < order[:, None])
    within = jnp.sum(same.astype(jnp.int32), axis=1)
    slot_of_pair = (lists_flat * per_list + within).reshape(rows_here, 2)
    slot_total = LIST_DEV * img_count * per_list

    arrival = [0]
    bit = sub_count // 2
    while bit >= 1:
        arrival = arrival + [d ^ bit for d in arrival]
        bit //= 2
    me_sub = lax.axis_index("sub")
    quarters = jnp.bitwise_xor(me_sub, jnp.array(arrival, dtype=jnp.int32))
    slot_ids = (
        jnp.arange(img_count, dtype=jnp.int32)[:, None, None] * per_list
        + quarters[None, :, None] * part
        + jnp.arange(part, dtype=jnp.int32)[None, None, :]
    ).reshape(-1, 1)
    hit_a = slot_of_pair[None, :, 0] == slot_ids
    hit_b = slot_of_pair[None, :, 1] == slot_ids
    hit = hit_a | hit_b
    pick = hit.astype(jnp.bfloat16)

    def to_bucket(rows):
        picked = jnp.dot(pick, rows, preferred_element_type=jnp.float32).astype(rows.dtype)
        return picked.reshape(img_count, LIST_DEV, per_list, rows.shape[1])

    def bucket_major(listed):
        shaped = listed.reshape((listed.shape[0], img_count, per_list) + listed.shape[2:])
        return jnp.moveaxis(shaped, 0, 1)

    def from_bucket(returned):
        flat = returned.reshape(slot_total, -1)
        return jnp.einsum(
            "kg,kc->gc", pick.astype(jnp.float32), flat,
            precision=lax.Precision.HIGHEST, preferred_element_type=jnp.float32,
        )

    values = embeddings.astype(jnp.float32)
    unit = (values * lax.rsqrt(jnp.sum(values * values, axis=1, keepdims=True) + 1e-06)).astype(
        jnp.bfloat16
    )
    mine = (
        jnp.arange(img_count, dtype=jnp.int32)[:, None] * per_list
        + me_sub * part
        + jnp.arange(part, dtype=jnp.int32)[None, :]
    ).reshape(-1, 1)
    mine_a = slot_of_pair[None, :, 0] == mine
    mine_b = slot_of_pair[None, :, 1] == mine
    mine_hit = mine_a | mine_b
    keys_f = rank_keys.astype(jnp.float32)
    key_sum = jnp.sum(
        jnp.where(mine_a, keys_f[None, :, 0], 0.0) + jnp.where(mine_b, keys_f[None, :, 1], 0.0),
        axis=1,
    )
    mine_keys = jnp.where(jnp.any(mine_hit, axis=1), key_sum, -4096.0).astype(jnp.bfloat16)
    width = unit.shape[1]
    quarter = jnp.dot(mine_hit.astype(jnp.bfloat16), unit, preferred_element_type=jnp.float32)
    half = width // 2
    quarter = quarter.astype(jnp.bfloat16).reshape(img_count, part, width)
    low_payload = jnp.concatenate(
        [
            quarter[:, :, :half],
            jnp.pad(mine_keys.reshape(img_count, 1, part), ((0, 0), (0, 0), (0, half - part))),
        ],
        axis=1,
    )
    high_payload = quarter[:, :, half:]

    def exchange_stage(got, bit):
        pairs = [(t, t ^ bit) for t in range(sub_count)]
        return jnp.concatenate([got, lax.ppermute(got, "sub", pairs)], axis=1)

    low_got = lax.all_to_all(low_payload, "img", split_axis=0, concat_axis=0, tiled=True)[:, None]
    high_got = lax.all_to_all(high_payload, "img", split_axis=0, concat_axis=0, tiled=True)[:, None]
    bit = sub_count // 2
    while bit >= 1:
        low_got = exchange_stage(low_got, bit)
        high_got = exchange_stage(high_got, bit)
        bit //= 2
    slot_count = slot_total
    key_rows = low_got[:, :, part, :part].reshape(slot_count).astype(jnp.float32)
    weight_mat, row_sums = fused_affinity(low_got, high_got, key_rows, part)
    weights = weight_mat.reshape(1, slot_count, slot_count)
    degree_slots = lax.all_to_all(
        bucket_major(row_sums), "img", split_axis=0, concat_axis=0, tiled=True
    )
    degree = jnp.sum(jnp.where(hit, degree_slots.reshape(slot_total, 1), 0.0), axis=0)
    inv = lax.rsqrt(degree)
    starting = labels.astype(jnp.float32)
    current = starting
    for step in range(2):
        scaled = (inv[:, None] * current).astype(jnp.bfloat16)
        arrived = lax.all_to_all(to_bucket(scaled), "img", split_axis=0, concat_axis=0, tiled=True)
        product = jnp.einsum(
            "ajk,akc->ajc", weights, list_major(arrived), preferred_element_type=jnp.float32
        )
        returned = lax.all_to_all(
            bucket_major(product), "img", split_axis=0, concat_axis=0, tiled=True
        )
        spread = from_bucket(returned)
        current = 0.8 * inv[:, None] * spread + 0.2 * starting
    return current.astype(jnp.bfloat16)


def solution(mesh):
    return jax.shard_map(
        on_device,
        mesh=mesh,
        in_specs=(P("img", None), P("img", "sub"), P("img", None), P("img", None)),
        out_specs=P("img", "sub"),
        check_vma=False,
    )
```

```python
import jax
import jax.numpy as jnp
from jax import lax
from jax.experimental import pallas as pl
from jax.experimental.pallas import tpu as pltpu
from jax.sharding import PartitionSpec as P

SLOTS = 2048
BAND = 64
LIST_DEV = 1


def list_major(bucket):
    moved = jnp.moveaxis(bucket, 1, 0)
    return moved.reshape((moved.shape[0], moved.shape[1] * moved.shape[2]) + moved.shape[3:])


def affinity_kernel(col_keys, low_rows, high_rows, weights, row_sums, joined):
    block_rows = weights.shape[0]
    slot_count = weights.shape[1]
    half = joined.shape[1] - high_rows.shape[-1]

    @pl.when(pl.program_id(0) == 0)
    def _():
        low = low_rows[...]
        high = high_rows[...]
        joined[:, :half] = low.reshape(slot_count, low.shape[-1])[:, :half]
        joined[:, half:] = high.reshape(slot_count, high.shape[-1])

    start = pl.multiple_of(pl.program_id(0) * block_rows, block_rows)
    contract = (((1,), (1,)), ((), ()))
    gram = lax.dot_general(
        joined[pl.ds(start, block_rows), :], joined[...], contract,
        preferred_element_type=jnp.float32,
    )
    own_keys = col_keys[:, pl.ds(start, block_rows)]
    diagonal = (
        lax.broadcasted_iota(jnp.int32, (block_rows, block_rows), 0)
        == lax.broadcasted_iota(jnp.int32, (block_rows, block_rows), 1)
    )
    row_keys = jnp.sum(jnp.where(diagonal, own_keys, 0.0), axis=1, keepdims=True)
    keep = jnp.abs(row_keys - col_keys[...]) <= BAND
    positive = jnp.maximum(gram, 0.0)
    cubed = jnp.where(keep, positive * positive * positive, 0.0).astype(jnp.bfloat16)
    weights[...] = cubed
    ones = jnp.ones((8, slot_count), jnp.bfloat16)
    summed = lax.dot_general(ones, cubed, contract, preferred_element_type=jnp.float32)
    row_sums[...] = summed[0:1, :]


def fused_affinity(low, high, keys, part):
    sources, quarters = high.shape[0], high.shape[1]
    slot_count = sources * quarters * part
    half = low.shape[3]
    width = half + high.shape[3]
    if part % 16 == 0:
        low_spec = pl.BlockSpec((sources, quarters, part, half), lambda i: (0, 0, 0, 0))
        high_spec = pl.BlockSpec(high.shape, lambda i: (0, 0, 0, 0))
    else:
        low = low[:, :, :part, :].reshape(slot_count, half)
        high = high.reshape(slot_count, width - half)
        low_spec = pl.BlockSpec(low.shape, lambda i: (0, 0))
        high_spec = pl.BlockSpec(high.shape, lambda i: (0, 0))
    block_rows = min(512, slot_count)
    return pl.pallas_call(
        affinity_kernel,
        grid=(slot_count // block_rows,),
        in_specs=[pl.BlockSpec((1, slot_count), lambda i: (0, 0)), low_spec, high_spec],
        out_specs=[
            pl.BlockSpec((block_rows, slot_count), lambda i: (i, 0)),
            pl.BlockSpec((1, block_rows), lambda i: (0, i)),
        ],
        out_shape=[
            jax.ShapeDtypeStruct((slot_count, slot_count), jnp.bfloat16),
            jax.ShapeDtypeStruct((1, slot_count), jnp.float32),
        ],
        scratch_shapes=[pltpu.VMEM((slot_count, width), jnp.bfloat16)],
        compiler_params=pltpu.CompilerParams(dimension_semantics=("arbitrary",)),
        cost_estimate=pl.CostEstimate(
            flops=2 * slot_count * slot_count * width + 22 * slot_count * slot_count,
            transcendentals=0,
            bytes_accessed=slot_count * width * 2 + 2 * slot_count * slot_count,
        ),
    )(keys.reshape(1, slot_count), low, high)


def on_device(embeddings, labels, image_lists, rank_keys):
    img_count = lax.axis_size("img")
    sub_count = lax.axis_size("sub")
    per_list = SLOTS // img_count
    part = per_list // sub_count
    rows_here = image_lists.shape[0]
    pair_count = rows_here * 2
    lists_flat = image_lists.reshape(-1)
    order = jnp.arange(pair_count, dtype=jnp.int32)
    same = (lists_flat[:, None] == lists_flat[None, :]) & (order[None, :] < order[:, None])
    within = jnp.sum(same.astype(jnp.int32), axis=1)
    slot_of_pair = (lists_flat * per_list + within).reshape(rows_here, 2)
    slot_total = LIST_DEV * img_count * per_list

    arrival = [0]
    bit = sub_count // 2
    while bit >= 1:
        arrival = arrival + [d ^ bit for d in arrival]
        bit //= 2
    me_sub = lax.axis_index("sub")
    quarters = jnp.bitwise_xor(me_sub, jnp.array(arrival, dtype=jnp.int32))
    slot_ids = (
        jnp.arange(img_count, dtype=jnp.int32)[:, None, None] * per_list
        + quarters[None, :, None] * part
        + jnp.arange(part, dtype=jnp.int32)[None, None, :]
    ).reshape(-1, 1)
    hit_a = slot_of_pair[None, :, 0] == slot_ids
    hit_b = slot_of_pair[None, :, 1] == slot_ids
    hit = hit_a | hit_b
    pick = hit.astype(jnp.bfloat16)

    def to_bucket(rows):
        picked = jnp.dot(pick, rows, preferred_element_type=jnp.float32).astype(rows.dtype)
        return picked.reshape(img_count, LIST_DEV, per_list, rows.shape[1])

    def bucket_major(listed):
        shaped = listed.reshape((listed.shape[0], img_count, per_list) + listed.shape[2:])
        return jnp.moveaxis(shaped, 0, 1)

    def from_bucket(returned):
        flat = returned.reshape(slot_total, -1)
        return jnp.einsum(
            "kg,kc->gc", pick.astype(jnp.float32), flat,
            precision=lax.Precision.HIGHEST, preferred_element_type=jnp.float32,
        )

    values = embeddings.astype(jnp.float32)
    unit = (values * lax.rsqrt(jnp.sum(values * values, axis=1, keepdims=True) + 1e-06)).astype(
        jnp.bfloat16
    )
    mine = (
        jnp.arange(img_count, dtype=jnp.int32)[:, None] * per_list
        + me_sub * part
        + jnp.arange(part, dtype=jnp.int32)[None, :]
    ).reshape(-1, 1)
    mine_a = slot_of_pair[None, :, 0] == mine
    mine_b = slot_of_pair[None, :, 1] == mine
    mine_hit = mine_a | mine_b
    keys_f = rank_keys.astype(jnp.float32)
    key_sum = jnp.sum(
        jnp.where(mine_a, keys_f[None, :, 0], 0.0) + jnp.where(mine_b, keys_f[None, :, 1], 0.0),
        axis=1,
    )
    mine_keys = jnp.where(jnp.any(mine_hit, axis=1), key_sum, -4096.0).astype(jnp.bfloat16)
    width = unit.shape[1]
    quarter = jnp.dot(mine_hit.astype(jnp.bfloat16), unit, preferred_element_type=jnp.float32)
    half = width // 2
    quarter = quarter.astype(jnp.bfloat16).reshape(img_count, part, width)
    low_payload = jnp.concatenate(
        [
            quarter[:, :, :half],
            jnp.pad(mine_keys.reshape(img_count, 1, part), ((0, 0), (0, 0), (0, half - part))),
        ],
        axis=1,
    )
    high_payload = quarter[:, :, half:]

    def exchange_stage(got, bit):
        pairs = [(t, t ^ bit) for t in range(sub_count)]
        return jnp.concatenate([got, lax.ppermute(got, "sub", pairs)], axis=1)

    low_got = lax.all_to_all(low_payload, "img", split_axis=0, concat_axis=0, tiled=True)[:, None]
    high_got = lax.all_to_all(high_payload, "img", split_axis=0, concat_axis=0, tiled=True)[:, None]
    bit = sub_count // 2
    while bit >= 1:
        low_got = exchange_stage(low_got, bit)
        high_got = exchange_stage(high_got, bit)
        bit //= 2
    slot_count = slot_total
    key_rows = low_got[:, :, part, :part].reshape(slot_count).astype(jnp.float32)
    weight_mat, row_sums = fused_affinity(low_got, high_got, key_rows, part)
    weights = weight_mat.reshape(1, slot_count, slot_count)
    degree_slots = lax.all_to_all(
        bucket_major(row_sums), "img", split_axis=0, concat_axis=0, tiled=True
    )
    degree = jnp.sum(jnp.where(hit, degree_slots.reshape(slot_total, 1), 0.0), axis=0)
    inv = lax.rsqrt(degree)
    starting = labels.astype(jnp.float32)
    current = starting
    for step in range(2):
        scaled = (inv[:, None] * current).astype(jnp.bfloat16)
        arrived = lax.all_to_all(to_bucket(scaled), "img", split_axis=0, concat_axis=0, tiled=True)
        product = jnp.einsum(
            "ajk,akc->ajc", weights, list_major(arrived), preferred_element_type=jnp.float32
        )
        returned = lax.all_to_all(
            bucket_major(product), "img", split_axis=0, concat_axis=0, tiled=True
        )
        spread = from_bucket(returned)
        current = 0.8 * inv[:, None] * spread + 0.2 * starting
    return current.astype(jnp.bfloat16)


def solution(mesh):
    return jax.shard_map(
        on_device,
        mesh=mesh,
        in_specs=(P("img", None), P("img", "sub"), P("img", None), P("img", None)),
        out_specs=P("img", "sub"),
        check_vma=False,
    )
```

```python
import jax
import jax.numpy as jnp
from jax import lax
from jax.experimental import pallas as pl
from jax.experimental.pallas import tpu as pltpu
from jax.sharding import PartitionSpec as P

SLOTS = 2048
BAND = 64
LIST_DEV = 1


def list_major(bucket):
    moved = jnp.moveaxis(bucket, 1, 0)
    return moved.reshape((moved.shape[0], moved.shape[1] * moved.shape[2]) + moved.shape[3:])


def affinity_kernel(col_keys, low_rows, high_rows, weights, row_sums, joined):
    block_rows = weights.shape[0]
    slot_count = weights.shape[1]
    half = joined.shape[1] - high_rows.shape[-1]

    @pl.when(pl.program_id(0) == 0)
    def _():
        low = low_rows[...]
        high = high_rows[...]
        joined[:, :half] = low.reshape(slot_count, low.shape[-1])[:, :half]
        joined[:, half:] = high.reshape(slot_count, high.shape[-1])

    start = pl.multiple_of(pl.program_id(0) * block_rows, block_rows)
    contract = (((1,), (1,)), ((), ()))
    gram = lax.dot_general(
        joined[pl.ds(start, block_rows), :], joined[...], contract,
        preferred_element_type=jnp.float32,
    )
    own_keys = col_keys[:, pl.ds(start, block_rows)]
    diagonal = (
        lax.broadcasted_iota(jnp.int32, (block_rows, block_rows), 0)
        == lax.broadcasted_iota(jnp.int32, (block_rows, block_rows), 1)
    )
    row_keys = jnp.sum(jnp.where(diagonal, own_keys, 0.0), axis=1, keepdims=True)
    keep = jnp.abs(row_keys - col_keys[...]) <= BAND
    positive = jnp.maximum(gram, 0.0)
    cubed = jnp.where(keep, positive * positive * positive, 0.0).astype(jnp.bfloat16)
    weights[...] = cubed
    ones = jnp.ones((8, slot_count), jnp.bfloat16)
    summed = lax.dot_general(ones, cubed, contract, preferred_element_type=jnp.float32)
    row_sums[...] = summed[0:1, :]


def fused_affinity(low, high, keys, part):
    sources, quarters = high.shape[0], high.shape[1]
    slot_count = sources * quarters * part
    half = low.shape[3]
    width = half + high.shape[3]
    if part % 16 == 0:
        low_spec = pl.BlockSpec((sources, quarters, part, half), lambda i: (0, 0, 0, 0))
        high_spec = pl.BlockSpec(high.shape, lambda i: (0, 0, 0, 0))
    else:
        low = low[:, :, :part, :].reshape(slot_count, half)
        high = high.reshape(slot_count, width - half)
        low_spec = pl.BlockSpec(low.shape, lambda i: (0, 0))
        high_spec = pl.BlockSpec(high.shape, lambda i: (0, 0))
    block_rows = min(512, slot_count)
    return pl.pallas_call(
        affinity_kernel,
        grid=(slot_count // block_rows,),
        in_specs=[pl.BlockSpec((1, slot_count), lambda i: (0, 0)), low_spec, high_spec],
        out_specs=[
            pl.BlockSpec((block_rows, slot_count), lambda i: (i, 0)),
            pl.BlockSpec((1, block_rows), lambda i: (0, i)),
        ],
        out_shape=[
            jax.ShapeDtypeStruct((slot_count, slot_count), jnp.bfloat16),
            jax.ShapeDtypeStruct((1, slot_count), jnp.float32),
        ],
        scratch_shapes=[pltpu.VMEM((slot_count, width), jnp.bfloat16)],
        compiler_params=pltpu.CompilerParams(dimension_semantics=("arbitrary",)),
        cost_estimate=pl.CostEstimate(
            flops=2 * slot_count * slot_count * width + 22 * slot_count * slot_count,
            transcendentals=0,
            bytes_accessed=slot_count * width * 2 + 2 * slot_count * slot_count,
        ),
    )(keys.reshape(1, slot_count), low, high)


def on_device(embeddings, labels, image_lists, rank_keys):
    img_count = lax.axis_size("img")
    sub_count = lax.axis_size("sub")
    per_list = SLOTS // img_count
    part = per_list // sub_count
    rows_here = image_lists.shape[0]
    pair_count = rows_here * 2
    lists_flat = image_lists.reshape(-1)
    order = jnp.arange(pair_count, dtype=jnp.int32)
    same = (lists_flat[:, None] == lists_flat[None, :]) & (order[None, :] < order[:, None])
    within = jnp.sum(same.astype(jnp.int32), axis=1)
    slot_of_pair = (lists_flat * per_list + within).reshape(rows_here, 2)
    slot_total = LIST_DEV * img_count * per_list

    arrival = [0]
    bit = sub_count // 2
    while bit >= 1:
        arrival = arrival + [d ^ bit for d in arrival]
        bit //= 2
    me_sub = lax.axis_index("sub")
    quarters = jnp.bitwise_xor(me_sub, jnp.array(arrival, dtype=jnp.int32))
    slot_ids = (
        jnp.arange(img_count, dtype=jnp.int32)[:, None, None] * per_list
        + quarters[None, :, None] * part
        + jnp.arange(part, dtype=jnp.int32)[None, None, :]
    ).reshape(-1, 1)
    hit_a = slot_of_pair[None, :, 0] == slot_ids
    hit_b = slot_of_pair[None, :, 1] == slot_ids
    hit = hit_a | hit_b
    pick = hit.astype(jnp.bfloat16)

    def to_bucket(rows):
        picked = jnp.dot(pick, rows, preferred_element_type=jnp.float32).astype(rows.dtype)
        return picked.reshape(img_count, LIST_DEV, per_list, rows.shape[1])

    def bucket_major(listed):
        shaped = listed.reshape((listed.shape[0], img_count, per_list) + listed.shape[2:])
        return jnp.moveaxis(shaped, 0, 1)

    def from_bucket(returned):
        flat = returned.reshape(slot_total, -1)
        return jnp.einsum(
            "kg,kc->gc", pick.astype(jnp.float32), flat,
            precision=lax.Precision.HIGHEST, preferred_element_type=jnp.float32,
        )

    values = embeddings.astype(jnp.float32)
    unit = (values * lax.rsqrt(jnp.sum(values * values, axis=1, keepdims=True) + 1e-06)).astype(
        jnp.bfloat16
    )
    mine = (
        jnp.arange(img_count, dtype=jnp.int32)[:, None] * per_list
        + me_sub * part
        + jnp.arange(part, dtype=jnp.int32)[None, :]
    ).reshape(-1, 1)
    mine_a = slot_of_pair[None, :, 0] == mine
    mine_b = slot_of_pair[None, :, 1] == mine
    mine_hit = mine_a | mine_b
    keys_f = rank_keys.astype(jnp.float32)
    key_sum = jnp.sum(
        jnp.where(mine_a, keys_f[None, :, 0], 0.0) + jnp.where(mine_b, keys_f[None, :, 1], 0.0),
        axis=1,
    )
    mine_keys = jnp.where(jnp.any(mine_hit, axis=1), key_sum, -4096.0).astype(jnp.bfloat16)
    width = unit.shape[1]
    quarter = jnp.dot(mine_hit.astype(jnp.bfloat16), unit, preferred_element_type=jnp.float32)
    half = max(128, width // 3 // 128 * 128)
    quarter = quarter.astype(jnp.bfloat16).reshape(img_count, part, width)
    low_payload = jnp.concatenate(
        [
            quarter[:, :, :half],
            jnp.pad(mine_keys.reshape(img_count, 1, part), ((0, 0), (0, 0), (0, half - part))),
        ],
        axis=1,
    )
    high_payload = quarter[:, :, half:]

    def exchange_stage(got, bit):
        pairs = [(t, t ^ bit) for t in range(sub_count)]
        return jnp.concatenate([got, lax.ppermute(got, "sub", pairs)], axis=1)

    low_got = lax.all_to_all(low_payload, "img", split_axis=0, concat_axis=0, tiled=True)[:, None]
    high_got = lax.all_to_all(high_payload, "img", split_axis=0, concat_axis=0, tiled=True)[:, None]
    bit = sub_count // 2
    while bit >= 1:
        low_got = exchange_stage(low_got, bit)
        high_got = exchange_stage(high_got, bit)
        bit //= 2
    slot_count = slot_total
    key_rows = low_got[:, :, part, :part].reshape(slot_count).astype(jnp.float32)
    weight_mat, row_sums = fused_affinity(low_got, high_got, key_rows, part)
    weights = weight_mat.reshape(1, slot_count, slot_count)
    degree_slots = lax.all_to_all(
        bucket_major(row_sums), "img", split_axis=0, concat_axis=0, tiled=True
    )
    degree = jnp.sum(jnp.where(hit, degree_slots.reshape(slot_total, 1), 0.0), axis=0)
    inv = lax.rsqrt(degree)
    starting = labels.astype(jnp.float32)
    current = starting
    for step in range(2):
        scaled = (inv[:, None] * current).astype(jnp.bfloat16)
        arrived = lax.all_to_all(to_bucket(scaled), "img", split_axis=0, concat_axis=0, tiled=True)
        product = jnp.einsum(
            "ajk,akc->ajc", weights, list_major(arrived), preferred_element_type=jnp.float32
        )
        returned = lax.all_to_all(
            bucket_major(product), "img", split_axis=0, concat_axis=0, tiled=True
        )
        spread = from_bucket(returned)
        current = 0.8 * inv[:, None] * spread + 0.2 * starting
    return current.astype(jnp.bfloat16)


def solution(mesh):
    return jax.shard_map(
        on_device,
        mesh=mesh,
        in_specs=(P("img", None), P("img", "sub"), P("img", None), P("img", None)),
        out_specs=P("img", "sub"),
        check_vma=False,
    )
```

```python
import jax
import jax.numpy as jnp
from jax import lax
from jax.experimental import pallas as pl
from jax.experimental.pallas import tpu as pltpu
from jax.sharding import PartitionSpec as P

SLOTS = 2048
BAND = 64
LIST_DEV = 1


def list_major(bucket):
    moved = jnp.moveaxis(bucket, 1, 0)
    return moved.reshape((moved.shape[0], moved.shape[1] * moved.shape[2]) + moved.shape[3:])


def affinity_kernel(col_keys, low_rows, high_rows, weights, row_sums, joined):
    block_rows = weights.shape[0]
    slot_count = weights.shape[1]
    half = joined.shape[1] - high_rows.shape[-1]

    @pl.when(pl.program_id(0) == 0)
    def _():
        low = low_rows[...]
        high = high_rows[...]
        joined[:, :half] = low.reshape(slot_count, low.shape[-1])[:, :half]
        joined[:, half:] = high.reshape(slot_count, high.shape[-1])

    start = pl.multiple_of(pl.program_id(0) * block_rows, block_rows)
    contract = (((1,), (1,)), ((), ()))
    gram = lax.dot_general(
        joined[pl.ds(start, block_rows), :], joined[...], contract,
        preferred_element_type=jnp.float32,
    )
    own_keys = col_keys[:, pl.ds(start, block_rows)]
    diagonal = (
        lax.broadcasted_iota(jnp.int32, (block_rows, block_rows), 0)
        == lax.broadcasted_iota(jnp.int32, (block_rows, block_rows), 1)
    )
    row_keys = jnp.sum(jnp.where(diagonal, own_keys, 0.0), axis=1, keepdims=True)
    keep = jnp.abs(row_keys - col_keys[...]) <= BAND
    positive = jnp.maximum(gram, 0.0)
    cubed = jnp.where(keep, positive * positive * positive, 0.0).astype(jnp.bfloat16)
    weights[...] = cubed
    ones = jnp.ones((8, slot_count), jnp.bfloat16)
    summed = lax.dot_general(ones, cubed, contract, preferred_element_type=jnp.float32)
    row_sums[...] = summed[0:1, :]


def fused_affinity(low, high, keys, part):
    sources, quarters = high.shape[0], high.shape[1]
    slot_count = sources * quarters * part
    half = low.shape[3]
    width = half + high.shape[3]
    if part % 16 == 0:
        low_spec = pl.BlockSpec((sources, quarters, part, half), lambda i: (0, 0, 0, 0))
        high_spec = pl.BlockSpec(high.shape, lambda i: (0, 0, 0, 0))
    else:
        low = low[:, :, :part, :].reshape(slot_count, half)
        high = high.reshape(slot_count, width - half)
        low_spec = pl.BlockSpec(low.shape, lambda i: (0, 0))
        high_spec = pl.BlockSpec(high.shape, lambda i: (0, 0))
    block_rows = min(512, slot_count)
    return pl.pallas_call(
        affinity_kernel,
        grid=(slot_count // block_rows,),
        in_specs=[pl.BlockSpec((1, slot_count), lambda i: (0, 0)), low_spec, high_spec],
        out_specs=[
            pl.BlockSpec((block_rows, slot_count), lambda i: (i, 0)),
            pl.BlockSpec((1, block_rows), lambda i: (0, i)),
        ],
        out_shape=[
            jax.ShapeDtypeStruct((slot_count, slot_count), jnp.bfloat16),
            jax.ShapeDtypeStruct((1, slot_count), jnp.float32),
        ],
        scratch_shapes=[pltpu.VMEM((slot_count, width), jnp.bfloat16)],
        compiler_params=pltpu.CompilerParams(dimension_semantics=("arbitrary",)),
        cost_estimate=pl.CostEstimate(
            flops=2 * slot_count * slot_count * width + 22 * slot_count * slot_count,
            transcendentals=0,
            bytes_accessed=slot_count * width * 2 + 2 * slot_count * slot_count,
        ),
    )(keys.reshape(1, slot_count), low, high)


def on_device(embeddings, labels, image_lists, rank_keys):
    img_count = lax.axis_size("img")
    sub_count = lax.axis_size("sub")
    per_list = SLOTS // img_count
    part = per_list // sub_count
    rows_here = image_lists.shape[0]
    pair_count = rows_here * 2
    lists_flat = image_lists.reshape(-1)
    order = jnp.arange(pair_count, dtype=jnp.int32)
    same = (lists_flat[:, None] == lists_flat[None, :]) & (order[None, :] < order[:, None])
    within = jnp.sum(same.astype(jnp.int32), axis=1)
    slot_of_pair = (lists_flat * per_list + within).reshape(rows_here, 2)
    slot_total = LIST_DEV * img_count * per_list

    arrival = [0]
    bit = sub_count // 2
    while bit >= 1:
        arrival = arrival + [d ^ bit for d in arrival]
        bit //= 2
    me_sub = lax.axis_index("sub")
    quarters = jnp.bitwise_xor(me_sub, jnp.array(arrival, dtype=jnp.int32))
    slot_ids = (
        jnp.arange(img_count, dtype=jnp.int32)[:, None, None] * per_list
        + quarters[None, :, None] * part
        + jnp.arange(part, dtype=jnp.int32)[None, None, :]
    ).reshape(-1, 1)
    hit_a = slot_of_pair[None, :, 0] == slot_ids
    hit_b = slot_of_pair[None, :, 1] == slot_ids
    hit = hit_a | hit_b
    pick = hit.astype(jnp.bfloat16)

    def to_bucket(rows):
        picked = jnp.dot(pick, rows, preferred_element_type=jnp.float32).astype(rows.dtype)
        return picked.reshape(img_count, LIST_DEV, per_list, rows.shape[1])

    def bucket_major(listed):
        shaped = listed.reshape((listed.shape[0], img_count, per_list) + listed.shape[2:])
        return jnp.moveaxis(shaped, 0, 1)

    def from_bucket(returned):
        flat = returned.reshape(slot_total, -1)
        return jnp.einsum(
            "kg,kc->gc", pick.astype(jnp.float32), flat,
            precision=lax.Precision.HIGH, preferred_element_type=jnp.float32,
        )

    values = embeddings.astype(jnp.float32)
    unit = (values * lax.rsqrt(jnp.sum(values * values, axis=1, keepdims=True) + 1e-06)).astype(
        jnp.bfloat16
    )
    mine = (
        jnp.arange(img_count, dtype=jnp.int32)[:, None] * per_list
        + me_sub * part
        + jnp.arange(part, dtype=jnp.int32)[None, :]
    ).reshape(-1, 1)
    mine_a = slot_of_pair[None, :, 0] == mine
    mine_b = slot_of_pair[None, :, 1] == mine
    mine_hit = mine_a | mine_b
    keys_f = rank_keys.astype(jnp.float32)
    key_sum = jnp.sum(
        jnp.where(mine_a, keys_f[None, :, 0], 0.0) + jnp.where(mine_b, keys_f[None, :, 1], 0.0),
        axis=1,
    )
    mine_keys = jnp.where(jnp.any(mine_hit, axis=1), key_sum, -4096.0).astype(jnp.bfloat16)
    width = unit.shape[1]
    quarter = jnp.dot(mine_hit.astype(jnp.bfloat16), unit, preferred_element_type=jnp.float32)
    half = max(128, width // 3 // 128 * 128)
    quarter = quarter.astype(jnp.bfloat16).reshape(img_count, part, width)
    low_payload = jnp.concatenate(
        [
            quarter[:, :, :half],
            jnp.pad(mine_keys.reshape(img_count, 1, part), ((0, 0), (0, 0), (0, half - part))),
        ],
        axis=1,
    )
    high_payload = quarter[:, :, half:]

    def exchange_stage(got, bit):
        pairs = [(t, t ^ bit) for t in range(sub_count)]
        return jnp.concatenate([got, lax.ppermute(got, "sub", pairs)], axis=1)

    low_got = lax.all_to_all(low_payload, "img", split_axis=0, concat_axis=0, tiled=True)[:, None]
    high_got = lax.all_to_all(high_payload, "img", split_axis=0, concat_axis=0, tiled=True)[:, None]
    bit = sub_count // 2
    while bit >= 1:
        low_got = exchange_stage(low_got, bit)
        high_got = exchange_stage(high_got, bit)
        bit //= 2
    slot_count = slot_total
    key_rows = low_got[:, :, part, :part].reshape(slot_count).astype(jnp.float32)
    weight_mat, row_sums = fused_affinity(low_got, high_got, key_rows, part)
    weights = weight_mat.reshape(1, slot_count, slot_count)
    degree_slots = lax.all_to_all(
        bucket_major(row_sums), "img", split_axis=0, concat_axis=0, tiled=True
    )
    degree = jnp.sum(jnp.where(hit, degree_slots.reshape(slot_total, 1), 0.0), axis=0)
    inv = lax.rsqrt(degree)
    starting = labels.astype(jnp.float32)
    current = starting
    for step in range(2):
        scaled = (inv[:, None] * current).astype(jnp.bfloat16)
        arrived = lax.all_to_all(to_bucket(scaled), "img", split_axis=0, concat_axis=0, tiled=True)
        product = jnp.einsum(
            "ajk,akc->ajc", weights, list_major(arrived), preferred_element_type=jnp.float32
        )
        returned = lax.all_to_all(
            bucket_major(product), "img", split_axis=0, concat_axis=0, tiled=True
        )
        spread = from_bucket(returned)
        current = 0.8 * inv[:, None] * spread + 0.2 * starting
    return current.astype(jnp.bfloat16)


def solution(mesh):
    return jax.shard_map(
        on_device,
        mesh=mesh,
        in_specs=(P("img", None), P("img", "sub"), P("img", None), P("img", None)),
        out_specs=P("img", "sub"),
        check_vma=False,
    )
```

```python
import functools

import jax
import jax.numpy as jnp
from jax import lax
from jax.experimental import pallas as pl
from jax.experimental.pallas import tpu as pltpu
from jax.sharding import PartitionSpec as P

SLOTS = 2048
BAND = 64
LIST_DEV = 1


def list_major(bucket):
    moved = jnp.moveaxis(bucket, 1, 0)
    return moved.reshape((moved.shape[0], moved.shape[1] * moved.shape[2]) + moved.shape[3:])


def affinity_kernel(col_keys, low_rows, high_rows, weights, row_sums, joined):
    block_rows = weights.shape[0]
    slot_count = weights.shape[1]
    half = joined.shape[1] - high_rows.shape[-1]

    @pl.when(pl.program_id(0) == 0)
    def _():
        low = low_rows[...]
        high = high_rows[...]
        joined[:, :half] = low.reshape(slot_count, low.shape[-1])[:, :half]
        joined[:, half:] = high.reshape(slot_count, high.shape[-1])

    start = pl.multiple_of(pl.program_id(0) * block_rows, block_rows)
    contract = (((1,), (1,)), ((), ()))
    gram = lax.dot_general(
        joined[pl.ds(start, block_rows), :], joined[...], contract,
        preferred_element_type=jnp.float32,
    )
    own_keys = col_keys[:, pl.ds(start, block_rows)]
    diagonal = (
        lax.broadcasted_iota(jnp.int32, (block_rows, block_rows), 0)
        == lax.broadcasted_iota(jnp.int32, (block_rows, block_rows), 1)
    )
    row_keys = jnp.sum(jnp.where(diagonal, own_keys, 0.0), axis=1, keepdims=True)
    keep = jnp.abs(row_keys - col_keys[...]) <= BAND
    positive = jnp.maximum(gram, 0.0)
    cubed = jnp.where(keep, positive * positive * positive, 0.0).astype(jnp.bfloat16)
    weights[...] = cubed
    ones = jnp.ones((8, slot_count), jnp.bfloat16)
    summed = lax.dot_general(ones, cubed, contract, preferred_element_type=jnp.float32)
    row_sums[...] = summed[0:1, :]


def fused_affinity(low, high, keys, part):
    sources, quarters = high.shape[0], high.shape[1]
    slot_count = sources * quarters * part
    half = low.shape[3]
    width = half + high.shape[3]
    if part % 16 == 0:
        low_spec = pl.BlockSpec((sources, quarters, part, half), lambda i: (0, 0, 0, 0))
        high_spec = pl.BlockSpec(high.shape, lambda i: (0, 0, 0, 0))
    else:
        low = low[:, :, :part, :].reshape(slot_count, half)
        high = high.reshape(slot_count, width - half)
        low_spec = pl.BlockSpec(low.shape, lambda i: (0, 0))
        high_spec = pl.BlockSpec(high.shape, lambda i: (0, 0))
    block_rows = min(512, slot_count)
    return pl.pallas_call(
        affinity_kernel,
        grid=(slot_count // block_rows,),
        in_specs=[pl.BlockSpec((1, slot_count), lambda i: (0, 0)), low_spec, high_spec],
        out_specs=[
            pl.BlockSpec((block_rows, slot_count), lambda i: (i, 0)),
            pl.BlockSpec((1, block_rows), lambda i: (0, i)),
        ],
        out_shape=[
            jax.ShapeDtypeStruct((slot_count, slot_count), jnp.bfloat16),
            jax.ShapeDtypeStruct((1, slot_count), jnp.float32),
        ],
        scratch_shapes=[pltpu.VMEM((slot_count, width), jnp.bfloat16)],
        compiler_params=pltpu.CompilerParams(dimension_semantics=("arbitrary",)),
        cost_estimate=pl.CostEstimate(
            flops=2 * slot_count * slot_count * width + 22 * slot_count * slot_count,
            transcendentals=0,
            bytes_accessed=slot_count * width * 2 + 2 * slot_count * slot_count,
        ),
    )(keys.reshape(1, slot_count), low, high)


def pieces_kernel(low_count, high_count, col_keys, *refs):
    low_refs = refs[:low_count]
    high_refs = refs[low_count:low_count + high_count]
    weights, row_sums, joined = refs[low_count + high_count:]
    block_rows = weights.shape[0]
    slot_count = weights.shape[1]
    quarters, part, width = joined.shape[1], joined.shape[2], joined.shape[3]
    half = low_refs[0].shape[-1]

    @pl.when(pl.program_id(0) == 0)
    def _():
        for group, lo, hi in ((low_refs, 0, half), (high_refs, half, width)):
            at = 0
            for ref in group:
                count = ref.shape[1]
                joined[:, at:at + count, :, lo:hi] = ref[...]
                at += count

    per_block = block_rows // (quarters * part)
    first = pl.multiple_of(pl.program_id(0) * per_block, per_block)
    start = pl.multiple_of(pl.program_id(0) * block_rows, block_rows)
    contract = (((1,), (1,)), ((), ()))
    gram = lax.dot_general(
        joined[pl.ds(first, per_block)].reshape(block_rows, width),
        joined[...].reshape(slot_count, width), contract,
        preferred_element_type=jnp.float32,
    )
    own_keys = col_keys[:, pl.ds(start, block_rows)]
    diagonal = (
        lax.broadcasted_iota(jnp.int32, (block_rows, block_rows), 0)
        == lax.broadcasted_iota(jnp.int32, (block_rows, block_rows), 1)
    )
    row_keys = jnp.sum(jnp.where(diagonal, own_keys, 0.0), axis=1, keepdims=True)
    keep = jnp.abs(row_keys - col_keys[...]) <= BAND
    positive = jnp.maximum(gram, 0.0)
    cubed = jnp.where(keep, positive * positive * positive, 0.0).astype(jnp.bfloat16)
    weights[...] = cubed
    ones = jnp.ones((8, slot_count), jnp.bfloat16)
    summed = lax.dot_general(ones, cubed, contract, preferred_element_type=jnp.float32)
    row_sums[...] = summed[0:1, :]


def pieces_affinity(low_pieces, high_pieces, keys, part):
    sources = low_pieces[0].shape[0]
    quarters = sum(piece.shape[1] for piece in low_pieces)
    half = low_pieces[0].shape[3]
    width = half + high_pieces[0].shape[3]
    if part % 16 != 0 or (2 * quarters * part) % 128 != 0:
        low = jnp.concatenate([piece[:, :, :part] for piece in low_pieces], axis=1)
        high = jnp.concatenate([piece[:, :, :part] for piece in high_pieces], axis=1)
        return fused_affinity(low, high, keys, part)
    slot_count = sources * quarters * part
    block_rows = min(512, slot_count)
    pieces = list(low_pieces) + list(high_pieces)
    specs = [
        pl.BlockSpec((sources, piece.shape[1], part, piece.shape[3]), lambda i: (0, 0, 0, 0))
        for piece in pieces
    ]
    return pl.pallas_call(
        functools.partial(pieces_kernel, len(low_pieces), len(high_pieces)),
        grid=(slot_count // block_rows,),
        in_specs=[pl.BlockSpec((1, slot_count), lambda i: (0, 0))] + specs,
        out_specs=[
            pl.BlockSpec((block_rows, slot_count), lambda i: (i, 0)),
            pl.BlockSpec((1, block_rows), lambda i: (0, i)),
        ],
        out_shape=[
            jax.ShapeDtypeStruct((slot_count, slot_count), jnp.bfloat16),
            jax.ShapeDtypeStruct((1, slot_count), jnp.float32),
        ],
        scratch_shapes=[pltpu.VMEM((sources, quarters, part, width), jnp.bfloat16)],
        compiler_params=pltpu.CompilerParams(dimension_semantics=("arbitrary",)),
        cost_estimate=pl.CostEstimate(
            flops=2 * slot_count * slot_count * width + 22 * slot_count * slot_count,
            transcendentals=0,
            bytes_accessed=slot_count * width * 2 + 2 * slot_count * slot_count,
        ),
    )(keys.reshape(1, slot_count), *pieces)


def on_device(embeddings, labels, image_lists, rank_keys):
    img_count = lax.axis_size("img")
    sub_count = lax.axis_size("sub")
    per_list = SLOTS // img_count
    part = per_list // sub_count
    rows_here = image_lists.shape[0]
    pair_count = rows_here * 2
    lists_flat = image_lists.reshape(-1)
    order = jnp.arange(pair_count, dtype=jnp.int32)
    same = (lists_flat[:, None] == lists_flat[None, :]) & (order[None, :] < order[:, None])
    within = jnp.sum(same.astype(jnp.int32), axis=1)
    slot_of_pair = (lists_flat * per_list + within).reshape(rows_here, 2)
    slot_total = LIST_DEV * img_count * per_list

    arrival = [0]
    bit = sub_count // 2
    while bit >= 1:
        arrival = arrival + [d ^ bit for d in arrival]
        bit //= 2
    me_sub = lax.axis_index("sub")
    quarters = jnp.bitwise_xor(me_sub, jnp.array(arrival, dtype=jnp.int32))
    slot_ids = (
        jnp.arange(img_count, dtype=jnp.int32)[:, None, None] * per_list
        + quarters[None, :, None] * part
        + jnp.arange(part, dtype=jnp.int32)[None, None, :]
    ).reshape(-1, 1)
    hit_a = slot_of_pair[None, :, 0] == slot_ids
    hit_b = slot_of_pair[None, :, 1] == slot_ids
    hit = hit_a | hit_b
    pick = hit.astype(jnp.bfloat16)

    def to_bucket(rows):
        picked = jnp.dot(pick, rows, preferred_element_type=jnp.float32).astype(rows.dtype)
        return picked.reshape(img_count, LIST_DEV, per_list, rows.shape[1])

    def bucket_major(listed):
        shaped = listed.reshape((listed.shape[0], img_count, per_list) + listed.shape[2:])
        return jnp.moveaxis(shaped, 0, 1)

    def from_bucket(returned):
        flat = returned.reshape(slot_total, -1)
        return jnp.einsum(
            "kg,kc->gc", pick.astype(jnp.float32), flat,
            precision=lax.Precision.HIGH, preferred_element_type=jnp.float32,
        )

    values = embeddings.astype(jnp.float32)
    unit = (values * lax.rsqrt(jnp.sum(values * values, axis=1, keepdims=True) + 1e-06)).astype(
        jnp.bfloat16
    )
    mine = (
        jnp.arange(img_count, dtype=jnp.int32)[:, None] * per_list
        + me_sub * part
        + jnp.arange(part, dtype=jnp.int32)[None, :]
    ).reshape(-1, 1)
    mine_a = slot_of_pair[None, :, 0] == mine
    mine_b = slot_of_pair[None, :, 1] == mine
    mine_hit = mine_a | mine_b
    keys_f = rank_keys.astype(jnp.float32)
    key_sum = jnp.sum(
        jnp.where(mine_a, keys_f[None, :, 0], 0.0) + jnp.where(mine_b, keys_f[None, :, 1], 0.0),
        axis=1,
    )
    mine_keys = jnp.where(jnp.any(mine_hit, axis=1), key_sum, -4096.0).astype(jnp.bfloat16)
    width = unit.shape[1]
    quarter = jnp.dot(mine_hit.astype(jnp.bfloat16), unit, preferred_element_type=jnp.float32)
    half = max(128, width // 3 // 128 * 128)
    quarter = quarter.astype(jnp.bfloat16).reshape(img_count, part, width)
    low_payload = jnp.concatenate(
        [
            quarter[:, :, :half],
            jnp.pad(mine_keys.reshape(img_count, 1, part), ((0, 0), (0, 0), (0, half - part))),
        ],
        axis=1,
    )
    high_payload = quarter[:, :, half:]

    def exchange_stage(got, bit):
        pairs = [(t, t ^ bit) for t in range(sub_count)]
        return jnp.concatenate([got, lax.ppermute(got, "sub", pairs)], axis=1)

    low_got = lax.all_to_all(low_payload, "img", split_axis=0, concat_axis=0, tiled=True)[:, None]
    high_got = lax.all_to_all(high_payload, "img", split_axis=0, concat_axis=0, tiled=True)[:, None]
    bit = sub_count // 2
    while bit > 1:
        low_got = exchange_stage(low_got, bit)
        high_got = exchange_stage(high_got, bit)
        bit //= 2
    last = [(t, t ^ bit) for t in range(sub_count)] if bit == 1 else None
    low_pieces = [low_got] + ([lax.ppermute(low_got, "sub", last)] if last else [])
    high_pieces = [high_got] + ([lax.ppermute(high_got, "sub", last)] if last else [])
    slot_count = slot_total
    key_rows = jnp.concatenate(
        [piece[:, :, part, :part] for piece in low_pieces], axis=1
    ).reshape(slot_count).astype(jnp.float32)
    weight_mat, row_sums = pieces_affinity(low_pieces, high_pieces, key_rows, part)
    weights = weight_mat.reshape(1, slot_count, slot_count)
    degree_slots = lax.all_to_all(
        bucket_major(row_sums), "img", split_axis=0, concat_axis=0, tiled=True
    )
    degree = jnp.sum(jnp.where(hit, degree_slots.reshape(slot_total, 1), 0.0), axis=0)
    inv = lax.rsqrt(degree)
    starting = labels.astype(jnp.float32)
    current = starting
    for step in range(2):
        scaled = (inv[:, None] * current).astype(jnp.bfloat16)
        arrived = lax.all_to_all(to_bucket(scaled), "img", split_axis=0, concat_axis=0, tiled=True)
        product = jnp.einsum(
            "ajk,akc->ajc", weights, list_major(arrived), preferred_element_type=jnp.float32
        )
        returned = lax.all_to_all(
            bucket_major(product), "img", split_axis=0, concat_axis=0, tiled=True
        )
        spread = from_bucket(returned)
        current = 0.8 * inv[:, None] * spread + 0.2 * starting
    return current.astype(jnp.bfloat16)


def solution(mesh):
    return jax.shard_map(
        on_device,
        mesh=mesh,
        in_specs=(P("img", None), P("img", "sub"), P("img", None), P("img", None)),
        out_specs=P("img", "sub"),
        check_vma=False,
    )
```

```python
import functools

import jax
import jax.numpy as jnp
from jax import lax
from jax.experimental import pallas as pl
from jax.experimental.pallas import tpu as pltpu
from jax.sharding import PartitionSpec as P

SLOTS = 2048
BAND = 64
LIST_DEV = 1


def list_major(bucket):
    moved = jnp.moveaxis(bucket, 1, 0)
    return moved.reshape((moved.shape[0], moved.shape[1] * moved.shape[2]) + moved.shape[3:])


def affinity_kernel(col_keys, low_rows, high_rows, weights, row_sums, joined):
    block_rows = weights.shape[0]
    slot_count = weights.shape[1]
    half = joined.shape[1] - high_rows.shape[-1]

    @pl.when(pl.program_id(0) == 0)
    def _():
        low = low_rows[...]
        high = high_rows[...]
        joined[:, :half] = low.reshape(slot_count, low.shape[-1])[:, :half]
        joined[:, half:] = high.reshape(slot_count, high.shape[-1])

    start = pl.multiple_of(pl.program_id(0) * block_rows, block_rows)
    contract = (((1,), (1,)), ((), ()))
    gram = lax.dot_general(
        joined[pl.ds(start, block_rows), :], joined[...], contract,
        preferred_element_type=jnp.float32,
    )
    own_keys = col_keys[:, pl.ds(start, block_rows)]
    diagonal = (
        lax.broadcasted_iota(jnp.int32, (block_rows, block_rows), 0)
        == lax.broadcasted_iota(jnp.int32, (block_rows, block_rows), 1)
    )
    row_keys = jnp.sum(jnp.where(diagonal, own_keys, 0.0), axis=1, keepdims=True)
    keep = jnp.abs(row_keys - col_keys[...]) <= BAND
    positive = jnp.maximum(gram, 0.0)
    cubed = jnp.where(keep, positive * positive * positive, 0.0).astype(jnp.bfloat16)
    weights[...] = cubed
    ones = jnp.ones((8, slot_count), jnp.bfloat16)
    summed = lax.dot_general(ones, cubed, contract, preferred_element_type=jnp.float32)
    row_sums[...] = summed[0:1, :]


def fused_affinity(low, high, keys, part):
    sources, quarters = high.shape[0], high.shape[1]
    slot_count = sources * quarters * part
    half = low.shape[3]
    width = half + high.shape[3]
    if part % 16 == 0:
        low_spec = pl.BlockSpec((sources, quarters, part, half), lambda i: (0, 0, 0, 0))
        high_spec = pl.BlockSpec(high.shape, lambda i: (0, 0, 0, 0))
    else:
        low = low[:, :, :part, :].reshape(slot_count, half)
        high = high.reshape(slot_count, width - half)
        low_spec = pl.BlockSpec(low.shape, lambda i: (0, 0))
        high_spec = pl.BlockSpec(high.shape, lambda i: (0, 0))
    block_rows = min(512, slot_count)
    return pl.pallas_call(
        affinity_kernel,
        grid=(slot_count // block_rows,),
        in_specs=[pl.BlockSpec((1, slot_count), lambda i: (0, 0)), low_spec, high_spec],
        out_specs=[
            pl.BlockSpec((block_rows, slot_count), lambda i: (i, 0)),
            pl.BlockSpec((1, block_rows), lambda i: (0, i)),
        ],
        out_shape=[
            jax.ShapeDtypeStruct((slot_count, slot_count), jnp.bfloat16),
            jax.ShapeDtypeStruct((1, slot_count), jnp.float32),
        ],
        scratch_shapes=[pltpu.VMEM((slot_count, width), jnp.bfloat16)],
        compiler_params=pltpu.CompilerParams(dimension_semantics=("arbitrary",)),
        cost_estimate=pl.CostEstimate(
            flops=2 * slot_count * slot_count * width + 22 * slot_count * slot_count,
            transcendentals=0,
            bytes_accessed=slot_count * width * 2 + 2 * slot_count * slot_count,
        ),
    )(keys.reshape(1, slot_count), low, high)


def pieces_kernel(low_count, high_count, col_keys, *refs):
    low_refs = refs[:low_count]
    high_refs = refs[low_count:low_count + high_count]
    weights, row_sums, joined = refs[low_count + high_count:]
    block_rows = weights.shape[0]
    slot_count = weights.shape[1]
    quarters, part, width = joined.shape[1], joined.shape[2], joined.shape[3]
    half = low_refs[0].shape[-1]

    @pl.when(pl.program_id(0) == 0)
    def _():
        for group, lo, hi in ((low_refs, 0, half), (high_refs, half, width)):
            at = 0
            for ref in group:
                for m in range(ref.shape[0]):
                    joined[:, at, :, lo:hi] = ref[m]
                    at += 1

    per_block = block_rows // (quarters * part)
    first = pl.multiple_of(pl.program_id(0) * per_block, per_block)
    start = pl.multiple_of(pl.program_id(0) * block_rows, block_rows)
    contract = (((1,), (1,)), ((), ()))
    gram = lax.dot_general(
        joined[pl.ds(first, per_block)].reshape(block_rows, width),
        joined[...].reshape(slot_count, width), contract,
        preferred_element_type=jnp.float32,
    )
    own_keys = col_keys[:, pl.ds(start, block_rows)]
    diagonal = (
        lax.broadcasted_iota(jnp.int32, (block_rows, block_rows), 0)
        == lax.broadcasted_iota(jnp.int32, (block_rows, block_rows), 1)
    )
    row_keys = jnp.sum(jnp.where(diagonal, own_keys, 0.0), axis=1, keepdims=True)
    keep = jnp.abs(row_keys - col_keys[...]) <= BAND
    positive = jnp.maximum(gram, 0.0)
    cubed = jnp.where(keep, positive * positive * positive, 0.0).astype(jnp.bfloat16)
    weights[...] = cubed
    ones = jnp.ones((8, slot_count), jnp.bfloat16)
    summed = lax.dot_general(ones, cubed, contract, preferred_element_type=jnp.float32)
    row_sums[...] = summed[0:1, :]


def pieces_affinity(low_pieces, high_pieces, keys, part):
    sources = low_pieces[0].shape[1]
    quarters = sum(piece.shape[0] for piece in low_pieces)
    half = low_pieces[0].shape[3]
    width = half + high_pieces[0].shape[3]
    if part % 16 != 0 or (2 * quarters * part) % 128 != 0:
        def source_major(group):
            stacked = jnp.concatenate([piece[:, :, :part] for piece in group], axis=0)
            return jnp.moveaxis(stacked, 0, 1)
        return fused_affinity(source_major(low_pieces), source_major(high_pieces), keys, part)
    slot_count = sources * quarters * part
    block_rows = min(512, slot_count)
    pieces = list(low_pieces) + list(high_pieces)
    specs = [
        pl.BlockSpec((piece.shape[0], sources, part, piece.shape[3]), lambda i: (0, 0, 0, 0))
        for piece in pieces
    ]
    return pl.pallas_call(
        functools.partial(pieces_kernel, len(low_pieces), len(high_pieces)),
        grid=(slot_count // block_rows,),
        in_specs=[pl.BlockSpec((1, slot_count), lambda i: (0, 0))] + specs,
        out_specs=[
            pl.BlockSpec((block_rows, slot_count), lambda i: (i, 0)),
            pl.BlockSpec((1, block_rows), lambda i: (0, i)),
        ],
        out_shape=[
            jax.ShapeDtypeStruct((slot_count, slot_count), jnp.bfloat16),
            jax.ShapeDtypeStruct((1, slot_count), jnp.float32),
        ],
        scratch_shapes=[pltpu.VMEM((sources, quarters, part, width), jnp.bfloat16)],
        compiler_params=pltpu.CompilerParams(dimension_semantics=("arbitrary",)),
        cost_estimate=pl.CostEstimate(
            flops=2 * slot_count * slot_count * width + 22 * slot_count * slot_count,
            transcendentals=0,
            bytes_accessed=slot_count * width * 2 + 2 * slot_count * slot_count,
        ),
    )(keys.reshape(1, slot_count), *pieces)


def on_device(embeddings, labels, image_lists, rank_keys):
    img_count = lax.axis_size("img")
    sub_count = lax.axis_size("sub")
    per_list = SLOTS // img_count
    part = per_list // sub_count
    rows_here = image_lists.shape[0]
    pair_count = rows_here * 2
    lists_flat = image_lists.reshape(-1)
    order = jnp.arange(pair_count, dtype=jnp.int32)
    same = (lists_flat[:, None] == lists_flat[None, :]) & (order[None, :] < order[:, None])
    within = jnp.sum(same.astype(jnp.int32), axis=1)
    slot_of_pair = (lists_flat * per_list + within).reshape(rows_here, 2)
    slot_total = LIST_DEV * img_count * per_list

    arrival = [0]
    bit = sub_count // 2
    while bit >= 1:
        arrival = arrival + [d ^ bit for d in arrival]
        bit //= 2
    me_sub = lax.axis_index("sub")
    quarters = jnp.bitwise_xor(me_sub, jnp.array(arrival, dtype=jnp.int32))
    slot_ids = (
        jnp.arange(img_count, dtype=jnp.int32)[:, None, None] * per_list
        + quarters[None, :, None] * part
        + jnp.arange(part, dtype=jnp.int32)[None, None, :]
    ).reshape(-1, 1)
    hit_a = slot_of_pair[None, :, 0] == slot_ids
    hit_b = slot_of_pair[None, :, 1] == slot_ids
    hit = hit_a | hit_b
    pick = hit.astype(jnp.bfloat16)

    def to_bucket(rows):
        picked = jnp.dot(pick, rows, preferred_element_type=jnp.float32).astype(rows.dtype)
        return picked.reshape(img_count, LIST_DEV, per_list, rows.shape[1])

    def bucket_major(listed):
        shaped = listed.reshape((listed.shape[0], img_count, per_list) + listed.shape[2:])
        return jnp.moveaxis(shaped, 0, 1)

    def from_bucket(returned):
        flat = returned.reshape(slot_total, -1)
        return jnp.einsum(
            "kg,kc->gc", pick.astype(jnp.float32), flat,
            precision=lax.Precision.HIGH, preferred_element_type=jnp.float32,
        )

    values = embeddings.astype(jnp.float32)
    unit = (values * lax.rsqrt(jnp.sum(values * values, axis=1, keepdims=True) + 1e-06)).astype(
        jnp.bfloat16
    )
    mine = (
        jnp.arange(img_count, dtype=jnp.int32)[:, None] * per_list
        + me_sub * part
        + jnp.arange(part, dtype=jnp.int32)[None, :]
    ).reshape(-1, 1)
    mine_a = slot_of_pair[None, :, 0] == mine
    mine_b = slot_of_pair[None, :, 1] == mine
    mine_hit = mine_a | mine_b
    keys_f = rank_keys.astype(jnp.float32)
    key_sum = jnp.sum(
        jnp.where(mine_a, keys_f[None, :, 0], 0.0) + jnp.where(mine_b, keys_f[None, :, 1], 0.0),
        axis=1,
    )
    mine_keys = jnp.where(jnp.any(mine_hit, axis=1), key_sum, -4096.0).astype(jnp.bfloat16)
    width = unit.shape[1]
    quarter = jnp.dot(mine_hit.astype(jnp.bfloat16), unit, preferred_element_type=jnp.float32)
    half = max(128, width // 3 // 128 * 128)
    quarter = quarter.astype(jnp.bfloat16).reshape(img_count, part, width)
    low_payload = jnp.concatenate(
        [
            quarter[:, :, :half],
            jnp.pad(mine_keys.reshape(img_count, 1, part), ((0, 0), (0, 0), (0, half - part))),
        ],
        axis=1,
    )
    high_payload = quarter[:, :, half:]

    def exchange_stage(got, bit):
        pairs = [(t, t ^ bit) for t in range(sub_count)]
        return jnp.concatenate([got, lax.ppermute(got, "sub", pairs)], axis=0)

    low_got = lax.all_to_all(low_payload, "img", split_axis=0, concat_axis=0, tiled=True)[None]
    high_got = lax.all_to_all(high_payload, "img", split_axis=0, concat_axis=0, tiled=True)[None]
    bit = sub_count // 2
    while bit > 1:
        low_got = exchange_stage(low_got, bit)
        high_got = exchange_stage(high_got, bit)
        bit //= 2
    last = [(t, t ^ bit) for t in range(sub_count)] if bit == 1 else None
    low_pieces = [low_got] + ([lax.ppermute(low_got, "sub", last)] if last else [])
    high_pieces = [high_got] + ([lax.ppermute(high_got, "sub", last)] if last else [])
    slot_count = slot_total
    key_rows = jnp.moveaxis(
        jnp.concatenate([piece[:, :, part, :part] for piece in low_pieces], axis=0), 0, 1
    ).reshape(slot_count).astype(jnp.float32)
    weight_mat, row_sums = pieces_affinity(low_pieces, high_pieces, key_rows, part)
    weights = weight_mat.reshape(1, slot_count, slot_count)
    degree_slots = lax.all_to_all(
        bucket_major(row_sums), "img", split_axis=0, concat_axis=0, tiled=True
    )
    degree = jnp.sum(jnp.where(hit, degree_slots.reshape(slot_total, 1), 0.0), axis=0)
    inv = lax.rsqrt(degree)
    starting = labels.astype(jnp.float32)
    current = starting
    for step in range(2):
        scaled = (inv[:, None] * current).astype(jnp.bfloat16)
        arrived = lax.all_to_all(to_bucket(scaled), "img", split_axis=0, concat_axis=0, tiled=True)
        product = jnp.einsum(
            "ajk,akc->ajc", weights, list_major(arrived), preferred_element_type=jnp.float32
        )
        returned = lax.all_to_all(
            bucket_major(product), "img", split_axis=0, concat_axis=0, tiled=True
        )
        spread = from_bucket(returned)
        current = 0.8 * inv[:, None] * spread + 0.2 * starting
    return current.astype(jnp.bfloat16)


def solution(mesh):
    return jax.shard_map(
        on_device,
        mesh=mesh,
        in_specs=(P("img", None), P("img", "sub"), P("img", None), P("img", None)),
        out_specs=P("img", "sub"),
        check_vma=False,
    )
```

```python
import functools

import jax
import jax.numpy as jnp
from jax import lax
from jax.experimental import pallas as pl
from jax.experimental.pallas import tpu as pltpu
from jax.sharding import PartitionSpec as P

SLOTS = 2048
BAND = 64
LIST_DEV = 1


def list_major(bucket):
    moved = jnp.moveaxis(bucket, 1, 0)
    return moved.reshape((moved.shape[0], moved.shape[1] * moved.shape[2]) + moved.shape[3:])


def affinity_kernel(col_keys, low_rows, high_rows, weights, row_sums, joined):
    block_rows = weights.shape[0]
    slot_count = weights.shape[1]
    half = joined.shape[1] - high_rows.shape[-1]

    @pl.when(pl.program_id(0) == 0)
    def _():
        low = low_rows[...]
        high = high_rows[...]
        joined[:, :half] = low.reshape(slot_count, low.shape[-1])[:, :half]
        joined[:, half:] = high.reshape(slot_count, high.shape[-1])

    start = pl.multiple_of(pl.program_id(0) * block_rows, block_rows)
    contract = (((1,), (1,)), ((), ()))
    gram = lax.dot_general(
        joined[pl.ds(start, block_rows), :], joined[...], contract,
        preferred_element_type=jnp.float32,
    )
    own_keys = col_keys[:, pl.ds(start, block_rows)]
    diagonal = (
        lax.broadcasted_iota(jnp.int32, (block_rows, block_rows), 0)
        == lax.broadcasted_iota(jnp.int32, (block_rows, block_rows), 1)
    )
    row_keys = jnp.sum(jnp.where(diagonal, own_keys, 0.0), axis=1, keepdims=True)
    keep = jnp.abs(row_keys - col_keys[...]) <= BAND
    positive = jnp.maximum(gram, 0.0)
    cubed = jnp.where(keep, positive * positive * positive, 0.0).astype(jnp.bfloat16)
    weights[...] = cubed
    ones = jnp.ones((8, slot_count), jnp.bfloat16)
    summed = lax.dot_general(ones, cubed, contract, preferred_element_type=jnp.float32)
    row_sums[...] = summed[0:1, :]


def fused_affinity(low, high, keys, part):
    sources, quarters = high.shape[0], high.shape[1]
    slot_count = sources * quarters * part
    half = low.shape[3]
    width = half + high.shape[3]
    if part % 16 == 0:
        low_spec = pl.BlockSpec((sources, quarters, part, half), lambda i: (0, 0, 0, 0))
        high_spec = pl.BlockSpec(high.shape, lambda i: (0, 0, 0, 0))
    else:
        low = low[:, :, :part, :].reshape(slot_count, half)
        high = high.reshape(slot_count, width - half)
        low_spec = pl.BlockSpec(low.shape, lambda i: (0, 0))
        high_spec = pl.BlockSpec(high.shape, lambda i: (0, 0))
    block_rows = min(512, slot_count)
    return pl.pallas_call(
        affinity_kernel,
        grid=(slot_count // block_rows,),
        in_specs=[pl.BlockSpec((1, slot_count), lambda i: (0, 0)), low_spec, high_spec],
        out_specs=[
            pl.BlockSpec((block_rows, slot_count), lambda i: (i, 0)),
            pl.BlockSpec((1, block_rows), lambda i: (0, i)),
        ],
        out_shape=[
            jax.ShapeDtypeStruct((slot_count, slot_count), jnp.bfloat16),
            jax.ShapeDtypeStruct((1, slot_count), jnp.float32),
        ],
        scratch_shapes=[pltpu.VMEM((slot_count, width), jnp.bfloat16)],
        compiler_params=pltpu.CompilerParams(dimension_semantics=("arbitrary",)),
        cost_estimate=pl.CostEstimate(
            flops=2 * slot_count * slot_count * width + 22 * slot_count * slot_count,
            transcendentals=0,
            bytes_accessed=slot_count * width * 2 + 2 * slot_count * slot_count,
        ),
    )(keys.reshape(1, slot_count), low, high)


def pieces_kernel(low_count, high_count, col_keys, *refs):
    low_refs = refs[:low_count]
    high_refs = refs[low_count:low_count + high_count]
    weights, row_sums, joined = refs[low_count + high_count:]
    block_rows = weights.shape[0]
    slot_count = weights.shape[1]
    quarters, part, width = joined.shape[1], joined.shape[2], joined.shape[3]
    half = low_refs[0].shape[-1]

    @pl.when(pl.program_id(0) == 0)
    def _():
        for group, lo, hi in ((low_refs, 0, half), (high_refs, half, width)):
            at = 0
            for ref in group:
                for m in range(ref.shape[0]):
                    joined[:, at, :, lo:hi] = ref[m]
                    at += 1

    per_block = block_rows // (quarters * part)
    first = pl.multiple_of(pl.program_id(0) * per_block, per_block)
    start = pl.multiple_of(pl.program_id(0) * block_rows, block_rows)
    contract = (((1,), (1,)), ((), ()))
    gram = lax.dot_general(
        joined[pl.ds(first, per_block)].reshape(block_rows, width),
        joined[...].reshape(slot_count, width), contract,
        preferred_element_type=jnp.float32,
    )
    own_keys = col_keys[:, pl.ds(start, block_rows)]
    diagonal = (
        lax.broadcasted_iota(jnp.int32, (block_rows, block_rows), 0)
        == lax.broadcasted_iota(jnp.int32, (block_rows, block_rows), 1)
    )
    row_keys = jnp.sum(jnp.where(diagonal, own_keys, 0.0), axis=1, keepdims=True)
    keep = jnp.abs(row_keys - col_keys[...]) <= BAND
    positive = jnp.maximum(gram, 0.0)
    cubed = jnp.where(keep, positive * positive * positive, 0.0).astype(jnp.bfloat16)
    weights[...] = cubed
    ones = jnp.ones((8, slot_count), jnp.bfloat16)
    summed = lax.dot_general(ones, cubed, contract, preferred_element_type=jnp.float32)
    row_sums[...] = summed[0:1, :]


def pieces_affinity(low_pieces, high_pieces, keys, part):
    sources = low_pieces[0].shape[1]
    quarters = sum(piece.shape[0] for piece in low_pieces)
    half = low_pieces[0].shape[3]
    width = half + high_pieces[0].shape[3]
    if part % 16 != 0 or (2 * quarters * part) % 128 != 0:
        def source_major(group):
            stacked = jnp.concatenate([piece[:, :, :part] for piece in group], axis=0)
            return jnp.moveaxis(stacked, 0, 1)
        return fused_affinity(source_major(low_pieces), source_major(high_pieces), keys, part)
    slot_count = sources * quarters * part
    block_rows = min(512, slot_count)
    pieces = list(low_pieces) + list(high_pieces)
    specs = [
        pl.BlockSpec((piece.shape[0], sources, part, piece.shape[3]), lambda i: (0, 0, 0, 0))
        for piece in pieces
    ]
    return pl.pallas_call(
        functools.partial(pieces_kernel, len(low_pieces), len(high_pieces)),
        grid=(slot_count // block_rows,),
        in_specs=[pl.BlockSpec((1, slot_count), lambda i: (0, 0))] + specs,
        out_specs=[
            pl.BlockSpec((block_rows, slot_count), lambda i: (i, 0)),
            pl.BlockSpec((1, block_rows), lambda i: (0, i)),
        ],
        out_shape=[
            jax.ShapeDtypeStruct((slot_count, slot_count), jnp.bfloat16),
            jax.ShapeDtypeStruct((1, slot_count), jnp.float32),
        ],
        scratch_shapes=[pltpu.VMEM((sources, quarters, part, width), jnp.bfloat16)],
        compiler_params=pltpu.CompilerParams(dimension_semantics=("arbitrary",)),
        cost_estimate=pl.CostEstimate(
            flops=2 * slot_count * slot_count * width + 22 * slot_count * slot_count,
            transcendentals=0,
            bytes_accessed=slot_count * width * 2 + 2 * slot_count * slot_count,
        ),
    )(keys.reshape(1, slot_count), *pieces)


def on_device(embeddings, labels, image_lists, rank_keys):
    img_count = lax.axis_size("img")
    sub_count = lax.axis_size("sub")
    per_list = SLOTS // img_count
    part = per_list // sub_count
    rows_here = image_lists.shape[0]
    pair_count = rows_here * 2
    lists_flat = image_lists.reshape(-1)
    order = jnp.arange(pair_count, dtype=jnp.int32)
    same = (lists_flat[:, None] == lists_flat[None, :]) & (order[None, :] < order[:, None])
    within = jnp.sum(same.astype(jnp.int32), axis=1)
    slot_of_pair = (lists_flat * per_list + within).reshape(rows_here, 2)
    slot_total = LIST_DEV * img_count * per_list

    arrival = [0]
    bit = sub_count // 2
    while bit >= 1:
        arrival = arrival + [d ^ bit for d in arrival]
        bit //= 2
    me_sub = lax.axis_index("sub")
    quarters = jnp.bitwise_xor(me_sub, jnp.array(arrival, dtype=jnp.int32))
    slot_ids = (
        jnp.arange(img_count, dtype=jnp.int32)[:, None, None] * per_list
        + quarters[None, :, None] * part
        + jnp.arange(part, dtype=jnp.int32)[None, None, :]
    ).reshape(-1, 1)
    hit_a = slot_of_pair[None, :, 0] == slot_ids
    hit_b = slot_of_pair[None, :, 1] == slot_ids
    hit = hit_a | hit_b
    pick = hit.astype(jnp.bfloat16)

    def to_bucket(rows):
        picked = jnp.dot(pick, rows, preferred_element_type=jnp.float32).astype(rows.dtype)
        return picked.reshape(img_count, LIST_DEV, per_list, rows.shape[1])

    def bucket_major(listed):
        shaped = listed.reshape((listed.shape[0], img_count, per_list) + listed.shape[2:])
        return jnp.moveaxis(shaped, 0, 1)

    def from_bucket(returned):
        flat = returned.reshape(slot_total, -1)
        return jnp.einsum(
            "kg,kc->gc", pick.astype(jnp.float32), flat,
            precision=lax.Precision.HIGH, preferred_element_type=jnp.float32,
        )

    values = embeddings.astype(jnp.float32)
    unit = (values * lax.rsqrt(jnp.sum(values * values, axis=1, keepdims=True) + 1e-06)).astype(
        jnp.bfloat16
    )
    mine = (
        jnp.arange(img_count, dtype=jnp.int32)[:, None] * per_list
        + me_sub * part
        + jnp.arange(part, dtype=jnp.int32)[None, :]
    ).reshape(-1, 1)
    mine_a = slot_of_pair[None, :, 0] == mine
    mine_b = slot_of_pair[None, :, 1] == mine
    mine_hit = mine_a | mine_b
    keys_f = rank_keys.astype(jnp.float32)
    key_sum = jnp.sum(
        jnp.where(mine_a, keys_f[None, :, 0], 0.0) + jnp.where(mine_b, keys_f[None, :, 1], 0.0),
        axis=1,
    )
    mine_keys = jnp.where(jnp.any(mine_hit, axis=1), key_sum, -4096.0).astype(jnp.bfloat16)
    width = unit.shape[1]
    half = max(128, width // 3 // 128 * 128)
    mine_pick = mine_hit.astype(jnp.bfloat16)

    def quarter_rows(columns):
        picked = jnp.dot(mine_pick, columns, preferred_element_type=jnp.float32)
        return picked.astype(jnp.bfloat16).reshape(img_count, part, columns.shape[1])

    low_payload = jnp.concatenate(
        [
            quarter_rows(unit[:, :half]),
            jnp.pad(mine_keys.reshape(img_count, 1, part), ((0, 0), (0, 0), (0, half - part))),
        ],
        axis=1,
    )
    high_payload = quarter_rows(unit[:, half:])

    def exchange_stage(got, bit):
        pairs = [(t, t ^ bit) for t in range(sub_count)]
        return jnp.concatenate([got, lax.ppermute(got, "sub", pairs)], axis=0)

    low_got = lax.all_to_all(low_payload, "img", split_axis=0, concat_axis=0, tiled=True)[None]
    high_got = lax.all_to_all(high_payload, "img", split_axis=0, concat_axis=0, tiled=True)[None]
    bit = sub_count // 2
    while bit > 1:
        low_got = exchange_stage(low_got, bit)
        high_got = exchange_stage(high_got, bit)
        bit //= 2
    last = [(t, t ^ bit) for t in range(sub_count)] if bit == 1 else None
    low_pieces = [low_got] + ([lax.ppermute(low_got, "sub", last)] if last else [])
    high_pieces = [high_got] + ([lax.ppermute(high_got, "sub", last)] if last else [])
    slot_count = slot_total
    key_rows = jnp.moveaxis(
        jnp.concatenate([piece[:, :, part, :part] for piece in low_pieces], axis=0), 0, 1
    ).reshape(slot_count).astype(jnp.float32)
    weight_mat, row_sums = pieces_affinity(low_pieces, high_pieces, key_rows, part)
    weights = weight_mat.reshape(1, slot_count, slot_count)
    degree_slots = lax.all_to_all(
        bucket_major(row_sums), "img", split_axis=0, concat_axis=0, tiled=True
    )
    degree = jnp.sum(jnp.where(hit, degree_slots.reshape(slot_total, 1), 0.0), axis=0)
    inv = lax.rsqrt(degree)
    starting = labels.astype(jnp.float32)
    current = starting
    for step in range(2):
        scaled = (inv[:, None] * current).astype(jnp.bfloat16)
        arrived = lax.all_to_all(to_bucket(scaled), "img", split_axis=0, concat_axis=0, tiled=True)
        product = jnp.einsum(
            "ajk,akc->ajc", weights, list_major(arrived), preferred_element_type=jnp.float32
        )
        returned = lax.all_to_all(
            bucket_major(product), "img", split_axis=0, concat_axis=0, tiled=True
        )
        spread = from_bucket(returned)
        current = 0.8 * inv[:, None] * spread + 0.2 * starting
    return current.astype(jnp.bfloat16)


def solution(mesh):
    return jax.shard_map(
        on_device,
        mesh=mesh,
        in_specs=(P("img", None), P("img", "sub"), P("img", None), P("img", None)),
        out_specs=P("img", "sub"),
        check_vma=False,
    )
```

```python
import functools

import jax
import jax.numpy as jnp
from jax import lax
from jax.experimental import pallas as pl
from jax.experimental.pallas import tpu as pltpu
from jax.sharding import PartitionSpec as P

SLOTS = 2048
BAND = 64
LIST_DEV = 1


def list_major(bucket):
    moved = jnp.moveaxis(bucket, 1, 0)
    return moved.reshape((moved.shape[0], moved.shape[1] * moved.shape[2]) + moved.shape[3:])


def affinity_kernel(col_keys, low_rows, high_rows, weights, row_sums, joined):
    block_rows = weights.shape[0]
    slot_count = weights.shape[1]
    half = joined.shape[1] - high_rows.shape[-1]

    @pl.when(pl.program_id(0) == 0)
    def _():
        low = low_rows[...]
        high = high_rows[...]
        joined[:, :half] = low.reshape(slot_count, low.shape[-1])[:, :half]
        joined[:, half:] = high.reshape(slot_count, high.shape[-1])

    start = pl.multiple_of(pl.program_id(0) * block_rows, block_rows)
    contract = (((1,), (1,)), ((), ()))
    gram = lax.dot_general(
        joined[pl.ds(start, block_rows), :], joined[...], contract,
        preferred_element_type=jnp.float32,
    )
    own_keys = col_keys[:, pl.ds(start, block_rows)]
    diagonal = (
        lax.broadcasted_iota(jnp.int32, (block_rows, block_rows), 0)
        == lax.broadcasted_iota(jnp.int32, (block_rows, block_rows), 1)
    )
    row_keys = jnp.sum(jnp.where(diagonal, own_keys, 0.0), axis=1, keepdims=True)
    keep = jnp.abs(row_keys - col_keys[...]) <= BAND
    positive = jnp.maximum(gram, 0.0)
    cubed = jnp.where(keep, positive * positive * positive, 0.0).astype(jnp.bfloat16)
    weights[...] = cubed
    ones = jnp.ones((8, slot_count), jnp.bfloat16)
    summed = lax.dot_general(ones, cubed, contract, preferred_element_type=jnp.float32)
    row_sums[...] = summed[0:1, :]


def fused_affinity(low, high, keys, part):
    sources, quarters = high.shape[0], high.shape[1]
    slot_count = sources * quarters * part
    half = low.shape[3]
    width = half + high.shape[3]
    if part % 16 == 0:
        low_spec = pl.BlockSpec((sources, quarters, part, half), lambda i: (0, 0, 0, 0))
        high_spec = pl.BlockSpec(high.shape, lambda i: (0, 0, 0, 0))
    else:
        low = low[:, :, :part, :].reshape(slot_count, half)
        high = high.reshape(slot_count, width - half)
        low_spec = pl.BlockSpec(low.shape, lambda i: (0, 0))
        high_spec = pl.BlockSpec(high.shape, lambda i: (0, 0))
    block_rows = min(512, slot_count)
    return pl.pallas_call(
        affinity_kernel,
        grid=(slot_count // block_rows,),
        in_specs=[pl.BlockSpec((1, slot_count), lambda i: (0, 0)), low_spec, high_spec],
        out_specs=[
            pl.BlockSpec((block_rows, slot_count), lambda i: (i, 0)),
            pl.BlockSpec((1, block_rows), lambda i: (0, i)),
        ],
        out_shape=[
            jax.ShapeDtypeStruct((slot_count, slot_count), jnp.bfloat16),
            jax.ShapeDtypeStruct((1, slot_count), jnp.float32),
        ],
        scratch_shapes=[pltpu.VMEM((slot_count, width), jnp.bfloat16)],
        compiler_params=pltpu.CompilerParams(dimension_semantics=("arbitrary",)),
        cost_estimate=pl.CostEstimate(
            flops=2 * slot_count * slot_count * width + 22 * slot_count * slot_count,
            transcendentals=0,
            bytes_accessed=slot_count * width * 2 + 2 * slot_count * slot_count,
        ),
    )(keys.reshape(1, slot_count), low, high)


def pieces_kernel(low_count, high_count, *refs):
    low_refs = refs[:low_count]
    high_refs = refs[low_count:low_count + high_count]
    weights, row_sums, joined, col_keys = refs[low_count + high_count:]
    block_rows = weights.shape[0]
    slot_count = weights.shape[1]
    quarters, part, width = joined.shape[1], joined.shape[2], joined.shape[3]
    half = low_refs[0].shape[-1]

    @pl.when(pl.program_id(0) == 0)
    def _():
        for group, lo, hi in ((low_refs, 0, half), (high_refs, half, width)):
            at = 0
            for ref in group:
                for m in range(ref.shape[0]):
                    joined[:, at, :, lo:hi] = ref[m, :, :part, :]
                    at += 1
        key_parts = [ref[m, :, part, :part] for ref in low_refs for m in range(ref.shape[0])]
        key_grid = jnp.concatenate(key_parts, axis=1).astype(jnp.float32)
        col_keys[...] = key_grid.reshape(1, slot_count)

    per_block = block_rows // (quarters * part)
    first = pl.multiple_of(pl.program_id(0) * per_block, per_block)
    start = pl.multiple_of(pl.program_id(0) * block_rows, block_rows)
    contract = (((1,), (1,)), ((), ()))
    gram = lax.dot_general(
        joined[pl.ds(first, per_block)].reshape(block_rows, width),
        joined[...].reshape(slot_count, width), contract,
        preferred_element_type=jnp.float32,
    )
    own_keys = col_keys[:, pl.ds(start, block_rows)]
    diagonal = (
        lax.broadcasted_iota(jnp.int32, (block_rows, block_rows), 0)
        == lax.broadcasted_iota(jnp.int32, (block_rows, block_rows), 1)
    )
    row_keys = jnp.sum(jnp.where(diagonal, own_keys, 0.0), axis=1, keepdims=True)
    keep = jnp.abs(row_keys - col_keys[...]) <= BAND
    positive = jnp.maximum(gram, 0.0)
    cubed = jnp.where(keep, positive * positive * positive, 0.0).astype(jnp.bfloat16)
    weights[...] = cubed
    ones = jnp.ones((8, slot_count), jnp.bfloat16)
    summed = lax.dot_general(ones, cubed, contract, preferred_element_type=jnp.float32)
    row_sums[...] = summed[0:1, :]


def pieces_affinity(low_pieces, high_pieces, keys, part):
    sources = low_pieces[0].shape[1]
    quarters = sum(piece.shape[0] for piece in low_pieces)
    half = low_pieces[0].shape[3]
    width = half + high_pieces[0].shape[3]
    if part % 16 != 0 or (2 * quarters * part) % 128 != 0:
        def source_major(group):
            stacked = jnp.concatenate([piece[:, :, :part] for piece in group], axis=0)
            return jnp.moveaxis(stacked, 0, 1)
        return fused_affinity(source_major(low_pieces), source_major(high_pieces), keys, part)
    slot_count = sources * quarters * part
    block_rows = min(512, slot_count)
    pieces = list(low_pieces) + list(high_pieces)
    specs = [pl.BlockSpec(piece.shape, lambda i: (0, 0, 0, 0)) for piece in pieces]
    return pl.pallas_call(
        functools.partial(pieces_kernel, len(low_pieces), len(high_pieces)),
        grid=(slot_count // block_rows,),
        in_specs=specs,
        out_specs=[
            pl.BlockSpec((block_rows, slot_count), lambda i: (i, 0)),
            pl.BlockSpec((1, block_rows), lambda i: (0, i)),
        ],
        out_shape=[
            jax.ShapeDtypeStruct((slot_count, slot_count), jnp.bfloat16),
            jax.ShapeDtypeStruct((1, slot_count), jnp.float32),
        ],
        scratch_shapes=[
            pltpu.VMEM((sources, quarters, part, width), jnp.bfloat16),
            pltpu.VMEM((1, slot_count), jnp.float32),
        ],
        compiler_params=pltpu.CompilerParams(dimension_semantics=("arbitrary",)),
        cost_estimate=pl.CostEstimate(
            flops=2 * slot_count * slot_count * width + 22 * slot_count * slot_count,
            transcendentals=0,
            bytes_accessed=slot_count * width * 2 + 2 * slot_count * slot_count,
        ),
    )(*pieces)


def on_device(embeddings, labels, image_lists, rank_keys):
    img_count = lax.axis_size("img")
    sub_count = lax.axis_size("sub")
    per_list = SLOTS // img_count
    part = per_list // sub_count
    rows_here = image_lists.shape[0]
    pair_count = rows_here * 2
    lists_flat = image_lists.reshape(-1)
    order = jnp.arange(pair_count, dtype=jnp.int32)
    same = (lists_flat[:, None] == lists_flat[None, :]) & (order[None, :] < order[:, None])
    within = jnp.sum(same.astype(jnp.int32), axis=1)
    slot_of_pair = (lists_flat * per_list + within).reshape(rows_here, 2)
    slot_total = LIST_DEV * img_count * per_list

    arrival = [0]
    bit = sub_count // 2
    while bit >= 1:
        arrival = arrival + [d ^ bit for d in arrival]
        bit //= 2
    me_sub = lax.axis_index("sub")
    quarters = jnp.bitwise_xor(me_sub, jnp.array(arrival, dtype=jnp.int32))
    slot_ids = (
        jnp.arange(img_count, dtype=jnp.int32)[:, None, None] * per_list
        + quarters[None, :, None] * part
        + jnp.arange(part, dtype=jnp.int32)[None, None, :]
    ).reshape(-1, 1)
    hit_a = slot_of_pair[None, :, 0] == slot_ids
    hit_b = slot_of_pair[None, :, 1] == slot_ids
    hit = hit_a | hit_b
    pick = hit.astype(jnp.bfloat16)

    def to_bucket(rows):
        picked = jnp.dot(pick, rows, preferred_element_type=jnp.float32).astype(rows.dtype)
        return picked.reshape(img_count, LIST_DEV, per_list, rows.shape[1])

    def bucket_major(listed):
        shaped = listed.reshape((listed.shape[0], img_count, per_list) + listed.shape[2:])
        return jnp.moveaxis(shaped, 0, 1)

    def from_bucket(returned):
        flat = returned.reshape(slot_total, -1)
        return jnp.einsum(
            "kg,kc->gc", pick.astype(jnp.float32), flat,
            precision=lax.Precision.HIGH, preferred_element_type=jnp.float32,
        )

    values = embeddings.astype(jnp.float32)
    unit = (values * lax.rsqrt(jnp.sum(values * values, axis=1, keepdims=True) + 1e-06)).astype(
        jnp.bfloat16
    )
    mine = (
        jnp.arange(img_count, dtype=jnp.int32)[:, None] * per_list
        + me_sub * part
        + jnp.arange(part, dtype=jnp.int32)[None, :]
    ).reshape(-1, 1)
    mine_a = slot_of_pair[None, :, 0] == mine
    mine_b = slot_of_pair[None, :, 1] == mine
    mine_hit = mine_a | mine_b
    keys_f = rank_keys.astype(jnp.float32)
    key_sum = jnp.sum(
        jnp.where(mine_a, keys_f[None, :, 0], 0.0) + jnp.where(mine_b, keys_f[None, :, 1], 0.0),
        axis=1,
    )
    mine_keys = jnp.where(jnp.any(mine_hit, axis=1), key_sum, -4096.0).astype(jnp.bfloat16)
    width = unit.shape[1]
    quarter = jnp.dot(mine_hit.astype(jnp.bfloat16), unit, preferred_element_type=jnp.float32)
    half = max(128, width // 3 // 128 * 128)
    quarter = quarter.astype(jnp.bfloat16).reshape(img_count, part, width)
    low_payload = jnp.concatenate(
        [
            quarter[:, :, :half],
            jnp.pad(mine_keys.reshape(img_count, 1, part), ((0, 0), (0, 0), (0, half - part))),
        ],
        axis=1,
    )
    high_payload = quarter[:, :, half:]

    def exchange_stage(got, bit):
        pairs = [(t, t ^ bit) for t in range(sub_count)]
        return jnp.concatenate([got, lax.ppermute(got, "sub", pairs)], axis=0)

    low_got = lax.all_to_all(low_payload, "img", split_axis=0, concat_axis=0, tiled=True)[None]
    high_got = lax.all_to_all(high_payload, "img", split_axis=0, concat_axis=0, tiled=True)[None]
    bit = sub_count // 2
    while bit > 1:
        low_got = exchange_stage(low_got, bit)
        high_got = exchange_stage(high_got, bit)
        bit //= 2
    last = [(t, t ^ bit) for t in range(sub_count)] if bit == 1 else None
    low_pieces = [low_got] + ([lax.ppermute(low_got, "sub", last)] if last else [])
    high_pieces = [high_got] + ([lax.ppermute(high_got, "sub", last)] if last else [])
    slot_count = slot_total
    key_rows = jnp.moveaxis(
        jnp.concatenate([piece[:, :, part, :part] for piece in low_pieces], axis=0), 0, 1
    ).reshape(slot_count).astype(jnp.float32)
    weight_mat, row_sums = pieces_affinity(low_pieces, high_pieces, key_rows, part)
    weights = weight_mat.reshape(1, slot_count, slot_count)
    degree_slots = lax.all_to_all(
        bucket_major(row_sums), "img", split_axis=0, concat_axis=0, tiled=True
    )
    degree = jnp.sum(jnp.where(hit, degree_slots.reshape(slot_total, 1), 0.0), axis=0)
    inv = lax.rsqrt(degree)
    starting = labels.astype(jnp.float32)
    current = starting
    for step in range(2):
        scaled = (inv[:, None] * current).astype(jnp.bfloat16)
        arrived = lax.all_to_all(to_bucket(scaled), "img", split_axis=0, concat_axis=0, tiled=True)
        product = jnp.einsum(
            "ajk,akc->ajc", weights, list_major(arrived), preferred_element_type=jnp.float32
        )
        returned = lax.all_to_all(
            bucket_major(product), "img", split_axis=0, concat_axis=0, tiled=True
        )
        spread = from_bucket(returned)
        current = 0.8 * inv[:, None] * spread + 0.2 * starting
    return current.astype(jnp.bfloat16)


def solution(mesh):
    return jax.shard_map(
        on_device,
        mesh=mesh,
        in_specs=(P("img", None), P("img", "sub"), P("img", None), P("img", None)),
        out_specs=P("img", "sub"),
        check_vma=False,
    )
```

```python
import functools

import jax
import jax.numpy as jnp
from jax import lax
from jax.experimental import pallas as pl
from jax.experimental.pallas import tpu as pltpu
from jax.sharding import PartitionSpec as P

SLOTS = 2048
BAND = 64
LIST_DEV = 1


def list_major(bucket):
    moved = jnp.moveaxis(bucket, 1, 0)
    return moved.reshape((moved.shape[0], moved.shape[1] * moved.shape[2]) + moved.shape[3:])


def affinity_kernel(col_keys, low_rows, high_rows, weights, row_sums, joined):
    block_rows = weights.shape[0]
    slot_count = weights.shape[1]
    half = joined.shape[1] - high_rows.shape[-1]

    @pl.when(pl.program_id(0) == 0)
    def _():
        low = low_rows[...]
        high = high_rows[...]
        joined[:, :half] = low.reshape(slot_count, low.shape[-1])[:, :half]
        joined[:, half:] = high.reshape(slot_count, high.shape[-1])

    start = pl.multiple_of(pl.program_id(0) * block_rows, block_rows)
    contract = (((1,), (1,)), ((), ()))
    gram = lax.dot_general(
        joined[pl.ds(start, block_rows), :], joined[...], contract,
        preferred_element_type=jnp.float32,
    )
    own_keys = col_keys[:, pl.ds(start, block_rows)]
    diagonal = (
        lax.broadcasted_iota(jnp.int32, (block_rows, block_rows), 0)
        == lax.broadcasted_iota(jnp.int32, (block_rows, block_rows), 1)
    )
    row_keys = jnp.sum(jnp.where(diagonal, own_keys, 0.0), axis=1, keepdims=True)
    keep = jnp.abs(row_keys - col_keys[...]) <= BAND
    positive = jnp.maximum(gram, 0.0)
    cubed = jnp.where(keep, positive * positive * positive, 0.0).astype(jnp.bfloat16)
    weights[...] = cubed
    ones = jnp.ones((8, slot_count), jnp.bfloat16)
    summed = lax.dot_general(ones, cubed, contract, preferred_element_type=jnp.float32)
    row_sums[...] = summed[0:1, :]


def fused_affinity(low, high, keys, part):
    sources, quarters = high.shape[0], high.shape[1]
    slot_count = sources * quarters * part
    half = low.shape[3]
    width = half + high.shape[3]
    if part % 16 == 0:
        low_spec = pl.BlockSpec((sources, quarters, part, half), lambda i: (0, 0, 0, 0))
        high_spec = pl.BlockSpec(high.shape, lambda i: (0, 0, 0, 0))
    else:
        low = low[:, :, :part, :].reshape(slot_count, half)
        high = high.reshape(slot_count, width - half)
        low_spec = pl.BlockSpec(low.shape, lambda i: (0, 0))
        high_spec = pl.BlockSpec(high.shape, lambda i: (0, 0))
    block_rows = min(512, slot_count)
    return pl.pallas_call(
        affinity_kernel,
        grid=(slot_count // block_rows,),
        in_specs=[pl.BlockSpec((1, slot_count), lambda i: (0, 0)), low_spec, high_spec],
        out_specs=[
            pl.BlockSpec((block_rows, slot_count), lambda i: (i, 0)),
            pl.BlockSpec((1, block_rows), lambda i: (0, i)),
        ],
        out_shape=[
            jax.ShapeDtypeStruct((slot_count, slot_count), jnp.bfloat16),
            jax.ShapeDtypeStruct((1, slot_count), jnp.float32),
        ],
        scratch_shapes=[pltpu.VMEM((slot_count, width), jnp.bfloat16)],
        compiler_params=pltpu.CompilerParams(dimension_semantics=("arbitrary",)),
        cost_estimate=pl.CostEstimate(
            flops=2 * slot_count * slot_count * width + 22 * slot_count * slot_count,
            transcendentals=0,
            bytes_accessed=slot_count * width * 2 + 2 * slot_count * slot_count,
        ),
    )(keys.reshape(1, slot_count), low, high)


def pieces_kernel(low_count, high_count, col_keys, *refs):
    low_refs = refs[:low_count]
    high_refs = refs[low_count:low_count + high_count]
    weights, row_sums, joined = refs[low_count + high_count:]
    block_rows = weights.shape[0]
    slot_count = weights.shape[1]
    quarters, part, width = joined.shape[1], joined.shape[2], joined.shape[3]
    half = low_refs[0].shape[-1]

    @pl.when(pl.program_id(0) == 0)
    def _():
        for group, lo, hi in ((low_refs, 0, half), (high_refs, half, width)):
            at = 0
            for ref in group:
                for m in range(ref.shape[0]):
                    joined[:, at, :, lo:hi] = ref[m]
                    at += 1

    per_block = block_rows // (quarters * part)
    first = pl.multiple_of(pl.program_id(0) * per_block, per_block)
    start = pl.multiple_of(pl.program_id(0) * block_rows, block_rows)
    contract = (((1,), (1,)), ((), ()))
    gram = lax.dot_general(
        joined[pl.ds(first, per_block)].reshape(block_rows, width),
        joined[...].reshape(slot_count, width), contract,
        preferred_element_type=jnp.float32,
    )
    own_keys = col_keys[:, pl.ds(start, block_rows)]
    diagonal = (
        lax.broadcasted_iota(jnp.int32, (block_rows, block_rows), 0)
        == lax.broadcasted_iota(jnp.int32, (block_rows, block_rows), 1)
    )
    row_keys = jnp.sum(jnp.where(diagonal, own_keys, 0.0), axis=1, keepdims=True)
    keep = jnp.abs(row_keys - col_keys[...]) <= BAND
    positive = jnp.maximum(gram, 0.0)
    cubed = jnp.where(keep, positive * positive * positive, 0.0).astype(jnp.bfloat16)
    weights[...] = cubed
    ones = jnp.ones((8, slot_count), jnp.bfloat16)
    summed = lax.dot_general(ones, cubed, contract, preferred_element_type=jnp.float32)
    row_sums[...] = summed[0:1, :]


def pieces_affinity(low_pieces, high_pieces, keys, part):
    sources = low_pieces[0].shape[1]
    quarters = sum(piece.shape[0] for piece in low_pieces)
    half = low_pieces[0].shape[3]
    width = half + high_pieces[0].shape[3]
    if part % 16 != 0 or (2 * quarters * part) % 128 != 0:
        def source_major(group):
            stacked = jnp.concatenate([piece[:, :, :part] for piece in group], axis=0)
            return jnp.moveaxis(stacked, 0, 1)
        return fused_affinity(source_major(low_pieces), source_major(high_pieces), keys, part)
    slot_count = sources * quarters * part
    block_rows = min(512, slot_count)
    pieces = list(low_pieces) + list(high_pieces)
    specs = [
        pl.BlockSpec((piece.shape[0], sources, part, piece.shape[3]), lambda i: (0, 0, 0, 0))
        for piece in pieces
    ]
    return pl.pallas_call(
        functools.partial(pieces_kernel, len(low_pieces), len(high_pieces)),
        grid=(slot_count // block_rows,),
        in_specs=[pl.BlockSpec((1, slot_count), lambda i: (0, 0))] + specs,
        out_specs=[
            pl.BlockSpec((block_rows, slot_count), lambda i: (i, 0)),
            pl.BlockSpec((1, block_rows), lambda i: (0, i)),
        ],
        out_shape=[
            jax.ShapeDtypeStruct((slot_count, slot_count), jnp.bfloat16),
            jax.ShapeDtypeStruct((1, slot_count), jnp.float32),
        ],
        scratch_shapes=[pltpu.VMEM((sources, quarters, part, width), jnp.bfloat16)],
        compiler_params=pltpu.CompilerParams(dimension_semantics=("arbitrary",)),
        cost_estimate=pl.CostEstimate(
            flops=2 * slot_count * slot_count * width + 22 * slot_count * slot_count,
            transcendentals=0,
            bytes_accessed=slot_count * width * 2 + 2 * slot_count * slot_count,
        ),
    )(keys.reshape(1, slot_count), *pieces)


def on_device(embeddings, labels, image_lists, rank_keys):
    img_count = lax.axis_size("img")
    sub_count = lax.axis_size("sub")
    per_list = SLOTS // img_count
    part = per_list // sub_count
    rows_here = image_lists.shape[0]
    pair_count = rows_here * 2
    lists_flat = image_lists.reshape(-1)
    order = jnp.arange(pair_count, dtype=jnp.int32)
    same = (lists_flat[:, None] == lists_flat[None, :]) & (order[None, :] < order[:, None])
    within = jnp.sum(same.astype(jnp.int32), axis=1)
    slot_of_pair = (lists_flat * per_list + within).reshape(rows_here, 2)
    slot_total = LIST_DEV * img_count * per_list

    arrival = [0]
    bit = sub_count // 2
    while bit >= 1:
        arrival = arrival + [d ^ bit for d in arrival]
        bit //= 2
    me_sub = lax.axis_index("sub")
    quarters = jnp.bitwise_xor(me_sub, jnp.array(arrival, dtype=jnp.int32))
    slot_ids = (
        jnp.arange(img_count, dtype=jnp.int32)[:, None, None] * per_list
        + quarters[None, :, None] * part
        + jnp.arange(part, dtype=jnp.int32)[None, None, :]
    ).reshape(-1, 1)
    hit_a = slot_of_pair[None, :, 0] == slot_ids
    hit_b = slot_of_pair[None, :, 1] == slot_ids
    hit = hit_a | hit_b
    pick = lax.optimization_barrier(hit.astype(jnp.bfloat16))

    def to_bucket(rows):
        picked = jnp.dot(pick, rows, preferred_element_type=jnp.float32).astype(rows.dtype)
        return picked.reshape(img_count, LIST_DEV, per_list, rows.shape[1])

    def bucket_major(listed):
        shaped = listed.reshape((listed.shape[0], img_count, per_list) + listed.shape[2:])
        return jnp.moveaxis(shaped, 0, 1)

    def from_bucket(returned):
        flat = returned.reshape(slot_total, -1)
        return jnp.einsum(
            "kg,kc->gc", pick.astype(jnp.float32), flat,
            precision=lax.Precision.HIGH, preferred_element_type=jnp.float32,
        )

    values = embeddings.astype(jnp.float32)
    unit = (values * lax.rsqrt(jnp.sum(values * values, axis=1, keepdims=True) + 1e-06)).astype(
        jnp.bfloat16
    )
    mine = (
        jnp.arange(img_count, dtype=jnp.int32)[:, None] * per_list
        + me_sub * part
        + jnp.arange(part, dtype=jnp.int32)[None, :]
    ).reshape(-1, 1)
    mine_a = slot_of_pair[None, :, 0] == mine
    mine_b = slot_of_pair[None, :, 1] == mine
    mine_hit = mine_a | mine_b
    keys_f = rank_keys.astype(jnp.float32)
    key_sum = jnp.sum(
        jnp.where(mine_a, keys_f[None, :, 0], 0.0) + jnp.where(mine_b, keys_f[None, :, 1], 0.0),
        axis=1,
    )
    mine_keys = jnp.where(jnp.any(mine_hit, axis=1), key_sum, -4096.0).astype(jnp.bfloat16)
    width = unit.shape[1]
    quarter = jnp.dot(mine_hit.astype(jnp.bfloat16), unit, preferred_element_type=jnp.float32)
    half = max(128, width // 3 // 128 * 128)
    quarter = quarter.astype(jnp.bfloat16).reshape(img_count, part, width)
    low_payload = jnp.concatenate(
        [
            quarter[:, :, :half],
            jnp.pad(mine_keys.reshape(img_count, 1, part), ((0, 0), (0, 0), (0, half - part))),
        ],
        axis=1,
    )
    high_payload = quarter[:, :, half:]

    def exchange_stage(got, bit):
        pairs = [(t, t ^ bit) for t in range(sub_count)]
        return jnp.concatenate([got, lax.ppermute(got, "sub", pairs)], axis=0)

    low_got = lax.all_to_all(low_payload, "img", split_axis=0, concat_axis=0, tiled=True)[None]
    high_got = lax.all_to_all(high_payload, "img", split_axis=0, concat_axis=0, tiled=True)[None]
    bit = sub_count // 2
    while bit > 1:
        low_got = exchange_stage(low_got, bit)
        high_got = exchange_stage(high_got, bit)
        bit //= 2
    last = [(t, t ^ bit) for t in range(sub_count)] if bit == 1 else None
    low_pieces = [low_got] + ([lax.ppermute(low_got, "sub", last)] if last else [])
    high_pieces = [high_got] + ([lax.ppermute(high_got, "sub", last)] if last else [])
    slot_count = slot_total
    key_rows = jnp.moveaxis(
        jnp.concatenate([piece[:, :, part, :part] for piece in low_pieces], axis=0), 0, 1
    ).reshape(slot_count).astype(jnp.float32)
    weight_mat, row_sums = pieces_affinity(low_pieces, high_pieces, key_rows, part)
    weights = weight_mat.reshape(1, slot_count, slot_count)
    degree_slots = lax.all_to_all(
        bucket_major(row_sums), "img", split_axis=0, concat_axis=0, tiled=True
    )
    degree = jnp.sum(jnp.where(pick > 0, degree_slots.reshape(slot_total, 1), 0.0), axis=0)
    inv = lax.rsqrt(degree)
    starting = labels.astype(jnp.float32)
    current = starting
    for step in range(2):
        scaled = (inv[:, None] * current).astype(jnp.bfloat16)
        arrived = lax.all_to_all(to_bucket(scaled), "img", split_axis=0, concat_axis=0, tiled=True)
        product = jnp.einsum(
            "ajk,akc->ajc", weights, list_major(arrived), preferred_element_type=jnp.float32
        )
        returned = lax.all_to_all(
            bucket_major(product), "img", split_axis=0, concat_axis=0, tiled=True
        )
        spread = from_bucket(returned)
        current = 0.8 * inv[:, None] * spread + 0.2 * starting
    return current.astype(jnp.bfloat16)


def solution(mesh):
    return jax.shard_map(
        on_device,
        mesh=mesh,
        in_specs=(P("img", None), P("img", "sub"), P("img", None), P("img", None)),
        out_specs=P("img", "sub"),
        check_vma=False,
    )
```

```python
import functools

import jax
import jax.numpy as jnp
from jax import lax
from jax.experimental import pallas as pl
from jax.experimental.pallas import tpu as pltpu
from jax.sharding import PartitionSpec as P

SLOTS = 2048
BAND = 64
LIST_DEV = 1


def list_major(bucket):
    moved = jnp.moveaxis(bucket, 1, 0)
    return moved.reshape((moved.shape[0], moved.shape[1] * moved.shape[2]) + moved.shape[3:])


def affinity_kernel(col_keys, low_rows, high_rows, weights, row_sums, joined):
    block_rows = weights.shape[0]
    slot_count = weights.shape[1]
    half = joined.shape[1] - high_rows.shape[-1]

    @pl.when(pl.program_id(0) == 0)
    def _():
        low = low_rows[...]
        high = high_rows[...]
        joined[:, :half] = low.reshape(slot_count, low.shape[-1])[:, :half]
        joined[:, half:] = high.reshape(slot_count, high.shape[-1])

    start = pl.multiple_of(pl.program_id(0) * block_rows, block_rows)
    contract = (((1,), (1,)), ((), ()))
    gram = lax.dot_general(
        joined[pl.ds(start, block_rows), :], joined[...], contract,
        preferred_element_type=jnp.float32,
    )
    own_keys = col_keys[:, pl.ds(start, block_rows)]
    diagonal = (
        lax.broadcasted_iota(jnp.int32, (block_rows, block_rows), 0)
        == lax.broadcasted_iota(jnp.int32, (block_rows, block_rows), 1)
    )
    row_keys = jnp.sum(jnp.where(diagonal, own_keys, 0.0), axis=1, keepdims=True)
    keep = jnp.abs(row_keys - col_keys[...]) <= BAND
    positive = jnp.maximum(gram, 0.0)
    cubed = jnp.where(keep, positive * positive * positive, 0.0).astype(jnp.bfloat16)
    weights[...] = cubed
    ones = jnp.ones((8, slot_count), jnp.bfloat16)
    summed = lax.dot_general(ones, cubed, contract, preferred_element_type=jnp.float32)
    row_sums[...] = summed[0:1, :]


def fused_affinity(low, high, keys, part):
    sources, quarters = high.shape[0], high.shape[1]
    slot_count = sources * quarters * part
    half = low.shape[3]
    width = half + high.shape[3]
    if part % 16 == 0:
        low_spec = pl.BlockSpec((sources, quarters, part, half), lambda i: (0, 0, 0, 0))
        high_spec = pl.BlockSpec(high.shape, lambda i: (0, 0, 0, 0))
    else:
        low = low[:, :, :part, :].reshape(slot_count, half)
        high = high.reshape(slot_count, width - half)
        low_spec = pl.BlockSpec(low.shape, lambda i: (0, 0))
        high_spec = pl.BlockSpec(high.shape, lambda i: (0, 0))
    block_rows = min(512, slot_count)
    return pl.pallas_call(
        affinity_kernel,
        grid=(slot_count // block_rows,),
        in_specs=[pl.BlockSpec((1, slot_count), lambda i: (0, 0)), low_spec, high_spec],
        out_specs=[
            pl.BlockSpec((block_rows, slot_count), lambda i: (i, 0)),
            pl.BlockSpec((1, block_rows), lambda i: (0, i)),
        ],
        out_shape=[
            jax.ShapeDtypeStruct((slot_count, slot_count), jnp.bfloat16),
            jax.ShapeDtypeStruct((1, slot_count), jnp.float32),
        ],
        scratch_shapes=[pltpu.VMEM((slot_count, width), jnp.bfloat16)],
        compiler_params=pltpu.CompilerParams(dimension_semantics=("arbitrary",)),
        cost_estimate=pl.CostEstimate(
            flops=2 * slot_count * slot_count * width + 22 * slot_count * slot_count,
            transcendentals=0,
            bytes_accessed=slot_count * width * 2 + 2 * slot_count * slot_count,
        ),
    )(keys.reshape(1, slot_count), low, high)


def pieces_kernel(low_count, high_count, col_keys, *refs):
    low_refs = refs[:low_count]
    high_refs = refs[low_count:low_count + high_count]
    weights, row_sums, joined = refs[low_count + high_count:]
    block_rows = weights.shape[0]
    slot_count = weights.shape[1]
    quarters, part, width = joined.shape[1], joined.shape[2], joined.shape[3]
    half = low_refs[0].shape[-1]

    @pl.when(pl.program_id(0) == 0)
    def _():
        for group, lo, hi in ((low_refs, 0, half), (high_refs, half, width)):
            at = 0
            for ref in group:
                for m in range(ref.shape[0]):
                    joined[:, at, :, lo:hi] = ref[m]
                    at += 1

    per_block = block_rows // (quarters * part)
    first = pl.multiple_of(pl.program_id(0) * per_block, per_block)
    start = pl.multiple_of(pl.program_id(0) * block_rows, block_rows)
    contract = (((1,), (1,)), ((), ()))
    gram = lax.dot_general(
        joined[pl.ds(first, per_block)].reshape(block_rows, width),
        joined[...].reshape(slot_count, width), contract,
        preferred_element_type=jnp.float32,
    )
    own_keys = col_keys[:, pl.ds(start, block_rows)]
    diagonal = (
        lax.broadcasted_iota(jnp.int32, (block_rows, block_rows), 0)
        == lax.broadcasted_iota(jnp.int32, (block_rows, block_rows), 1)
    )
    row_keys = jnp.sum(jnp.where(diagonal, own_keys, 0.0), axis=1, keepdims=True)
    keep = jnp.abs(row_keys - col_keys[...]) <= BAND
    positive = jnp.maximum(gram, 0.0)
    cubed = jnp.where(keep, positive * positive * positive, 0.0).astype(jnp.bfloat16)
    weights[...] = cubed
    ones = jnp.ones((8, slot_count), jnp.bfloat16)
    summed = lax.dot_general(ones, cubed, contract, preferred_element_type=jnp.float32)
    row_sums[...] = summed[0:1, :]


def pieces_affinity(low_pieces, high_pieces, keys, part):
    sources = low_pieces[0].shape[1]
    quarters = sum(piece.shape[0] for piece in low_pieces)
    half = low_pieces[0].shape[3]
    width = half + high_pieces[0].shape[3]
    if part % 16 != 0 or (2 * quarters * part) % 128 != 0:
        def source_major(group):
            stacked = jnp.concatenate([piece[:, :, :part] for piece in group], axis=0)
            return jnp.moveaxis(stacked, 0, 1)
        return fused_affinity(source_major(low_pieces), source_major(high_pieces), keys, part)
    slot_count = sources * quarters * part
    block_rows = min(512, slot_count)
    pieces = list(low_pieces) + list(high_pieces)
    specs = [
        pl.BlockSpec((piece.shape[0], sources, part, piece.shape[3]), lambda i: (0, 0, 0, 0))
        for piece in pieces
    ]
    return pl.pallas_call(
        functools.partial(pieces_kernel, len(low_pieces), len(high_pieces)),
        grid=(slot_count // block_rows,),
        in_specs=[pl.BlockSpec((1, slot_count), lambda i: (0, 0))] + specs,
        out_specs=[
            pl.BlockSpec((block_rows, slot_count), lambda i: (i, 0)),
            pl.BlockSpec((1, block_rows), lambda i: (0, i)),
        ],
        out_shape=[
            jax.ShapeDtypeStruct((slot_count, slot_count), jnp.bfloat16),
            jax.ShapeDtypeStruct((1, slot_count), jnp.float32),
        ],
        scratch_shapes=[pltpu.VMEM((sources, quarters, part, width), jnp.bfloat16)],
        compiler_params=pltpu.CompilerParams(dimension_semantics=("arbitrary",)),
        cost_estimate=pl.CostEstimate(
            flops=2 * slot_count * slot_count * width + 22 * slot_count * slot_count,
            transcendentals=0,
            bytes_accessed=slot_count * width * 2 + 2 * slot_count * slot_count,
        ),
    )(keys.reshape(1, slot_count), *pieces)


def on_device(embeddings, labels, image_lists, rank_keys):
    img_count = lax.axis_size("img")
    sub_count = lax.axis_size("sub")
    per_list = SLOTS // img_count
    part = per_list // sub_count
    rows_here = image_lists.shape[0]
    pair_count = rows_here * 2
    lists_flat = image_lists.reshape(-1)
    order = jnp.arange(pair_count, dtype=jnp.int32)
    same = (lists_flat[:, None] == lists_flat[None, :]) & (order[None, :] < order[:, None])
    within = jnp.sum(same.astype(jnp.int32), axis=1)
    slot_of_pair = (lists_flat * per_list + within).reshape(rows_here, 2)
    slot_total = LIST_DEV * img_count * per_list

    arrival = [0]
    bit = sub_count // 2
    while bit >= 1:
        arrival = arrival + [d ^ bit for d in arrival]
        bit //= 2
    me_sub = lax.axis_index("sub")
    quarters = jnp.bitwise_xor(me_sub, jnp.array(arrival, dtype=jnp.int32))
    slot_ids = (
        jnp.arange(img_count, dtype=jnp.int32)[:, None, None] * per_list
        + quarters[None, :, None] * part
        + jnp.arange(part, dtype=jnp.int32)[None, None, :]
    ).reshape(-1, 1)
    hit_a = slot_of_pair[None, :, 0] == slot_ids
    hit_b = slot_of_pair[None, :, 1] == slot_ids
    hit = hit_a | hit_b
    pick = hit.astype(jnp.bfloat16)

    def to_bucket(rows):
        picked = jnp.dot(pick, rows, preferred_element_type=jnp.float32).astype(rows.dtype)
        return picked.reshape(img_count, LIST_DEV, per_list, rows.shape[1])

    def bucket_major(listed):
        shaped = listed.reshape((listed.shape[0], img_count, per_list) + listed.shape[2:])
        return jnp.moveaxis(shaped, 0, 1)

    def from_bucket(returned):
        flat = returned.reshape(slot_total, -1)
        return jnp.einsum(
            "kg,kc->gc", pick.astype(jnp.float32), flat,
            precision=lax.Precision.HIGH, preferred_element_type=jnp.float32,
        )

    values = embeddings.astype(jnp.float32)
    unit = (values * lax.rsqrt(jnp.sum(values * values, axis=1, keepdims=True) + 1e-06)).astype(
        jnp.bfloat16
    )
    mine = (
        jnp.arange(img_count, dtype=jnp.int32)[:, None] * per_list
        + me_sub * part
        + jnp.arange(part, dtype=jnp.int32)[None, :]
    ).reshape(-1, 1)
    mine_a = slot_of_pair[None, :, 0] == mine
    mine_b = slot_of_pair[None, :, 1] == mine
    mine_hit = mine_a | mine_b
    keys_f = rank_keys.astype(jnp.float32)
    key_sum = jnp.sum(
        jnp.where(mine_a, keys_f[None, :, 0], 0.0) + jnp.where(mine_b, keys_f[None, :, 1], 0.0),
        axis=1,
    )
    mine_keys = jnp.where(jnp.any(mine_hit, axis=1), key_sum, -4096.0).astype(jnp.bfloat16)
    width = unit.shape[1]
    quarter = jnp.dot(mine_hit.astype(jnp.bfloat16), unit, preferred_element_type=jnp.float32)
    half = max(128, width // 3 // 128 * 128)
    quarter = quarter.astype(jnp.bfloat16).reshape(img_count, part, width)
    low_payload = jnp.concatenate(
        [
            quarter[:, :, :half],
            jnp.pad(mine_keys.reshape(img_count, 1, part), ((0, 0), (0, 0), (0, half - part))),
        ],
        axis=1,
    )
    high_payload = quarter[:, :, half:]

    def exchange_stage(got, bit):
        pairs = [(t, t ^ bit) for t in range(sub_count)]
        return jnp.concatenate([got, lax.ppermute(got, "sub", pairs)], axis=0)

    low_got = lax.all_to_all(low_payload, "img", split_axis=0, concat_axis=0, tiled=True)[None]
    high_got = lax.all_to_all(high_payload, "img", split_axis=0, concat_axis=0, tiled=True)[None]
    high_got, pick = lax.optimization_barrier((high_got, pick))
    bit = sub_count // 2
    while bit > 1:
        low_got = exchange_stage(low_got, bit)
        high_got = exchange_stage(high_got, bit)
        bit //= 2
    last = [(t, t ^ bit) for t in range(sub_count)] if bit == 1 else None
    low_pieces = [low_got] + ([lax.ppermute(low_got, "sub", last)] if last else [])
    high_pieces = [high_got] + ([lax.ppermute(high_got, "sub", last)] if last else [])
    slot_count = slot_total
    key_rows = jnp.moveaxis(
        jnp.concatenate([piece[:, :, part, :part] for piece in low_pieces], axis=0), 0, 1
    ).reshape(slot_count).astype(jnp.float32)
    weight_mat, row_sums = pieces_affinity(low_pieces, high_pieces, key_rows, part)
    weights = weight_mat.reshape(1, slot_count, slot_count)
    degree_slots = lax.all_to_all(
        bucket_major(row_sums), "img", split_axis=0, concat_axis=0, tiled=True
    )
    degree = jnp.sum(jnp.where(pick > 0, degree_slots.reshape(slot_total, 1), 0.0), axis=0)
    inv = lax.rsqrt(degree)
    starting = labels.astype(jnp.float32)
    current = starting
    for step in range(2):
        scaled = (inv[:, None] * current).astype(jnp.bfloat16)
        arrived = lax.all_to_all(to_bucket(scaled), "img", split_axis=0, concat_axis=0, tiled=True)
        product = jnp.einsum(
            "ajk,akc->ajc", weights, list_major(arrived), preferred_element_type=jnp.float32
        )
        returned = lax.all_to_all(
            bucket_major(product), "img", split_axis=0, concat_axis=0, tiled=True
        )
        spread = from_bucket(returned)
        current = 0.8 * inv[:, None] * spread + 0.2 * starting
    return current.astype(jnp.bfloat16)


def solution(mesh):
    return jax.shard_map(
        on_device,
        mesh=mesh,
        in_specs=(P("img", None), P("img", "sub"), P("img", None), P("img", None)),
        out_specs=P("img", "sub"),
        check_vma=False,
    )
```

```python
import functools

import jax
import jax.numpy as jnp
from jax import lax
from jax.experimental import pallas as pl
from jax.experimental.pallas import tpu as pltpu
from jax.sharding import PartitionSpec as P

SLOTS = 2048
BAND = 64
LIST_DEV = 1


def list_major(bucket):
    moved = jnp.moveaxis(bucket, 1, 0)
    return moved.reshape((moved.shape[0], moved.shape[1] * moved.shape[2]) + moved.shape[3:])


def affinity_kernel(col_keys, low_rows, high_rows, weights, row_sums, joined):
    block_rows = weights.shape[0]
    slot_count = weights.shape[1]
    half = joined.shape[1] - high_rows.shape[-1]

    @pl.when(pl.program_id(0) == 0)
    def _():
        low = low_rows[...]
        high = high_rows[...]
        joined[:, :half] = low.reshape(slot_count, low.shape[-1])[:, :half]
        joined[:, half:] = high.reshape(slot_count, high.shape[-1])

    start = pl.multiple_of(pl.program_id(0) * block_rows, block_rows)
    contract = (((1,), (1,)), ((), ()))
    gram = lax.dot_general(
        joined[pl.ds(start, block_rows), :], joined[...], contract,
        preferred_element_type=jnp.float32,
    )
    own_keys = col_keys[:, pl.ds(start, block_rows)]
    diagonal = (
        lax.broadcasted_iota(jnp.int32, (block_rows, block_rows), 0)
        == lax.broadcasted_iota(jnp.int32, (block_rows, block_rows), 1)
    )
    row_keys = jnp.sum(jnp.where(diagonal, own_keys, 0.0), axis=1, keepdims=True)
    keep = jnp.abs(row_keys - col_keys[...]) <= BAND
    positive = jnp.maximum(gram, 0.0)
    cubed = jnp.where(keep, positive * positive * positive, 0.0).astype(jnp.bfloat16)
    weights[...] = cubed
    ones = jnp.ones((8, slot_count), jnp.bfloat16)
    summed = lax.dot_general(ones, cubed, contract, preferred_element_type=jnp.float32)
    row_sums[...] = summed[0:1, :]


def fused_affinity(low, high, keys, part):
    sources, quarters = high.shape[0], high.shape[1]
    slot_count = sources * quarters * part
    half = low.shape[3]
    width = half + high.shape[3]
    if part % 16 == 0:
        low_spec = pl.BlockSpec((sources, quarters, part, half), lambda i: (0, 0, 0, 0))
        high_spec = pl.BlockSpec(high.shape, lambda i: (0, 0, 0, 0))
    else:
        low = low[:, :, :part, :].reshape(slot_count, half)
        high = high.reshape(slot_count, width - half)
        low_spec = pl.BlockSpec(low.shape, lambda i: (0, 0))
        high_spec = pl.BlockSpec(high.shape, lambda i: (0, 0))
    block_rows = min(512, slot_count)
    return pl.pallas_call(
        affinity_kernel,
        grid=(slot_count // block_rows,),
        in_specs=[pl.BlockSpec((1, slot_count), lambda i: (0, 0)), low_spec, high_spec],
        out_specs=[
            pl.BlockSpec((block_rows, slot_count), lambda i: (i, 0)),
            pl.BlockSpec((1, block_rows), lambda i: (0, i)),
        ],
        out_shape=[
            jax.ShapeDtypeStruct((slot_count, slot_count), jnp.bfloat16),
            jax.ShapeDtypeStruct((1, slot_count), jnp.float32),
        ],
        scratch_shapes=[pltpu.VMEM((slot_count, width), jnp.bfloat16)],
        compiler_params=pltpu.CompilerParams(dimension_semantics=("arbitrary",)),
        cost_estimate=pl.CostEstimate(
            flops=2 * slot_count * slot_count * width + 22 * slot_count * slot_count,
            transcendentals=0,
            bytes_accessed=slot_count * width * 2 + 2 * slot_count * slot_count,
        ),
    )(keys.reshape(1, slot_count), low, high)


def pieces_kernel(low_count, high_count, col_keys, *refs):
    low_refs = refs[:low_count]
    high_refs = refs[low_count:low_count + high_count]
    weights, row_sums, joined = refs[low_count + high_count:]
    block_rows = weights.shape[0]
    slot_count = weights.shape[1]
    quarters, part, width = joined.shape[1], joined.shape[2], joined.shape[3]
    half = low_refs[0].shape[-1]

    @pl.when(pl.program_id(0) == 0)
    def _():
        for group, lo, hi in ((low_refs, 0, half), (high_refs, half, width)):
            at = 0
            for ref in group:
                for m in range(ref.shape[0]):
                    joined[:, at, :, lo:hi] = ref[m]
                    at += 1

    per_block = block_rows // (quarters * part)
    first = pl.multiple_of(pl.program_id(0) * per_block, per_block)
    start = pl.multiple_of(pl.program_id(0) * block_rows, block_rows)
    contract = (((1,), (1,)), ((), ()))
    gram = lax.dot_general(
        joined[pl.ds(first, per_block)].reshape(block_rows, width),
        joined[...].reshape(slot_count, width), contract,
        preferred_element_type=jnp.float32,
    )
    own_keys = col_keys[:, pl.ds(start, block_rows)]
    diagonal = (
        lax.broadcasted_iota(jnp.int32, (block_rows, block_rows), 0)
        == lax.broadcasted_iota(jnp.int32, (block_rows, block_rows), 1)
    )
    row_keys = jnp.sum(jnp.where(diagonal, own_keys, 0.0), axis=1, keepdims=True)
    keep = jnp.abs(row_keys - col_keys[...]) <= BAND
    positive = jnp.maximum(gram, 0.0)
    cubed = jnp.where(keep, positive * positive * positive, 0.0).astype(jnp.bfloat16)
    weights[...] = cubed
    ones = jnp.ones((8, slot_count), jnp.bfloat16)
    summed = lax.dot_general(ones, cubed, contract, preferred_element_type=jnp.float32)
    row_sums[...] = summed[0:1, :]


def pieces_affinity(low_pieces, high_pieces, keys, part):
    sources = low_pieces[0].shape[1]
    quarters = sum(piece.shape[0] for piece in low_pieces)
    half = low_pieces[0].shape[3]
    width = half + high_pieces[0].shape[3]
    if part % 16 != 0 or (2 * quarters * part) % 128 != 0:
        def source_major(group):
            stacked = jnp.concatenate([piece[:, :, :part] for piece in group], axis=0)
            return jnp.moveaxis(stacked, 0, 1)
        return fused_affinity(source_major(low_pieces), source_major(high_pieces), keys, part)
    slot_count = sources * quarters * part
    block_rows = min(512, slot_count)
    pieces = list(low_pieces) + list(high_pieces)
    specs = [
        pl.BlockSpec((piece.shape[0], sources, part, piece.shape[3]), lambda i: (0, 0, 0, 0))
        for piece in pieces
    ]
    return pl.pallas_call(
        functools.partial(pieces_kernel, len(low_pieces), len(high_pieces)),
        grid=(slot_count // block_rows,),
        in_specs=[pl.BlockSpec((1, slot_count), lambda i: (0, 0))] + specs,
        out_specs=[
            pl.BlockSpec((block_rows, slot_count), lambda i: (i, 0)),
            pl.BlockSpec((1, block_rows), lambda i: (0, i)),
        ],
        out_shape=[
            jax.ShapeDtypeStruct((slot_count, slot_count), jnp.bfloat16),
            jax.ShapeDtypeStruct((1, slot_count), jnp.float32),
        ],
        scratch_shapes=[pltpu.VMEM((sources, quarters, part, width), jnp.bfloat16)],
        compiler_params=pltpu.CompilerParams(dimension_semantics=("arbitrary",)),
        cost_estimate=pl.CostEstimate(
            flops=2 * slot_count * slot_count * width + 22 * slot_count * slot_count,
            transcendentals=0,
            bytes_accessed=slot_count * width * 2 + 2 * slot_count * slot_count,
        ),
    )(keys.reshape(1, slot_count), *pieces)


def on_device(embeddings, labels, image_lists, rank_keys):
    img_count = lax.axis_size("img")
    sub_count = lax.axis_size("sub")
    per_list = SLOTS // img_count
    part = per_list // sub_count
    rows_here = image_lists.shape[0]
    pair_count = rows_here * 2
    lists_flat = image_lists.reshape(-1)
    order = jnp.arange(pair_count, dtype=jnp.int32)
    same = (lists_flat[:, None] == lists_flat[None, :]) & (order[None, :] < order[:, None])
    within = jnp.sum(same.astype(jnp.int32), axis=1)
    slot_of_pair = (lists_flat * per_list + within).reshape(rows_here, 2)
    slot_total = LIST_DEV * img_count * per_list

    arrival = [0]
    bit = sub_count // 2
    while bit >= 1:
        arrival = arrival + [d ^ bit for d in arrival]
        bit //= 2
    me_sub = lax.axis_index("sub")
    quarters = jnp.bitwise_xor(me_sub, jnp.array(arrival, dtype=jnp.int32))
    slot_ids = (
        jnp.arange(img_count, dtype=jnp.int32)[:, None, None] * per_list
        + quarters[None, :, None] * part
        + jnp.arange(part, dtype=jnp.int32)[None, None, :]
    ).reshape(-1, 1)
    hit_a = slot_of_pair[None, :, 0] == slot_ids
    hit_b = slot_of_pair[None, :, 1] == slot_ids
    hit = hit_a | hit_b
    pick = hit.astype(jnp.bfloat16)

    def to_bucket(rows):
        picked = jnp.dot(pick, rows, preferred_element_type=jnp.float32).astype(rows.dtype)
        return picked.reshape(img_count, LIST_DEV, per_list, rows.shape[1])

    def bucket_major(listed):
        shaped = listed.reshape((listed.shape[0], img_count, per_list) + listed.shape[2:])
        return jnp.moveaxis(shaped, 0, 1)

    def from_bucket(returned):
        flat = returned.reshape(slot_total, -1)
        return jnp.einsum(
            "kg,kc->gc", pick.astype(jnp.float32), flat,
            precision=lax.Precision.HIGH, preferred_element_type=jnp.float32,
        )

    values = embeddings.astype(jnp.float32)
    unit = (values * lax.rsqrt(jnp.sum(values * values, axis=1, keepdims=True) + 1e-06)).astype(
        jnp.bfloat16
    )
    mine = (
        jnp.arange(img_count, dtype=jnp.int32)[:, None] * per_list
        + me_sub * part
        + jnp.arange(part, dtype=jnp.int32)[None, :]
    ).reshape(-1, 1)
    mine_a = slot_of_pair[None, :, 0] == mine
    mine_b = slot_of_pair[None, :, 1] == mine
    mine_hit = mine_a | mine_b
    keys_f = rank_keys.astype(jnp.float32)
    key_sum = jnp.sum(
        jnp.where(mine_a, keys_f[None, :, 0], 0.0) + jnp.where(mine_b, keys_f[None, :, 1], 0.0),
        axis=1,
    )
    mine_keys = jnp.where(jnp.any(mine_hit, axis=1), key_sum, -4096.0).astype(jnp.bfloat16)
    width = unit.shape[1]
    quarter = jnp.dot(mine_hit.astype(jnp.bfloat16), unit, preferred_element_type=jnp.float32)
    half = max(128, width // 3 // 128 * 128)
    quarter = quarter.astype(jnp.bfloat16).reshape(img_count, part, width)
    low_payload = jnp.concatenate(
        [
            quarter[:, :, :half],
            jnp.pad(mine_keys.reshape(img_count, 1, part), ((0, 0), (0, 0), (0, half - part))),
        ],
        axis=1,
    )
    high_payload = quarter[:, :, half:]

    def exchange_stage(got, bit):
        pairs = [(t, t ^ bit) for t in range(sub_count)]
        return jnp.concatenate([got, lax.ppermute(got, "sub", pairs)], axis=0)

    low_got = lax.all_to_all(low_payload, "img", split_axis=0, concat_axis=0, tiled=True)[None]
    high_got = lax.all_to_all(high_payload, "img", split_axis=0, concat_axis=0, tiled=True)[None]
    bit = sub_count // 2
    while bit > 1:
        low_got = exchange_stage(low_got, bit)
        high_got = exchange_stage(high_got, bit)
        bit //= 2
    last = [(t, t ^ bit) for t in range(sub_count)] if bit == 1 else None
    low_pieces = [low_got] + ([lax.ppermute(low_got, "sub", last)] if last else [])
    high_pieces = [high_got] + ([lax.ppermute(high_got, "sub", last)] if last else [])
    low_pieces[-1], pick = lax.optimization_barrier((low_pieces[-1], pick))
    slot_count = slot_total
    key_rows = jnp.moveaxis(
        jnp.concatenate([piece[:, :, part, :part] for piece in low_pieces], axis=0), 0, 1
    ).reshape(slot_count).astype(jnp.float32)
    weight_mat, row_sums = pieces_affinity(low_pieces, high_pieces, key_rows, part)
    weights = weight_mat.reshape(1, slot_count, slot_count)
    degree_slots = lax.all_to_all(
        bucket_major(row_sums), "img", split_axis=0, concat_axis=0, tiled=True
    )
    degree = jnp.sum(jnp.where(pick > 0, degree_slots.reshape(slot_total, 1), 0.0), axis=0)
    inv = lax.rsqrt(degree)
    starting = labels.astype(jnp.float32)
    current = starting
    for step in range(2):
        scaled = (inv[:, None] * current).astype(jnp.bfloat16)
        arrived = lax.all_to_all(to_bucket(scaled), "img", split_axis=0, concat_axis=0, tiled=True)
        product = jnp.einsum(
            "ajk,akc->ajc", weights, list_major(arrived), preferred_element_type=jnp.float32
        )
        returned = lax.all_to_all(
            bucket_major(product), "img", split_axis=0, concat_axis=0, tiled=True
        )
        spread = from_bucket(returned)
        current = 0.8 * inv[:, None] * spread + 0.2 * starting
    return current.astype(jnp.bfloat16)


def solution(mesh):
    return jax.shard_map(
        on_device,
        mesh=mesh,
        in_specs=(P("img", None), P("img", "sub"), P("img", None), P("img", None)),
        out_specs=P("img", "sub"),
        check_vma=False,
    )
```

```python
import functools

import jax
import jax.numpy as jnp
from jax import lax
from jax.experimental import pallas as pl
from jax.experimental.pallas import tpu as pltpu
from jax.sharding import PartitionSpec as P

SLOTS = 2048
BAND = 64
LIST_DEV = 1


def list_major(bucket):
    moved = jnp.moveaxis(bucket, 1, 0)
    return moved.reshape((moved.shape[0], moved.shape[1] * moved.shape[2]) + moved.shape[3:])


def affinity_kernel(col_keys, low_rows, high_rows, weights, row_sums, joined):
    block_rows = weights.shape[0]
    slot_count = weights.shape[1]
    half = joined.shape[1] - high_rows.shape[-1]

    @pl.when(pl.program_id(0) == 0)
    def _():
        low = low_rows[...]
        high = high_rows[...]
        joined[:, :half] = low.reshape(slot_count, low.shape[-1])[:, :half]
        joined[:, half:] = high.reshape(slot_count, high.shape[-1])

    start = pl.multiple_of(pl.program_id(0) * block_rows, block_rows)
    contract = (((1,), (1,)), ((), ()))
    gram = lax.dot_general(
        joined[pl.ds(start, block_rows), :], joined[...], contract,
        preferred_element_type=jnp.float32,
    )
    own_keys = col_keys[:, pl.ds(start, block_rows)]
    diagonal = (
        lax.broadcasted_iota(jnp.int32, (block_rows, block_rows), 0)
        == lax.broadcasted_iota(jnp.int32, (block_rows, block_rows), 1)
    )
    row_keys = jnp.sum(jnp.where(diagonal, own_keys, 0.0), axis=1, keepdims=True)
    keep = jnp.abs(row_keys - col_keys[...]) <= BAND
    positive = jnp.maximum(gram, 0.0)
    cubed = jnp.where(keep, positive * positive * positive, 0.0).astype(jnp.bfloat16)
    weights[...] = cubed
    ones = jnp.ones((8, slot_count), jnp.bfloat16)
    summed = lax.dot_general(ones, cubed, contract, preferred_element_type=jnp.float32)
    row_sums[...] = summed[0:1, :]


def fused_affinity(low, high, keys, part):
    sources, quarters = high.shape[0], high.shape[1]
    slot_count = sources * quarters * part
    half = low.shape[3]
    width = half + high.shape[3]
    if part % 16 == 0:
        low_spec = pl.BlockSpec((sources, quarters, part, half), lambda i: (0, 0, 0, 0))
        high_spec = pl.BlockSpec(high.shape, lambda i: (0, 0, 0, 0))
    else:
        low = low[:, :, :part, :].reshape(slot_count, half)
        high = high.reshape(slot_count, width - half)
        low_spec = pl.BlockSpec(low.shape, lambda i: (0, 0))
        high_spec = pl.BlockSpec(high.shape, lambda i: (0, 0))
    block_rows = min(512, slot_count)
    return pl.pallas_call(
        affinity_kernel,
        grid=(slot_count // block_rows,),
        in_specs=[pl.BlockSpec((1, slot_count), lambda i: (0, 0)), low_spec, high_spec],
        out_specs=[
            pl.BlockSpec((block_rows, slot_count), lambda i: (i, 0)),
            pl.BlockSpec((1, block_rows), lambda i: (0, i)),
        ],
        out_shape=[
            jax.ShapeDtypeStruct((slot_count, slot_count), jnp.bfloat16),
            jax.ShapeDtypeStruct((1, slot_count), jnp.float32),
        ],
        scratch_shapes=[pltpu.VMEM((slot_count, width), jnp.bfloat16)],
        compiler_params=pltpu.CompilerParams(dimension_semantics=("arbitrary",)),
        cost_estimate=pl.CostEstimate(
            flops=2 * slot_count * slot_count * width + 22 * slot_count * slot_count,
            transcendentals=0,
            bytes_accessed=slot_count * width * 2 + 2 * slot_count * slot_count,
        ),
    )(keys.reshape(1, slot_count), low, high)


def pieces_kernel(low_count, high_count, col_keys, *refs):
    low_refs = refs[:low_count]
    high_refs = refs[low_count:low_count + high_count]
    weights, row_sums, joined = refs[low_count + high_count:]
    block_rows = weights.shape[0]
    slot_count = weights.shape[1]
    quarters, part, width = joined.shape[1], joined.shape[2], joined.shape[3]
    half = low_refs[0].shape[-1]

    @pl.when(pl.program_id(0) == 0)
    def _():
        for group, lo, hi in ((low_refs, 0, half), (high_refs, half, width)):
            at = 0
            for ref in group:
                for m in range(ref.shape[0]):
                    joined[:, at, :, lo:hi] = ref[m]
                    at += 1

    per_block = block_rows // (quarters * part)
    first = pl.multiple_of(pl.program_id(0) * per_block, per_block)
    start = pl.multiple_of(pl.program_id(0) * block_rows, block_rows)
    contract = (((1,), (1,)), ((), ()))
    gram = lax.dot_general(
        joined[pl.ds(first, per_block)].reshape(block_rows, width),
        joined[...].reshape(slot_count, width), contract,
        preferred_element_type=jnp.float32,
    )
    own_keys = col_keys[:, pl.ds(start, block_rows)]
    diagonal = (
        lax.broadcasted_iota(jnp.int32, (block_rows, block_rows), 0)
        == lax.broadcasted_iota(jnp.int32, (block_rows, block_rows), 1)
    )
    row_keys = jnp.sum(jnp.where(diagonal, own_keys, 0.0), axis=1, keepdims=True)
    keep = jnp.abs(row_keys - col_keys[...]) <= BAND
    positive = jnp.maximum(gram, 0.0)
    cubed = jnp.where(keep, positive * positive * positive, 0.0).astype(jnp.bfloat16)
    weights[...] = cubed
    ones = jnp.ones((8, slot_count), jnp.bfloat16)
    summed = lax.dot_general(ones, cubed, contract, preferred_element_type=jnp.float32)
    row_sums[...] = summed[0:1, :]


def pieces_affinity(low_pieces, high_pieces, keys, part):
    sources = low_pieces[0].shape[1]
    quarters = sum(piece.shape[0] for piece in low_pieces)
    half = low_pieces[0].shape[3]
    width = half + high_pieces[0].shape[3]
    if part % 16 != 0 or (2 * quarters * part) % 128 != 0:
        def source_major(group):
            stacked = jnp.concatenate([piece[:, :, :part] for piece in group], axis=0)
            return jnp.moveaxis(stacked, 0, 1)
        return fused_affinity(source_major(low_pieces), source_major(high_pieces), keys, part)
    slot_count = sources * quarters * part
    block_rows = min(512, slot_count)
    pieces = list(low_pieces) + list(high_pieces)
    specs = [
        pl.BlockSpec((piece.shape[0], sources, part, piece.shape[3]), lambda i: (0, 0, 0, 0))
        for piece in pieces
    ]
    return pl.pallas_call(
        functools.partial(pieces_kernel, len(low_pieces), len(high_pieces)),
        grid=(slot_count // block_rows,),
        in_specs=[pl.BlockSpec((1, slot_count), lambda i: (0, 0))] + specs,
        out_specs=[
            pl.BlockSpec((block_rows, slot_count), lambda i: (i, 0)),
            pl.BlockSpec((1, block_rows), lambda i: (0, i)),
        ],
        out_shape=[
            jax.ShapeDtypeStruct((slot_count, slot_count), jnp.bfloat16),
            jax.ShapeDtypeStruct((1, slot_count), jnp.float32),
        ],
        scratch_shapes=[pltpu.VMEM((sources, quarters, part, width), jnp.bfloat16)],
        compiler_params=pltpu.CompilerParams(dimension_semantics=("arbitrary",)),
        cost_estimate=pl.CostEstimate(
            flops=2 * slot_count * slot_count * width + 22 * slot_count * slot_count,
            transcendentals=0,
            bytes_accessed=slot_count * width * 2 + 2 * slot_count * slot_count,
        ),
    )(keys.reshape(1, slot_count), *pieces)


def on_device(embeddings, labels, image_lists, rank_keys):
    img_count = lax.axis_size("img")
    sub_count = lax.axis_size("sub")
    per_list = SLOTS // img_count
    part = per_list // sub_count
    rows_here = image_lists.shape[0]
    pair_count = rows_here * 2
    lists_flat = image_lists.reshape(-1)
    order = jnp.arange(pair_count, dtype=jnp.int32)
    same = (lists_flat[:, None] == lists_flat[None, :]) & (order[None, :] < order[:, None])
    within = jnp.sum(same.astype(jnp.int32), axis=1)
    slot_of_pair = (lists_flat * per_list + within).reshape(rows_here, 2)
    slot_total = LIST_DEV * img_count * per_list

    arrival = [0]
    bit = sub_count // 2
    while bit >= 1:
        arrival = arrival + [d ^ bit for d in arrival]
        bit //= 2
    me_sub = lax.axis_index("sub")
    quarters = jnp.bitwise_xor(me_sub, jnp.array(arrival, dtype=jnp.int32))
    slot_ids = (
        jnp.arange(img_count, dtype=jnp.int32)[:, None, None] * per_list
        + quarters[None, :, None] * part
        + jnp.arange(part, dtype=jnp.int32)[None, None, :]
    ).reshape(-1, 1)
    hit_a = slot_of_pair[None, :, 0] == slot_ids
    hit_b = slot_of_pair[None, :, 1] == slot_ids
    hit = hit_a | hit_b
    pick = hit.astype(jnp.bfloat16)

    def to_bucket(rows):
        picked = jnp.dot(pick, rows, preferred_element_type=jnp.float32).astype(rows.dtype)
        return picked.reshape(img_count, LIST_DEV, per_list, rows.shape[1])

    def bucket_major(listed):
        shaped = listed.reshape((listed.shape[0], img_count, per_list) + listed.shape[2:])
        return jnp.moveaxis(shaped, 0, 1)

    def from_bucket(returned):
        flat = returned.reshape(slot_total, -1)
        return jnp.einsum(
            "kg,kc->gc", pick.astype(jnp.float32), flat,
            precision=lax.Precision.HIGH, preferred_element_type=jnp.float32,
        )

    values = embeddings.astype(jnp.float32)
    unit = (values * lax.rsqrt(jnp.sum(values * values, axis=1, keepdims=True) + 1e-06)).astype(
        jnp.bfloat16
    )
    mine = (
        jnp.arange(img_count, dtype=jnp.int32)[:, None] * per_list
        + me_sub * part
        + jnp.arange(part, dtype=jnp.int32)[None, :]
    ).reshape(-1, 1)
    mine_a = slot_of_pair[None, :, 0] == mine
    mine_b = slot_of_pair[None, :, 1] == mine
    mine_hit = mine_a | mine_b
    keys_f = rank_keys.astype(jnp.float32)
    key_sum = jnp.sum(
        jnp.where(mine_a, keys_f[None, :, 0], 0.0) + jnp.where(mine_b, keys_f[None, :, 1], 0.0),
        axis=1,
    )
    mine_keys = jnp.where(jnp.any(mine_hit, axis=1), key_sum, -4096.0).astype(jnp.bfloat16)
    width = unit.shape[1]
    quarter = jnp.dot(mine_hit.astype(jnp.bfloat16), unit, preferred_element_type=jnp.float32)
    half = max(128, width // 6 // 128 * 128)
    quarter = quarter.astype(jnp.bfloat16).reshape(img_count, part, width)
    low_payload = jnp.concatenate(
        [
            quarter[:, :, :half],
            jnp.pad(mine_keys.reshape(img_count, 1, part), ((0, 0), (0, 0), (0, half - part))),
        ],
        axis=1,
    )
    high_payload = quarter[:, :, half:]

    def exchange_stage(got, bit):
        pairs = [(t, t ^ bit) for t in range(sub_count)]
        return jnp.concatenate([got, lax.ppermute(got, "sub", pairs)], axis=0)

    low_got = lax.all_to_all(low_payload, "img", split_axis=0, concat_axis=0, tiled=True)[None]
    high_got = lax.all_to_all(high_payload, "img", split_axis=0, concat_axis=0, tiled=True)[None]
    bit = sub_count // 2
    while bit > 1:
        low_got = exchange_stage(low_got, bit)
        high_got = exchange_stage(high_got, bit)
        bit //= 2
    last = [(t, t ^ bit) for t in range(sub_count)] if bit == 1 else None
    low_pieces = [low_got] + ([lax.ppermute(low_got, "sub", last)] if last else [])
    high_pieces = [high_got] + ([lax.ppermute(high_got, "sub", last)] if last else [])
    slot_count = slot_total
    key_rows = jnp.moveaxis(
        jnp.concatenate([piece[:, :, part, :part] for piece in low_pieces], axis=0), 0, 1
    ).reshape(slot_count).astype(jnp.float32)
    weight_mat, row_sums = pieces_affinity(low_pieces, high_pieces, key_rows, part)
    weights = weight_mat.reshape(1, slot_count, slot_count)
    degree_slots = lax.all_to_all(
        bucket_major(row_sums), "img", split_axis=0, concat_axis=0, tiled=True
    )
    degree = jnp.sum(jnp.where(hit, degree_slots.reshape(slot_total, 1), 0.0), axis=0)
    inv = lax.rsqrt(degree)
    starting = labels.astype(jnp.float32)
    current = starting
    for step in range(2):
        scaled = (inv[:, None] * current).astype(jnp.bfloat16)
        arrived = lax.all_to_all(to_bucket(scaled), "img", split_axis=0, concat_axis=0, tiled=True)
        product = jnp.einsum(
            "ajk,akc->ajc", weights, list_major(arrived), preferred_element_type=jnp.float32
        )
        returned = lax.all_to_all(
            bucket_major(product), "img", split_axis=0, concat_axis=0, tiled=True
        )
        spread = from_bucket(returned)
        current = 0.8 * inv[:, None] * spread + 0.2 * starting
    return current.astype(jnp.bfloat16)


def solution(mesh):
    return jax.shard_map(
        on_device,
        mesh=mesh,
        in_specs=(P("img", None), P("img", "sub"), P("img", None), P("img", None)),
        out_specs=P("img", "sub"),
        check_vma=False,
    )
```

```python
import functools

import jax
import jax.numpy as jnp
from jax import lax
from jax.experimental import pallas as pl
from jax.experimental.pallas import tpu as pltpu
from jax.sharding import PartitionSpec as P

SLOTS = 2048
BAND = 64
LIST_DEV = 1


def list_major(bucket):
    moved = jnp.moveaxis(bucket, 1, 0)
    return moved.reshape((moved.shape[0], moved.shape[1] * moved.shape[2]) + moved.shape[3:])


def affinity_kernel(col_keys, low_rows, high_rows, weights, row_sums, joined):
    block_rows = weights.shape[0]
    slot_count = weights.shape[1]
    half = joined.shape[1] - high_rows.shape[-1]

    @pl.when(pl.program_id(0) == 0)
    def _():
        low = low_rows[...]
        high = high_rows[...]
        joined[:, :half] = low.reshape(slot_count, low.shape[-1])[:, :half]
        joined[:, half:] = high.reshape(slot_count, high.shape[-1])

    start = pl.multiple_of(pl.program_id(0) * block_rows, block_rows)
    contract = (((1,), (1,)), ((), ()))
    gram = lax.dot_general(
        joined[pl.ds(start, block_rows), :], joined[...], contract,
        preferred_element_type=jnp.float32,
    )
    own_keys = col_keys[:, pl.ds(start, block_rows)]
    diagonal = (
        lax.broadcasted_iota(jnp.int32, (block_rows, block_rows), 0)
        == lax.broadcasted_iota(jnp.int32, (block_rows, block_rows), 1)
    )
    row_keys = jnp.sum(jnp.where(diagonal, own_keys, 0.0), axis=1, keepdims=True)
    keep = jnp.abs(row_keys - col_keys[...]) <= BAND
    positive = jnp.maximum(gram, 0.0)
    cubed = jnp.where(keep, positive * positive * positive, 0.0).astype(jnp.bfloat16)
    weights[...] = cubed
    ones = jnp.ones((8, slot_count), jnp.bfloat16)
    summed = lax.dot_general(ones, cubed, contract, preferred_element_type=jnp.float32)
    row_sums[...] = summed[0:1, :]


def fused_affinity(low, high, keys, part):
    sources, quarters = high.shape[0], high.shape[1]
    slot_count = sources * quarters * part
    half = low.shape[3]
    width = half + high.shape[3]
    if part % 16 == 0:
        low_spec = pl.BlockSpec((sources, quarters, part, half), lambda i: (0, 0, 0, 0))
        high_spec = pl.BlockSpec(high.shape, lambda i: (0, 0, 0, 0))
    else:
        low = low[:, :, :part, :].reshape(slot_count, half)
        high = high.reshape(slot_count, width - half)
        low_spec = pl.BlockSpec(low.shape, lambda i: (0, 0))
        high_spec = pl.BlockSpec(high.shape, lambda i: (0, 0))
    block_rows = min(512, slot_count)
    return pl.pallas_call(
        affinity_kernel,
        grid=(slot_count // block_rows,),
        in_specs=[pl.BlockSpec((1, slot_count), lambda i: (0, 0)), low_spec, high_spec],
        out_specs=[
            pl.BlockSpec((block_rows, slot_count), lambda i: (i, 0)),
            pl.BlockSpec((1, block_rows), lambda i: (0, i)),
        ],
        out_shape=[
            jax.ShapeDtypeStruct((slot_count, slot_count), jnp.bfloat16),
            jax.ShapeDtypeStruct((1, slot_count), jnp.float32),
        ],
        scratch_shapes=[pltpu.VMEM((slot_count, width), jnp.bfloat16)],
        compiler_params=pltpu.CompilerParams(dimension_semantics=("arbitrary",)),
        cost_estimate=pl.CostEstimate(
            flops=2 * slot_count * slot_count * width + 22 * slot_count * slot_count,
            transcendentals=0,
            bytes_accessed=slot_count * width * 2 + 2 * slot_count * slot_count,
        ),
    )(keys.reshape(1, slot_count), low, high)


def pieces_kernel(low_count, high_count, col_keys, *refs):
    low_refs = refs[:low_count]
    high_refs = refs[low_count:low_count + high_count]
    weights, row_sums, joined = refs[low_count + high_count:]
    block_rows = weights.shape[0]
    slot_count = weights.shape[1]
    quarters, part, width = joined.shape[1], joined.shape[2], joined.shape[3]
    half = low_refs[0].shape[-1]

    @pl.when(pl.program_id(0) == 0)
    def _():
        for group, lo, hi in ((low_refs, 0, half), (high_refs, half, width)):
            at = 0
            for ref in group:
                for m in range(ref.shape[0]):
                    joined[:, at, :, lo:hi] = ref[m]
                    at += 1

    per_block = block_rows // (quarters * part)
    first = pl.multiple_of(pl.program_id(0) * per_block, per_block)
    start = pl.multiple_of(pl.program_id(0) * block_rows, block_rows)
    contract = (((1,), (1,)), ((), ()))
    gram = lax.dot_general(
        joined[pl.ds(first, per_block)].reshape(block_rows, width),
        joined[...].reshape(slot_count, width), contract,
        preferred_element_type=jnp.float32,
    )
    own_keys = col_keys[:, pl.ds(start, block_rows)]
    diagonal = (
        lax.broadcasted_iota(jnp.int32, (block_rows, block_rows), 0)
        == lax.broadcasted_iota(jnp.int32, (block_rows, block_rows), 1)
    )
    row_keys = jnp.sum(jnp.where(diagonal, own_keys, 0.0), axis=1, keepdims=True)
    keep = jnp.abs(row_keys - col_keys[...]) <= BAND
    positive = jnp.maximum(gram, 0.0)
    cubed = jnp.where(keep, positive * positive * positive, 0.0).astype(jnp.bfloat16)
    weights[...] = cubed
    ones = jnp.ones((8, slot_count), jnp.bfloat16)
    summed = lax.dot_general(ones, cubed, contract, preferred_element_type=jnp.float32)
    row_sums[...] = summed[0:1, :]


def pieces_affinity(low_pieces, high_pieces, keys, part):
    sources = low_pieces[0].shape[1]
    quarters = sum(piece.shape[0] for piece in low_pieces)
    half = low_pieces[0].shape[3]
    width = half + high_pieces[0].shape[3]
    if part % 16 != 0 or (2 * quarters * part) % 128 != 0:
        def source_major(group):
            stacked = jnp.concatenate([piece[:, :, :part] for piece in group], axis=0)
            return jnp.moveaxis(stacked, 0, 1)
        return fused_affinity(source_major(low_pieces), source_major(high_pieces), keys, part)
    slot_count = sources * quarters * part
    block_rows = min(512, slot_count)
    pieces = list(low_pieces) + list(high_pieces)
    specs = [
        pl.BlockSpec((piece.shape[0], sources, part, piece.shape[3]), lambda i: (0, 0, 0, 0))
        for piece in pieces
    ]
    return pl.pallas_call(
        functools.partial(pieces_kernel, len(low_pieces), len(high_pieces)),
        grid=(slot_count // block_rows,),
        in_specs=[pl.BlockSpec((1, slot_count), lambda i: (0, 0))] + specs,
        out_specs=[
            pl.BlockSpec((block_rows, slot_count), lambda i: (i, 0)),
            pl.BlockSpec((1, block_rows), lambda i: (0, i)),
        ],
        out_shape=[
            jax.ShapeDtypeStruct((slot_count, slot_count), jnp.bfloat16),
            jax.ShapeDtypeStruct((1, slot_count), jnp.float32),
        ],
        scratch_shapes=[pltpu.VMEM((sources, quarters, part, width), jnp.bfloat16)],
        compiler_params=pltpu.CompilerParams(dimension_semantics=("arbitrary",)),
        cost_estimate=pl.CostEstimate(
            flops=2 * slot_count * slot_count * width + 22 * slot_count * slot_count,
            transcendentals=0,
            bytes_accessed=slot_count * width * 2 + 2 * slot_count * slot_count,
        ),
    )(keys.reshape(1, slot_count), *pieces)


def on_device(embeddings, labels, image_lists, rank_keys):
    img_count = lax.axis_size("img")
    sub_count = lax.axis_size("sub")
    per_list = SLOTS // img_count
    part = per_list // sub_count
    rows_here = image_lists.shape[0]
    pair_count = rows_here * 2
    lists_flat = image_lists.reshape(-1)
    order = jnp.arange(pair_count, dtype=jnp.int32)
    same = (lists_flat[:, None] == lists_flat[None, :]) & (order[None, :] < order[:, None])
    within = jnp.sum(same.astype(jnp.int32), axis=1)
    slot_of_pair = (lists_flat * per_list + within).reshape(rows_here, 2)
    slot_total = LIST_DEV * img_count * per_list

    arrival = [0]
    bit = sub_count // 2
    while bit >= 1:
        arrival = arrival + [d ^ bit for d in arrival]
        bit //= 2
    me_sub = lax.axis_index("sub")
    quarters = jnp.bitwise_xor(me_sub, jnp.array(arrival, dtype=jnp.int32))
    slot_ids = (
        jnp.arange(img_count, dtype=jnp.int32)[:, None, None] * per_list
        + quarters[None, :, None] * part
        + jnp.arange(part, dtype=jnp.int32)[None, None, :]
    ).reshape(-1, 1)
    hit_a = slot_of_pair[None, :, 0] == slot_ids
    hit_b = slot_of_pair[None, :, 1] == slot_ids
    hit = hit_a | hit_b
    pick = hit.astype(jnp.bfloat16)

    def to_bucket(rows):
        picked = jnp.dot(pick, rows, preferred_element_type=jnp.float32).astype(rows.dtype)
        return picked.reshape(img_count, LIST_DEV, per_list, rows.shape[1])

    def bucket_major(listed):
        shaped = listed.reshape((listed.shape[0], img_count, per_list) + listed.shape[2:])
        return jnp.moveaxis(shaped, 0, 1)

    def from_bucket(returned):
        flat = returned.reshape(slot_total, -1)
        return jnp.einsum(
            "kg,kc->gc", pick.astype(jnp.float32), flat,
            precision=lax.Precision.HIGH, preferred_element_type=jnp.float32,
        )

    values = embeddings.astype(jnp.float32)
    unit = (values * lax.rsqrt(jnp.sum(values * values, axis=1, keepdims=True) + 1e-06)).astype(
        jnp.bfloat16
    )
    mine = (
        jnp.arange(img_count, dtype=jnp.int32)[:, None] * per_list
        + me_sub * part
        + jnp.arange(part, dtype=jnp.int32)[None, :]
    ).reshape(-1, 1)
    mine_a = slot_of_pair[None, :, 0] == mine
    mine_b = slot_of_pair[None, :, 1] == mine
    mine_hit = mine_a | mine_b
    keys_f = rank_keys.astype(jnp.float32)
    key_sum = jnp.sum(
        jnp.where(mine_a, keys_f[None, :, 0], 0.0) + jnp.where(mine_b, keys_f[None, :, 1], 0.0),
        axis=1,
    )
    mine_keys = jnp.where(jnp.any(mine_hit, axis=1), key_sum, -4096.0).astype(jnp.bfloat16)
    width = unit.shape[1]
    quarter = jnp.dot(mine_hit.astype(jnp.bfloat16), unit, preferred_element_type=jnp.float32)
    half = max(128, width // 2 // 128 * 128)
    quarter = quarter.astype(jnp.bfloat16).reshape(img_count, part, width)
    low_payload = jnp.concatenate(
        [
            quarter[:, :, :half],
            jnp.pad(mine_keys.reshape(img_count, 1, part), ((0, 0), (0, 0), (0, half - part))),
        ],
        axis=1,
    )
    high_payload = quarter[:, :, half:]

    def exchange_stage(got, bit):
        pairs = [(t, t ^ bit) for t in range(sub_count)]
        return jnp.concatenate([got, lax.ppermute(got, "sub", pairs)], axis=0)

    low_got = lax.all_to_all(low_payload, "img", split_axis=0, concat_axis=0, tiled=True)[None]
    high_got = lax.all_to_all(high_payload, "img", split_axis=0, concat_axis=0, tiled=True)[None]
    bit = sub_count // 2
    while bit > 1:
        low_got = exchange_stage(low_got, bit)
        high_got = exchange_stage(high_got, bit)
        bit //= 2
    last = [(t, t ^ bit) for t in range(sub_count)] if bit == 1 else None
    low_pieces = [low_got] + ([lax.ppermute(low_got, "sub", last)] if last else [])
    high_pieces = [high_got] + ([lax.ppermute(high_got, "sub", last)] if last else [])
    slot_count = slot_total
    key_rows = jnp.moveaxis(
        jnp.concatenate([piece[:, :, part, :part] for piece in low_pieces], axis=0), 0, 1
    ).reshape(slot_count).astype(jnp.float32)
    weight_mat, row_sums = pieces_affinity(low_pieces, high_pieces, key_rows, part)
    weights = weight_mat.reshape(1, slot_count, slot_count)
    degree_slots = lax.all_to_all(
        bucket_major(row_sums), "img", split_axis=0, concat_axis=0, tiled=True
    )
    degree = jnp.sum(jnp.where(hit, degree_slots.reshape(slot_total, 1), 0.0), axis=0)
    inv = lax.rsqrt(degree)
    starting = labels.astype(jnp.float32)
    current = starting
    for step in range(2):
        scaled = (inv[:, None] * current).astype(jnp.bfloat16)
        arrived = lax.all_to_all(to_bucket(scaled), "img", split_axis=0, concat_axis=0, tiled=True)
        product = jnp.einsum(
            "ajk,akc->ajc", weights, list_major(arrived), preferred_element_type=jnp.float32
        )
        returned = lax.all_to_all(
            bucket_major(product), "img", split_axis=0, concat_axis=0, tiled=True
        )
        spread = from_bucket(returned)
        current = 0.8 * inv[:, None] * spread + 0.2 * starting
    return current.astype(jnp.bfloat16)


def solution(mesh):
    return jax.shard_map(
        on_device,
        mesh=mesh,
        in_specs=(P("img", None), P("img", "sub"), P("img", None), P("img", None)),
        out_specs=P("img", "sub"),
        check_vma=False,
    )
```

```python
import functools

import jax
import jax.numpy as jnp
from jax import lax
from jax.experimental import pallas as pl
from jax.experimental.pallas import tpu as pltpu
from jax.sharding import PartitionSpec as P

SLOTS = 2048
BAND = 64
LIST_DEV = 1


def list_major(bucket):
    moved = jnp.moveaxis(bucket, 1, 0)
    return moved.reshape((moved.shape[0], moved.shape[1] * moved.shape[2]) + moved.shape[3:])


def affinity_kernel(col_keys, low_rows, high_rows, weights, row_sums, joined):
    block_rows = weights.shape[0]
    slot_count = weights.shape[1]
    half = joined.shape[1] - high_rows.shape[-1]

    @pl.when(pl.program_id(0) == 0)
    def _():
        low = low_rows[...]
        high = high_rows[...]
        joined[:, :half] = low.reshape(slot_count, low.shape[-1])[:, :half]
        joined[:, half:] = high.reshape(slot_count, high.shape[-1])

    start = pl.multiple_of(pl.program_id(0) * block_rows, block_rows)
    contract = (((1,), (1,)), ((), ()))
    gram = lax.dot_general(
        joined[pl.ds(start, block_rows), :], joined[...], contract,
        preferred_element_type=jnp.float32,
    )
    own_keys = col_keys[:, pl.ds(start, block_rows)]
    diagonal = (
        lax.broadcasted_iota(jnp.int32, (block_rows, block_rows), 0)
        == lax.broadcasted_iota(jnp.int32, (block_rows, block_rows), 1)
    )
    row_keys = jnp.sum(jnp.where(diagonal, own_keys, 0.0), axis=1, keepdims=True)
    keep = jnp.abs(row_keys - col_keys[...]) <= BAND
    positive = jnp.maximum(gram, 0.0)
    cubed = jnp.where(keep, positive * positive * positive, 0.0).astype(jnp.bfloat16)
    weights[...] = cubed
    ones = jnp.ones((8, slot_count), jnp.bfloat16)
    summed = lax.dot_general(ones, cubed, contract, preferred_element_type=jnp.float32)
    row_sums[...] = summed[0:1, :]


def fused_affinity(low, high, keys, part):
    sources, quarters = high.shape[0], high.shape[1]
    slot_count = sources * quarters * part
    half = low.shape[3]
    width = half + high.shape[3]
    if part % 16 == 0:
        low_spec = pl.BlockSpec((sources, quarters, part, half), lambda i: (0, 0, 0, 0))
        high_spec = pl.BlockSpec(high.shape, lambda i: (0, 0, 0, 0))
    else:
        low = low[:, :, :part, :].reshape(slot_count, half)
        high = high.reshape(slot_count, width - half)
        low_spec = pl.BlockSpec(low.shape, lambda i: (0, 0))
        high_spec = pl.BlockSpec(high.shape, lambda i: (0, 0))
    block_rows = min(512, slot_count)
    return pl.pallas_call(
        affinity_kernel,
        grid=(slot_count // block_rows,),
        in_specs=[pl.BlockSpec((1, slot_count), lambda i: (0, 0)), low_spec, high_spec],
        out_specs=[
            pl.BlockSpec((block_rows, slot_count), lambda i: (i, 0)),
            pl.BlockSpec((1, block_rows), lambda i: (0, i)),
        ],
        out_shape=[
            jax.ShapeDtypeStruct((slot_count, slot_count), jnp.bfloat16),
            jax.ShapeDtypeStruct((1, slot_count), jnp.float32),
        ],
        scratch_shapes=[pltpu.VMEM((slot_count, width), jnp.bfloat16)],
        compiler_params=pltpu.CompilerParams(dimension_semantics=("arbitrary",)),
        cost_estimate=pl.CostEstimate(
            flops=2 * slot_count * slot_count * width + 22 * slot_count * slot_count,
            transcendentals=0,
            bytes_accessed=slot_count * width * 2 + 2 * slot_count * slot_count,
        ),
    )(keys.reshape(1, slot_count), low, high)


def pieces_kernel(low_count, high_count, col_keys, *refs):
    low_refs = refs[:low_count]
    high_refs = refs[low_count:low_count + high_count]
    weights, row_sums, joined = refs[low_count + high_count:]
    block_rows = weights.shape[0]
    slot_count = weights.shape[1]
    quarters, part, width = joined.shape[1], joined.shape[2], joined.shape[3]
    half = low_refs[0].shape[-1]

    @pl.when(pl.program_id(0) == 0)
    def _():
        for group, lo, hi in ((low_refs, 0, half), (high_refs, half, width)):
            at = 0
            for ref in group:
                for m in range(ref.shape[0]):
                    joined[:, at, :, lo:hi] = ref[m]
                    at += 1

    per_block = block_rows // (quarters * part)
    first = pl.multiple_of(pl.program_id(0) * per_block, per_block)
    start = pl.multiple_of(pl.program_id(0) * block_rows, block_rows)
    contract = (((1,), (1,)), ((), ()))
    gram = lax.dot_general(
        joined[pl.ds(first, per_block)].reshape(block_rows, width),
        joined[...].reshape(slot_count, width), contract,
        preferred_element_type=jnp.float32,
    )
    own_keys = col_keys[:, pl.ds(start, block_rows)]
    diagonal = (
        lax.broadcasted_iota(jnp.int32, (block_rows, block_rows), 0)
        == lax.broadcasted_iota(jnp.int32, (block_rows, block_rows), 1)
    )
    row_keys = jnp.sum(jnp.where(diagonal, own_keys, 0.0), axis=1, keepdims=True)
    keep = jnp.abs(row_keys - col_keys[...]) <= BAND
    positive = jnp.maximum(gram, 0.0)
    cubed = jnp.where(keep, positive * positive * positive, 0.0).astype(jnp.bfloat16)
    weights[...] = cubed
    ones = jnp.ones((8, slot_count), jnp.bfloat16)
    summed = lax.dot_general(ones, cubed, contract, preferred_element_type=jnp.float32)
    row_sums[...] = summed[0:1, :]


def pieces_affinity(low_pieces, high_pieces, keys, part):
    sources = low_pieces[0].shape[1]
    quarters = sum(piece.shape[0] for piece in low_pieces)
    half = low_pieces[0].shape[3]
    width = half + high_pieces[0].shape[3]
    if part % 16 != 0 or (2 * quarters * part) % 128 != 0:
        def source_major(group):
            stacked = jnp.concatenate([piece[:, :, :part] for piece in group], axis=0)
            return jnp.moveaxis(stacked, 0, 1)
        return fused_affinity(source_major(low_pieces), source_major(high_pieces), keys, part)
    slot_count = sources * quarters * part
    block_rows = min(1024, slot_count)
    pieces = list(low_pieces) + list(high_pieces)
    specs = [
        pl.BlockSpec((piece.shape[0], sources, part, piece.shape[3]), lambda i: (0, 0, 0, 0))
        for piece in pieces
    ]
    return pl.pallas_call(
        functools.partial(pieces_kernel, len(low_pieces), len(high_pieces)),
        grid=(slot_count // block_rows,),
        in_specs=[pl.BlockSpec((1, slot_count), lambda i: (0, 0))] + specs,
        out_specs=[
            pl.BlockSpec((block_rows, slot_count), lambda i: (i, 0)),
            pl.BlockSpec((1, block_rows), lambda i: (0, i)),
        ],
        out_shape=[
            jax.ShapeDtypeStruct((slot_count, slot_count), jnp.bfloat16),
            jax.ShapeDtypeStruct((1, slot_count), jnp.float32),
        ],
        scratch_shapes=[pltpu.VMEM((sources, quarters, part, width), jnp.bfloat16)],
        compiler_params=pltpu.CompilerParams(dimension_semantics=("arbitrary",)),
        cost_estimate=pl.CostEstimate(
            flops=2 * slot_count * slot_count * width + 22 * slot_count * slot_count,
            transcendentals=0,
            bytes_accessed=slot_count * width * 2 + 2 * slot_count * slot_count,
        ),
    )(keys.reshape(1, slot_count), *pieces)


def on_device(embeddings, labels, image_lists, rank_keys):
    img_count = lax.axis_size("img")
    sub_count = lax.axis_size("sub")
    per_list = SLOTS // img_count
    part = per_list // sub_count
    rows_here = image_lists.shape[0]
    pair_count = rows_here * 2
    lists_flat = image_lists.reshape(-1)
    order = jnp.arange(pair_count, dtype=jnp.int32)
    same = (lists_flat[:, None] == lists_flat[None, :]) & (order[None, :] < order[:, None])
    within = jnp.sum(same.astype(jnp.int32), axis=1)
    slot_of_pair = (lists_flat * per_list + within).reshape(rows_here, 2)
    slot_total = LIST_DEV * img_count * per_list

    arrival = [0]
    bit = sub_count // 2
    while bit >= 1:
        arrival = arrival + [d ^ bit for d in arrival]
        bit //= 2
    me_sub = lax.axis_index("sub")
    quarters = jnp.bitwise_xor(me_sub, jnp.array(arrival, dtype=jnp.int32))
    slot_ids = (
        jnp.arange(img_count, dtype=jnp.int32)[:, None, None] * per_list
        + quarters[None, :, None] * part
        + jnp.arange(part, dtype=jnp.int32)[None, None, :]
    ).reshape(-1, 1)
    hit_a = slot_of_pair[None, :, 0] == slot_ids
    hit_b = slot_of_pair[None, :, 1] == slot_ids
    hit = hit_a | hit_b
    pick = hit.astype(jnp.bfloat16)

    def to_bucket(rows):
        picked = jnp.dot(pick, rows, preferred_element_type=jnp.float32).astype(rows.dtype)
        return picked.reshape(img_count, LIST_DEV, per_list, rows.shape[1])

    def bucket_major(listed):
        shaped = listed.reshape((listed.shape[0], img_count, per_list) + listed.shape[2:])
        return jnp.moveaxis(shaped, 0, 1)

    def from_bucket(returned):
        flat = returned.reshape(slot_total, -1)
        return jnp.einsum(
            "kg,kc->gc", pick.astype(jnp.float32), flat,
            precision=lax.Precision.HIGH, preferred_element_type=jnp.float32,
        )

    values = embeddings.astype(jnp.float32)
    unit = (values * lax.rsqrt(jnp.sum(values * values, axis=1, keepdims=True) + 1e-06)).astype(
        jnp.bfloat16
    )
    mine = (
        jnp.arange(img_count, dtype=jnp.int32)[:, None] * per_list
        + me_sub * part
        + jnp.arange(part, dtype=jnp.int32)[None, :]
    ).reshape(-1, 1)
    mine_a = slot_of_pair[None, :, 0] == mine
    mine_b = slot_of_pair[None, :, 1] == mine
    mine_hit = mine_a | mine_b
    keys_f = rank_keys.astype(jnp.float32)
    key_sum = jnp.sum(
        jnp.where(mine_a, keys_f[None, :, 0], 0.0) + jnp.where(mine_b, keys_f[None, :, 1], 0.0),
        axis=1,
    )
    mine_keys = jnp.where(jnp.any(mine_hit, axis=1), key_sum, -4096.0).astype(jnp.bfloat16)
    width = unit.shape[1]
    quarter = jnp.dot(mine_hit.astype(jnp.bfloat16), unit, preferred_element_type=jnp.float32)
    half = max(128, width // 3 // 128 * 128)
    quarter = quarter.astype(jnp.bfloat16).reshape(img_count, part, width)
    low_payload = jnp.concatenate(
        [
            quarter[:, :, :half],
            jnp.pad(mine_keys.reshape(img_count, 1, part), ((0, 0), (0, 0), (0, half - part))),
        ],
        axis=1,
    )
    high_payload = quarter[:, :, half:]

    def exchange_stage(got, bit):
        pairs = [(t, t ^ bit) for t in range(sub_count)]
        return jnp.concatenate([got, lax.ppermute(got, "sub", pairs)], axis=0)

    low_got = lax.all_to_all(low_payload, "img", split_axis=0, concat_axis=0, tiled=True)[None]
    high_got = lax.all_to_all(high_payload, "img", split_axis=0, concat_axis=0, tiled=True)[None]
    bit = sub_count // 2
    while bit > 1:
        low_got = exchange_stage(low_got, bit)
        high_got = exchange_stage(high_got, bit)
        bit //= 2
    last = [(t, t ^ bit) for t in range(sub_count)] if bit == 1 else None
    low_pieces = [low_got] + ([lax.ppermute(low_got, "sub", last)] if last else [])
    high_pieces = [high_got] + ([lax.ppermute(high_got, "sub", last)] if last else [])
    slot_count = slot_total
    key_rows = jnp.moveaxis(
        jnp.concatenate([piece[:, :, part, :part] for piece in low_pieces], axis=0), 0, 1
    ).reshape(slot_count).astype(jnp.float32)
    weight_mat, row_sums = pieces_affinity(low_pieces, high_pieces, key_rows, part)
    weights = weight_mat.reshape(1, slot_count, slot_count)
    degree_slots = lax.all_to_all(
        bucket_major(row_sums), "img", split_axis=0, concat_axis=0, tiled=True
    )
    degree = jnp.sum(jnp.where(hit, degree_slots.reshape(slot_total, 1), 0.0), axis=0)
    inv = lax.rsqrt(degree)
    starting = labels.astype(jnp.float32)
    current = starting
    for step in range(2):
        scaled = (inv[:, None] * current).astype(jnp.bfloat16)
        arrived = lax.all_to_all(to_bucket(scaled), "img", split_axis=0, concat_axis=0, tiled=True)
        product = jnp.einsum(
            "ajk,akc->ajc", weights, list_major(arrived), preferred_element_type=jnp.float32
        )
        returned = lax.all_to_all(
            bucket_major(product), "img", split_axis=0, concat_axis=0, tiled=True
        )
        spread = from_bucket(returned)
        current = 0.8 * inv[:, None] * spread + 0.2 * starting
    return current.astype(jnp.bfloat16)


def solution(mesh):
    return jax.shard_map(
        on_device,
        mesh=mesh,
        in_specs=(P("img", None), P("img", "sub"), P("img", None), P("img", None)),
        out_specs=P("img", "sub"),
        check_vma=False,
    )
```
